32 devices in a mesh: seq: 16 (over z, y, core), section: 2 (over x).
Axes of the slice: x: 2, y: 2, z: 4, core: 2. Of those that a mesh axis runs over, the one named last changes fastest.
Arguments:
- inputs: bfloat16 [2, 2048, 2048], P('section', 'seq'), may hold values from -6 to 6
- b_proj: bfloat16 [2, 2048, 128], P('section', 'seq'), may hold values from -0.59765625 to 0.59765625
- c_proj: bfloat16 [2, 2048, 128], P('section', 'seq'), may hold values from -0.59765625 to 0.59765625
- decay_log: float32 [2, 2048, 32], P('section', 'seq'), may hold values from -1 to 0, as said below
- level_weight: float32 [2, 2048, 5, 32], P('section', 'seq'), may hold values from 0.25 to 2
- out_grad: bfloat16 [2, 2048, 2048], P('section', 'seq'), may hold values from -6 to 6
- final_state_grad: float32 [2, 32, 128, 64], P('section'), may hold values from -0.125 to 0.125
Outputs:
- upstream_grad: bfloat16 [2, 2048, 2048], P('section', 'seq')
- b_grad: float32 [2, 2048, 128], P('section', 'seq')
- c_grad: float32 [2, 2048, 128], P('section', 'seq')
- decay_grad: float32 [2, 2048, 32], P('section', 'seq')
- weight_grad: float32 [2, 2048, 5, 32], P('section', 'seq')
The draws below stay inside these ranges and needn't reach their ends.
Inputs may be any that keep to these rules, and one draw needn't show every extreme that they name: `decay_log`: negative; per head a rate that varies from token to token and from block to block.
All inputs are finite; a program needn't handle non-finite values.
Results may differ from the reference program's by a relative error of at most 0.001.
Values may be sent and summed in bfloat16 or wider, within the bound.
No kernel may reach another device: no remote copies, remote signals or barrier semaphores. Data moves between devices by JAX's collectives and lax.ppermute only.
A program may use at most 128 MiB of HBM per device.

```python
import math
import jax
import jax.numpy as jnp
from jax import lax

HEAD_TOTAL = 32
P_SIZE = 64
N = 128
TOK_DEV = 128
BITS = 4
LEVELS = 5
SEQUENCE_TOKENS = 2048
RELAY_SECTIONS = 2
N_SEQ = 16


def draw_decay_log(key, part):
    random_keys = jax.random.split(key, 6)
    slow_share = 0.5
    slow_heads = jax.random.uniform(random_keys[0], (RELAY_SECTIONS, 1, HEAD_TOTAL)) < slow_share
    fast_rate = jnp.exp(jax.random.uniform(random_keys[1], (RELAY_SECTIONS, 1, HEAD_TOTAL), minval=math.log(1.0 / TOK_DEV), maxval=math.log(1.0 / 30.0)))
    baseline_rate = jnp.where(slow_heads, 0.25 / SEQUENCE_TOKENS, fast_rate)
    block_multiplier = jnp.exp(jax.random.uniform(random_keys[2], (RELAY_SECTIONS, SEQUENCE_TOKENS // TOK_DEV, 1, HEAD_TOTAL), minval=math.log(0.5), maxval=math.log(2.0)))
    block_multiplier = jnp.broadcast_to(block_multiplier, (RELAY_SECTIONS, SEQUENCE_TOKENS // TOK_DEV, TOK_DEV, HEAD_TOTAL)).reshape(RELAY_SECTIONS, SEQUENCE_TOKENS, HEAD_TOTAL)
    jitter_level = jax.random.uniform(random_keys[3], (RELAY_SECTIONS, SEQUENCE_TOKENS, HEAD_TOTAL), minval=0.5, maxval=1.5)
    spike_position = jax.random.randint(random_keys[4], (RELAY_SECTIONS, 2, HEAD_TOTAL), 0, SEQUENCE_TOKENS)
    spike_log_decay = jax.random.uniform(random_keys[5], (RELAY_SECTIONS, 2, HEAD_TOTAL), minval=math.log(0.5), maxval=math.log(0.8))
    spike_positions = jnp.arange(SEQUENCE_TOKENS)[None, :, None]
    spike_events = jnp.where(spike_positions == spike_position[:, 0:1, :], spike_log_decay[:, 0:1, :], 0.0) + jnp.where(spike_positions == spike_position[:, 1:2, :], spike_log_decay[:, 1:2, :], 0.0)
    return (-baseline_rate * block_multiplier * jitter_level + spike_events).astype(jnp.float32)


def block_scale(rng, extent, pieces, least, top_value):
    loudness, own = 1.0, jax.random.fold_in(rng, 6)
    for axis_at, shards_of in pieces:
        heights = jnp.exp(jax.random.uniform(jax.random.fold_in(own, axis_at), (shards_of,), jnp.float32, least / len(pieces), top_value / len(pieces)))
        loudness = loudness * jnp.repeat(heights, extent[axis_at] // shards_of).reshape([-1 if axis == axis_at else 1 for axis in range(len(extent))])
    return loudness


def centred(stream_key, extent, deviation, most, cuts=(), held_as=jnp.bfloat16):
    level = block_scale(stream_key, extent, cuts, -0.22, 0.18) if cuts else 1.0
    values = jax.random.normal(stream_key, extent, jnp.float32) * deviation * level
    return jnp.minimum(jnp.maximum(values, -most), most).astype(held_as)


def setup_inputs(seed: int = 0) -> dict:
    key_list = jax.random.split(jax.random.key(seed), 8)
    inputs = centred(key_list[0], (RELAY_SECTIONS, SEQUENCE_TOKENS, HEAD_TOTAL * P_SIZE), 1.0, 6.0, ((0, 2), (1, 16)))
    b_proj = centred(key_list[1], (RELAY_SECTIONS, SEQUENCE_TOKENS, N), 0.1, 0.59765625, ((0, 2), (1, 16)))
    c_proj = centred(key_list[2], (RELAY_SECTIONS, SEQUENCE_TOKENS, N), 0.1, 0.59765625, ((0, 2), (1, 16)))
    decay_log = draw_decay_log(jax.random.fold_in(key_list[7], 71), 0)
    level_weight = jnp.clip(jnp.exp(math.log(2.0) - 2.0794415 * jax.random.uniform(key_list[4], (RELAY_SECTIONS, SEQUENCE_TOKENS, LEVELS, HEAD_TOTAL), jnp.float32) ** block_scale(key_list[4], (RELAY_SECTIONS, SEQUENCE_TOKENS, LEVELS, HEAD_TOTAL), ((0, 2), (1, 16)), -0.2, 0.2)), 0.25, 2.0)
    out_grad = centred(key_list[5], (RELAY_SECTIONS, SEQUENCE_TOKENS, HEAD_TOTAL * P_SIZE), 1.0, 6.0, ((0, 2), (1, 16)))
    final_state_grad = centred(key_list[6], (RELAY_SECTIONS, HEAD_TOTAL, N, P_SIZE), (HEAD_TOTAL * P_SIZE) ** -0.5, 0.125, ((0, 2),), jnp.float32)
    return dict(inputs=inputs, b_proj=b_proj, c_proj=c_proj, decay_log=decay_log, level_weight=level_weight, out_grad=out_grad, final_state_grad=final_state_grad)


highest = lax.Precision.HIGHEST

def block_state(inputs, b_proj, decay_log):
    length, head_count = decay_log.shape
    running = jnp.cumsum(decay_log, axis=0)
    block_total = running[-1]
    factor = jnp.exp(block_total[None, :] - running)
    weighted = inputs.astype(jnp.float32).reshape(length, head_count, -1) * factor[:, :, None]
    state = jnp.einsum('tn,thp->hnp', b_proj.astype(jnp.float32), weighted, precision=highest)
    return (state, block_total)

def block_mixer(inputs, b_proj, c_proj, decay_log, level_weight, carries):
    length, head_count = decay_log.shape
    running = jnp.cumsum(decay_log, axis=0)
    values = inputs.astype(jnp.float32).reshape(length, head_count, -1)
    b_full = b_proj.astype(jnp.float32)
    c_full = c_proj.astype(jnp.float32)
    scores = jnp.dot(c_full, b_full.T, precision=highest)
    causal = jnp.arange(length)[:, None] >= jnp.arange(length)[None, :]
    spread = running[:, None, :] - running[None, :, :]
    decays = jnp.exp(jnp.where(causal[:, :, None], spread, -jnp.inf))
    mixing = decays * scores[:, :, None]
    local_part = jnp.einsum('tsh,shp->thp', mixing, values, precision=highest)
    result = level_weight[:, 0, :, None] * local_part
    lift = jnp.exp(running)
    for level_index in range(carries.shape[0]):
        reach = jnp.einsum('tn,hnp->thp', c_full, carries[level_index], precision=highest)
        result = result + (level_weight[:, level_index + 1, :] * lift)[:, :, None] * reach
    return result.reshape(length, -1)

def fenwick_carries(states, totals):
    blocks = totals.shape[0]
    inclusive = jnp.cumsum(totals, axis=0)
    before = inclusive - totals
    target = jnp.arange(blocks)[:, None]
    source = jnp.arange(blocks)[None, :]
    gaps = before[:, None, :] - inclusive[None, :, :]
    result = []
    for level_index in range(BITS):
        width = 2 ** level_index
        base = target // (2 * width) * (2 * width)
        member = (source >= base) & (source < base + width) & (target // width % 2 == 1)
        weights = jnp.exp(jnp.where(member[:, :, None], gaps, -jnp.inf))
        result.append(jnp.einsum('deh,ehnp->dhnp', weights, states, precision=highest))
    after = inclusive[-1][None, :] - inclusive
    final_state = jnp.einsum('eh,ehnp->hnp', jnp.exp(after), states, precision=highest)
    return (jnp.stack(result, axis=1), final_state)

def state_step(operands):
    return block_state(operands[0], operands[1], operands[2])

def mixer_step(operands):
    return block_mixer(operands[0], operands[1], operands[2], operands[3], operands[4], operands[5])

def section_forward(inputs_full, b_full, c_full, decay_full, weight_full):
    inputs_blocks = inputs_full.reshape(N_SEQ, TOK_DEV, -1)
    b_blocks = b_full.reshape(N_SEQ, TOK_DEV, -1)
    c_blocks = c_full.reshape(N_SEQ, TOK_DEV, -1)
    decay_blocks = decay_full.reshape(N_SEQ, TOK_DEV, -1)
    weight_blocks = weight_full.reshape(N_SEQ, TOK_DEV, LEVELS, -1)
    states, totals = lax.map(jax.checkpoint(state_step), (inputs_blocks, b_blocks, decay_blocks))
    carries, final_state = fenwick_carries(states, totals)
    mixed = lax.map(jax.checkpoint(mixer_step), (inputs_blocks, b_blocks, c_blocks, decay_blocks, weight_blocks, carries))
    return (mixed.reshape(SEQUENCE_TOKENS, -1), final_state)

def reference(inputs, b_proj, c_proj, decay_log, level_weight, out_grad, final_state_grad):
    input_list = []
    b_list = []
    c_list = []
    decay_list = []
    weight_list = []
    for section_index in range(RELAY_SECTIONS):
        unused, pull = jax.vjp(section_forward, inputs[section_index].astype(jnp.float32), b_proj[section_index].astype(jnp.float32), c_proj[section_index].astype(jnp.float32), decay_log[section_index], level_weight[section_index])
        grads = pull((out_grad[section_index].astype(jnp.float32), final_state_grad[section_index]))
        input_list.append(grads[0])
        b_list.append(grads[1])
        c_list.append(grads[2])
        decay_list.append(grads[3])
        weight_list.append(grads[4])
    input_grad = jnp.stack(input_list)
    upstream_grad = jnp.roll(input_grad, -1, axis=0).astype(jnp.bfloat16)
    return (upstream_grad, jnp.stack(b_list), jnp.stack(c_list), jnp.stack(decay_list), jnp.stack(weight_list))
```

```python
import jax
import jax.numpy as jnp
from jax import lax
from jax.sharding import PartitionSpec as P

highest = lax.Precision.HIGHEST


def from_partner(value, axis, apart):
    return lax.ppermute(value, axis, [(i, i ^ 1 << apart) for i in range(lax.axis_size(axis))])


def passed_along(block, axis, distance):
    devices = range(lax.axis_size(axis))
    route = [((i - distance) % len(devices), i) for i in devices]
    return lax.ppermute(block, axis, route)


def block_state(inputs, b_proj, decay_log):
    length, head_count = decay_log.shape
    running = jnp.cumsum(decay_log, axis=0)
    block_total = running[-1]
    factor = jnp.exp(block_total[None, :] - running)
    weighted = inputs.astype(jnp.float32).reshape(length, head_count, -1) * factor[:, :, None]
    state = jnp.einsum("tn,thp->hnp", b_proj.astype(jnp.float32), weighted, precision=highest)
    return (state, block_total)


def mixer_local(inputs, b_proj, c_proj, decay_log, first_weight):
    length, head_count = decay_log.shape
    running = jnp.cumsum(decay_log, axis=0)
    values = inputs.reshape(length, head_count, -1)
    scores = jnp.dot(c_proj, b_proj.T, precision=highest)
    causal = jnp.arange(length)[:, None] >= jnp.arange(length)[None, :]
    spread = running[:, None, :] - running[None, :, :]
    decays = jnp.exp(jnp.where(causal[:, :, None], spread, -jnp.inf))
    mixing = decays * scores[:, :, None]
    local_part = jnp.einsum("tsh,shp->thp", mixing, values, precision=highest)
    result = first_weight[:, :, None] * local_part
    return result.reshape(length, -1)


def mixer_carry(c_proj, decay_log, upper_weight, carries):
    length, head_count = decay_log.shape
    running = jnp.cumsum(decay_log, axis=0)
    lift = jnp.exp(running)
    result = jnp.zeros((length, head_count, carries.shape[-1]), jnp.float32)
    for level_index in range(carries.shape[0]):
        reach = jnp.einsum("tn,hnp->thp", c_proj, carries[level_index], precision=highest)
        result = result + (upper_weight[:, level_index, :] * lift)[:, :, None] * reach
    return result.reshape(length, -1)


def level_logs(totals, position, levels):
    count = totals.shape[0]
    index = jnp.arange(count)
    own, peer, prefix = [], [], []
    for level_index in range(levels):
        width = 1 << level_index
        base = position // width * width
        other = (position // width ^ 1) * width
        in_own = (index >= base) & (index < base + width)
        in_peer = (index >= other) & (index < other + width)
        in_prefix = (index >= base) & (index < position)
        own.append(jnp.sum(jnp.where(in_own[:, None], totals, 0.0), axis=0))
        peer.append(jnp.sum(jnp.where(in_peer[:, None], totals, 0.0), axis=0))
        prefix.append(jnp.sum(jnp.where(in_prefix[:, None], totals, 0.0), axis=0))
    return (own, peer, prefix)


def halves_usable(state):
    return state.shape[0] % 2 == 0


def exchange_state(state, level_index):
    if level_index == 0 or not halves_usable(state):
        return from_partner(state, "seq", level_index)
    half = state.shape[0] // 2
    core = lax.axis_index("seq") % 2
    mine = lax.dynamic_slice_in_dim(state, core * half, half, 0)
    got = from_partner(mine, "seq", level_index)
    other = from_partner(got, "seq", 0)
    low = jnp.where(core == 0, got, other)
    high = jnp.where(core == 0, other, got)
    return jnp.concatenate([low, high], axis=0)


def exchange_grad(own_grad, peer_grad, level_index):
    if level_index == 0 or not halves_usable(peer_grad):
        return own_grad + from_partner(peer_grad, "seq", level_index)
    half = peer_grad.shape[0] // 2
    core = lax.axis_index("seq") % 2
    mine = lax.dynamic_slice_in_dim(peer_grad, core * half, half, 0)
    theirs = lax.dynamic_slice_in_dim(peer_grad, (1 - core) * half, half, 0)
    summed = mine + from_partner(theirs, "seq", 0)
    back = from_partner(summed, "seq", level_index)
    own_half = lax.dynamic_slice_in_dim(own_grad, core * half, half, 0)
    return lax.dynamic_update_slice_in_dim(own_grad, own_half + back, core * half, 0)


def state_spread(b_proj, decay_log, state_grad):
    running = jnp.cumsum(decay_log, axis=0)
    factor = jnp.exp(running[-1][None, :] - running)
    pulled = jnp.einsum("tn,hnp->thp", b_proj.astype(jnp.float32), state_grad, precision=highest)
    return (factor, pulled)


def state_backward(inputs, decay_log, state_grad, total_grad, factor, pulled):
    length, head_count = decay_log.shape
    values = inputs.astype(jnp.float32).reshape(length, head_count, -1)
    weighted = values * factor[:, :, None]
    b_grad = jnp.einsum("thp,hnp->tn", weighted, state_grad, precision=highest)
    log_grad = jnp.sum(values * pulled, axis=2) * factor
    running_grad = (-log_grad).at[-1].add(total_grad + jnp.sum(log_grad, axis=0))
    decay_grad = jnp.cumsum(running_grad[::-1], axis=0)[::-1]
    return (b_grad, decay_grad)


def body(inputs, b_proj, c_proj, decay_log, level_weight, out_grad, final_state_grad):
    own_inputs = inputs[0]
    own_b = b_proj[0]
    own_c = c_proj[0]
    own_decay = decay_log[0]
    own_weight = level_weight[0]
    own_grad = out_grad[0]
    length, head_count = own_decay.shape
    head_size = own_inputs.shape[1] // head_count
    group = 8
    group_width = group * head_size
    levels = lax.axis_size("seq").bit_length() - 1
    position = lax.axis_index("seq")
    b_full = own_b.astype(jnp.float32)
    c_full = own_c.astype(jnp.float32)
    grad_full = own_grad.astype(jnp.float32)

    state_now, total_now = block_state(own_inputs, own_b, own_decay)
    totals = lax.all_gather(total_now, "seq")
    own_logs, peer_logs, prefixes = level_logs(totals, position, levels)
    uppers = [position // 2**level_index % 2 == 1 for level_index in range(levels)]

    saved_own = []
    saved_peer = []
    carries = []
    for level_index in range(levels):
        upper = uppers[level_index]
        peer_state = exchange_state(state_now, level_index)
        saved_own.append(state_now)
        saved_peer.append(peer_state)
        carries.append(
            jnp.where(upper, jnp.exp(prefixes[level_index])[:, None, None] * peer_state, 0.0)
        )
        if level_index < levels - 1:
            state_now = jnp.where(
                upper,
                jnp.exp(own_logs[level_index])[:, None, None] * peer_state + state_now,
                jnp.exp(peer_logs[level_index])[:, None, None] * state_now + peer_state,
            )
    all_carries = jnp.stack(carries)

    unused, pull_carry = jax.vjp(mixer_carry, c_full, own_decay, own_weight[:, 1:, :], all_carries)
    c_carry, decay_carry, weight_carry, carry_grads = pull_carry(grad_full)

    state_grad = jnp.where(position == 0, final_state_grad[0], 0.0)
    joined_grads = [None] * levels
    for level_index in reversed(range(levels)):
        upper = uppers[level_index]
        joined_grads[level_index] = state_grad
        own_sg = jnp.where(
            upper, state_grad, jnp.exp(peer_logs[level_index])[:, None, None] * state_grad
        )
        peer_sg = jnp.where(
            upper,
            jnp.exp(own_logs[level_index])[:, None, None] * state_grad
            + jnp.exp(prefixes[level_index])[:, None, None] * carry_grads[level_index],
            state_grad,
        )
        state_grad = exchange_grad(own_sg, peer_sg, level_index)

    own_log_grads = []
    peer_log_grads = []
    prefix_grads = []
    for level_index in range(levels):
        upper = uppers[level_index]
        joined_grad = joined_grads[level_index]
        with_peer = jnp.sum(joined_grad * saved_peer[level_index], axis=(1, 2))
        with_own = jnp.sum(joined_grad * saved_own[level_index], axis=(1, 2))
        carry_peer = jnp.sum(carry_grads[level_index] * saved_peer[level_index], axis=(1, 2))
        own_log_grads.append(jnp.where(upper, jnp.exp(own_logs[level_index]) * with_peer, 0.0))
        peer_log_grads.append(jnp.where(upper, 0.0, jnp.exp(peer_logs[level_index]) * with_own))
        prefix_grads.append(jnp.where(upper, jnp.exp(prefixes[level_index]) * carry_peer, 0.0))
    unused, pull_logs = jax.vjp(lambda t: level_logs(t, position, levels), totals)
    (totals_grad,) = pull_logs((own_log_grads, peer_log_grads, prefix_grads))
    totals_grad = lax.psum(totals_grad, "seq")
    log_grad = lax.dynamic_index_in_dim(totals_grad, position, 0, keepdims=False)

    def group_step(group_index, buffers):
        input_buf, b_acc, c_acc, decay_buf, weight_buf = buffers
        first_head = group_index * group
        first_col = group_index * group_width
        piece_inputs = lax.dynamic_slice_in_dim(own_inputs, first_col, group_width, 1).astype(
            jnp.float32
        )
        piece_decay = lax.dynamic_slice_in_dim(own_decay, first_head, group, 1)
        piece_weight = lax.dynamic_slice_in_dim(own_weight[:, 0, :], first_head, group, 1)
        piece_grad = lax.dynamic_slice_in_dim(grad_full, first_col, group_width, 1)
        unused, pull = jax.vjp(mixer_local, piece_inputs, b_full, c_full, piece_decay, piece_weight)
        grads = pull(piece_grad)
        input_buf = lax.dynamic_update_slice_in_dim(input_buf, grads[0], first_col, 1)
        decay_buf = lax.dynamic_update_slice_in_dim(decay_buf, grads[3], first_head, 1)
        weight_buf = lax.dynamic_update_slice_in_dim(weight_buf, grads[4], first_head, 1)
        return (input_buf, b_acc + grads[1], c_acc + grads[2], decay_buf, weight_buf)

    start_buffers = (
        jnp.zeros(own_inputs.shape, jnp.float32),
        jnp.zeros(own_b.shape, jnp.float32),
        jnp.zeros(own_c.shape, jnp.float32),
        jnp.zeros(own_decay.shape, jnp.float32),
        jnp.zeros((length, head_count), jnp.float32),
    )
    input_buf, b_acc, c_acc, decay_buf, weight_first = lax.fori_loop(
        0, head_count // group, group_step, start_buffers
    )

    factor, pulled = state_spread(own_b, own_decay, state_grad)
    b_extra, decay_extra = state_backward(
        own_inputs, own_decay, state_grad, log_grad, factor, pulled
    )
    input_grad = input_buf + (factor[:, :, None] * pulled).reshape(length, -1)
    upstream = passed_along(input_grad.astype(jnp.bfloat16), "section", -1)
    b_grad = b_acc + b_extra
    c_grad = c_acc + c_carry
    decay_grad = decay_buf + decay_carry + decay_extra
    weight_grad = jnp.concatenate([weight_first[:, None, :], weight_carry], axis=1)
    return (upstream[None], b_grad[None], c_grad[None], decay_grad[None], weight_grad[None])


def solution(mesh):
    return jax.shard_map(
        body,
        mesh=mesh,
        in_specs=(
            P("section", "seq", None),
            P("section", "seq", None),
            P("section", "seq", None),
            P("section", "seq", None),
            P("section", "seq", None, None),
            P("section", "seq", None),
            P("section", None, None, None),
        ),
        out_specs=(
            P("section", "seq", None),
            P("section", "seq", None),
            P("section", "seq", None),
            P("section", "seq", None),
            P("section", "seq", None, None),
        ),
        check_vma=False,
    )
```

```python
import jax
import jax.numpy as jnp
from jax import lax
from jax.sharding import PartitionSpec as P

highest = lax.Precision.HIGHEST


def from_partner(value, axis, apart):
    return lax.ppermute(value, axis, [(i, i ^ 1 << apart) for i in range(lax.axis_size(axis))])


def passed_along(block, axis, distance):
    devices = range(lax.axis_size(axis))
    route = [((i - distance) % len(devices), i) for i in devices]
    return lax.ppermute(block, axis, route)


def block_state(inputs, b_proj, decay_log):
    length, head_count = decay_log.shape
    running = jnp.cumsum(decay_log, axis=0)
    block_total = running[-1]
    factor = jnp.exp(block_total[None, :] - running)
    weighted = inputs.astype(jnp.float32).reshape(length, head_count, -1) * factor[:, :, None]
    state = jnp.einsum("tn,thp->hnp", b_proj.astype(jnp.float32), weighted, precision=highest)
    return (state, block_total)


def mixer_local(inputs, b_proj, c_proj, decay_log, first_weight):
    length, head_count = decay_log.shape
    running = jnp.cumsum(decay_log, axis=0)
    values = inputs.reshape(length, head_count, -1)
    scores = jnp.dot(c_proj, b_proj.T, precision=highest)
    causal = jnp.arange(length)[:, None] >= jnp.arange(length)[None, :]
    spread = running[:, None, :] - running[None, :, :]
    decays = jnp.exp(jnp.where(causal[:, :, None], spread, -jnp.inf))
    mixing = decays * scores[:, :, None]
    local_part = jnp.einsum("tsh,shp->thp", mixing, values, precision=highest)
    result = first_weight[:, :, None] * local_part
    return result.reshape(length, -1)


def mixer_carry(c_proj, decay_log, upper_weight, carries):
    length, head_count = decay_log.shape
    running = jnp.cumsum(decay_log, axis=0)
    lift = jnp.exp(running)
    result = jnp.zeros((length, head_count, carries.shape[-1]), jnp.float32)
    for level_index in range(carries.shape[0]):
        reach = jnp.einsum("tn,hnp->thp", c_proj, carries[level_index], precision=highest)
        result = result + (upper_weight[:, level_index, :] * lift)[:, :, None] * reach
    return result.reshape(length, -1)


def level_logs(totals, position, levels):
    count = totals.shape[0]
    index = jnp.arange(count)
    own, peer, prefix = [], [], []
    for level_index in range(levels):
        width = 1 << level_index
        base = position // width * width
        other = (position // width ^ 1) * width
        in_own = (index >= base) & (index < base + width)
        in_peer = (index >= other) & (index < other + width)
        in_prefix = (index >= base) & (index < position)
        own.append(jnp.sum(jnp.where(in_own[:, None], totals, 0.0), axis=0))
        peer.append(jnp.sum(jnp.where(in_peer[:, None], totals, 0.0), axis=0))
        prefix.append(jnp.sum(jnp.where(in_prefix[:, None], totals, 0.0), axis=0))
    return (own, peer, prefix)


def gather_blocks(value, axis):
    position = lax.axis_index(axis)
    blocks = value[None]
    for level_index in range(lax.axis_size(axis).bit_length() - 1):
        other = from_partner(blocks, axis, level_index)
        upper = position // 2**level_index % 2 == 1
        blocks = jnp.where(
            upper,
            jnp.concatenate([other, blocks], axis=0),
            jnp.concatenate([blocks, other], axis=0),
        )
    return blocks


def sum_over(value, axis):
    for level_index in range(lax.axis_size(axis).bit_length() - 1):
        value = value + from_partner(value, axis, level_index)
    return value


def halves_usable(state):
    return state.shape[0] % 2 == 0


def exchange_state(state, level_index):
    if level_index == 0 or not halves_usable(state):
        return from_partner(state, "seq", level_index)
    half = state.shape[0] // 2
    core = lax.axis_index("seq") % 2
    mine = lax.dynamic_slice_in_dim(state, core * half, half, 0)
    got = from_partner(mine, "seq", level_index)
    other = from_partner(got, "seq", 0)
    low = jnp.where(core == 0, got, other)
    high = jnp.where(core == 0, other, got)
    return jnp.concatenate([low, high], axis=0)


def exchange_grad(own_grad, peer_grad, level_index):
    if level_index == 0 or not halves_usable(peer_grad):
        return own_grad + from_partner(peer_grad, "seq", level_index)
    half = peer_grad.shape[0] // 2
    core = lax.axis_index("seq") % 2
    mine = lax.dynamic_slice_in_dim(peer_grad, core * half, half, 0)
    theirs = lax.dynamic_slice_in_dim(peer_grad, (1 - core) * half, half, 0)
    summed = mine + from_partner(theirs, "seq", 0)
    back = from_partner(summed, "seq", level_index)
    own_half = lax.dynamic_slice_in_dim(own_grad, core * half, half, 0)
    return lax.dynamic_update_slice_in_dim(own_grad, own_half + back, core * half, 0)


def state_spread(b_proj, decay_log, state_grad):
    running = jnp.cumsum(decay_log, axis=0)
    factor = jnp.exp(running[-1][None, :] - running)
    pulled = jnp.einsum("tn,hnp->thp", b_proj.astype(jnp.float32), state_grad, precision=highest)
    return (factor, pulled)


def state_backward(inputs, decay_log, state_grad, total_grad, factor, pulled):
    length, head_count = decay_log.shape
    values = inputs.astype(jnp.float32).reshape(length, head_count, -1)
    weighted = values * factor[:, :, None]
    b_grad = jnp.einsum("thp,hnp->tn", weighted, state_grad, precision=highest)
    log_grad = jnp.sum(values * pulled, axis=2) * factor
    running_grad = (-log_grad).at[-1].add(total_grad + jnp.sum(log_grad, axis=0))
    decay_grad = jnp.cumsum(running_grad[::-1], axis=0)[::-1]
    return (b_grad, decay_grad)


def body(inputs, b_proj, c_proj, decay_log, level_weight, out_grad, final_state_grad):
    own_inputs = inputs[0]
    own_b = b_proj[0]
    own_c = c_proj[0]
    own_decay = decay_log[0]
    own_weight = level_weight[0]
    own_grad = out_grad[0]
    length, head_count = own_decay.shape
    head_size = own_inputs.shape[1] // head_count
    group = 8
    group_width = group * head_size
    levels = lax.axis_size("seq").bit_length() - 1
    position = lax.axis_index("seq")
    b_full = own_b.astype(jnp.float32)
    c_full = own_c.astype(jnp.float32)
    grad_full = own_grad.astype(jnp.float32)

    state_now, total_now = block_state(own_inputs, own_b, own_decay)
    totals = gather_blocks(total_now, "seq")
    own_logs, peer_logs, prefixes = level_logs(totals, position, levels)
    uppers = [position // 2**level_index % 2 == 1 for level_index in range(levels)]

    unused, pull_carry = jax.vjp(
        mixer_carry, c_full, own_decay, own_weight[:, 1:, :],
        jnp.zeros((levels,) + state_now.shape, jnp.float32),
    )
    carry_grads = pull_carry(grad_full)[3]

    saved_own = [None] * levels
    saved_peer = [None] * levels
    carries = [None] * levels
    joined_grads = [None] * levels
    state_grad = jnp.where(position == 0, final_state_grad[0], 0.0)
    for step in range(levels):
        state_now, state_grad = lax.optimization_barrier((state_now, state_grad))
        level_index = step
        upper = uppers[level_index]
        peer_state = exchange_state(state_now, level_index)
        saved_own[level_index] = state_now
        saved_peer[level_index] = peer_state
        carries[level_index] = jnp.where(
            upper, jnp.exp(prefixes[level_index])[:, None, None] * peer_state, 0.0
        )
        if level_index < levels - 1:
            state_now = jnp.where(
                upper,
                jnp.exp(own_logs[level_index])[:, None, None] * peer_state + state_now,
                jnp.exp(peer_logs[level_index])[:, None, None] * state_now + peer_state,
            )
        level_index = levels - 1 - step
        upper = uppers[level_index]
        joined_grads[level_index] = state_grad
        own_sg = jnp.where(
            upper, state_grad, jnp.exp(peer_logs[level_index])[:, None, None] * state_grad
        )
        peer_sg = jnp.where(
            upper,
            jnp.exp(own_logs[level_index])[:, None, None] * state_grad
            + jnp.exp(prefixes[level_index])[:, None, None] * carry_grads[level_index],
            state_grad,
        )
        state_grad = exchange_grad(own_sg, peer_sg, level_index)
    all_carries = jnp.stack(carries)

    unused, pull_carry = jax.vjp(mixer_carry, c_full, own_decay, own_weight[:, 1:, :], all_carries)
    c_carry, decay_carry, weight_carry, unused_grads = pull_carry(grad_full)

    own_log_grads = []
    peer_log_grads = []
    prefix_grads = []
    for level_index in range(levels):
        upper = uppers[level_index]
        joined_grad = joined_grads[level_index]
        with_peer = jnp.sum(joined_grad * saved_peer[level_index], axis=(1, 2))
        with_own = jnp.sum(joined_grad * saved_own[level_index], axis=(1, 2))
        carry_peer = jnp.sum(carry_grads[level_index] * saved_peer[level_index], axis=(1, 2))
        own_log_grads.append(jnp.where(upper, jnp.exp(own_logs[level_index]) * with_peer, 0.0))
        peer_log_grads.append(jnp.where(upper, 0.0, jnp.exp(peer_logs[level_index]) * with_own))
        prefix_grads.append(jnp.where(upper, jnp.exp(prefixes[level_index]) * carry_peer, 0.0))
    unused, pull_logs = jax.vjp(lambda t: level_logs(t, position, levels), totals)
    (totals_grad,) = pull_logs((own_log_grads, peer_log_grads, prefix_grads))
    totals_grad = sum_over(totals_grad, "seq")
    log_grad = lax.dynamic_index_in_dim(totals_grad, position, 0, keepdims=False)

    def group_step(group_index, buffers):
        input_buf, b_acc, c_acc, decay_buf, weight_buf = buffers
        first_head = group_index * group
        first_col = group_index * group_width
        piece_inputs = lax.dynamic_slice_in_dim(own_inputs, first_col, group_width, 1).astype(
            jnp.float32
        )
        piece_decay = lax.dynamic_slice_in_dim(own_decay, first_head, group, 1)
        piece_weight = lax.dynamic_slice_in_dim(own_weight[:, 0, :], first_head, group, 1)
        piece_grad = lax.dynamic_slice_in_dim(grad_full, first_col, group_width, 1)
        unused, pull = jax.vjp(mixer_local, piece_inputs, b_full, c_full, piece_decay, piece_weight)
        grads = pull(piece_grad)
        input_buf = lax.dynamic_update_slice_in_dim(input_buf, grads[0], first_col, 1)
        decay_buf = lax.dynamic_update_slice_in_dim(decay_buf, grads[3], first_head, 1)
        weight_buf = lax.dynamic_update_slice_in_dim(weight_buf, grads[4], first_head, 1)
        return (input_buf, b_acc + grads[1], c_acc + grads[2], decay_buf, weight_buf)

    start_buffers = (
        jnp.zeros(own_inputs.shape, jnp.float32),
        jnp.zeros(own_b.shape, jnp.float32),
        jnp.zeros(own_c.shape, jnp.float32),
        jnp.zeros(own_decay.shape, jnp.float32),
        jnp.zeros((length, head_count), jnp.float32),
    )
    input_buf, b_acc, c_acc, decay_buf, weight_first = lax.fori_loop(
        0, head_count // group, group_step, start_buffers
    )

    factor, pulled = state_spread(own_b, own_decay, state_grad)
    b_extra, decay_extra = state_backward(
        own_inputs, own_decay, state_grad, log_grad, factor, pulled
    )
    input_grad = input_buf + (factor[:, :, None] * pulled).reshape(length, -1)
    upstream = passed_along(input_grad.astype(jnp.bfloat16), "section", -1)
    b_grad = b_acc + b_extra
    c_grad = c_acc + c_carry
    decay_grad = decay_buf + decay_carry + decay_extra
    weight_grad = jnp.concatenate([weight_first[:, None, :], weight_carry], axis=1)
    return (upstream[None], b_grad[None], c_grad[None], decay_grad[None], weight_grad[None])


def solution(mesh):
    return jax.shard_map(
        body,
        mesh=mesh,
        in_specs=(
            P("section", "seq", None),
            P("section", "seq", None),
            P("section", "seq", None),
            P("section", "seq", None),
            P("section", "seq", None, None),
            P("section", "seq", None),
            P("section", None, None, None),
        ),
        out_specs=(
            P("section", "seq", None),
            P("section", "seq", None),
            P("section", "seq", None),
            P("section", "seq", None),
            P("section", "seq", None, None),
        ),
        check_vma=False,
    )
```

```python
import jax
import jax.numpy as jnp
from jax import lax
from jax.sharding import PartitionSpec as P

highest = lax.Precision.HIGHEST


def from_partner(value, axis, apart):
    return lax.ppermute(value, axis, [(i, i ^ 1 << apart) for i in range(lax.axis_size(axis))])


def passed_along(block, axis, distance):
    devices = range(lax.axis_size(axis))
    route = [((i - distance) % len(devices), i) for i in devices]
    return lax.ppermute(block, axis, route)


def block_state(inputs, b_proj, decay_log):
    length, head_count = decay_log.shape
    running = jnp.cumsum(decay_log, axis=0)
    block_total = running[-1]
    factor = jnp.exp(block_total[None, :] - running)
    weighted = inputs.astype(jnp.float32).reshape(length, head_count, -1) * factor[:, :, None]
    state = jnp.einsum("tn,thp->hnp", b_proj.astype(jnp.float32), weighted, precision=highest)
    return (state, block_total)


def mixer_local(inputs, b_proj, c_proj, decay_log, first_weight):
    length, head_count = decay_log.shape
    running = jnp.cumsum(decay_log, axis=0)
    values = inputs.reshape(length, head_count, -1)
    scores = jnp.dot(c_proj, b_proj.T, precision=highest)
    causal = jnp.arange(length)[:, None] >= jnp.arange(length)[None, :]
    spread = running[:, None, :] - running[None, :, :]
    decays = jnp.exp(jnp.where(causal[:, :, None], spread, -jnp.inf))
    mixing = decays * scores[:, :, None]
    local_part = jnp.einsum("tsh,shp->thp", mixing, values, precision=highest)
    result = first_weight[:, :, None] * local_part
    return result.reshape(length, -1)


def mixer_carry(c_proj, decay_log, upper_weight, carries):
    length, head_count = decay_log.shape
    running = jnp.cumsum(decay_log, axis=0)
    lift = jnp.exp(running)
    result = jnp.zeros((length, head_count, carries.shape[-1]), jnp.float32)
    for level_index in range(carries.shape[0]):
        reach = jnp.einsum("tn,hnp->thp", c_proj, carries[level_index], precision=highest)
        result = result + (upper_weight[:, level_index, :] * lift)[:, :, None] * reach
    return result.reshape(length, -1)


def level_logs(totals, position, levels):
    count = totals.shape[0]
    index = jnp.arange(count)
    own, peer, prefix = [], [], []
    for level_index in range(levels):
        width = 1 << level_index
        base = position // width * width
        other = (position // width ^ 1) * width
        in_own = (index >= base) & (index < base + width)
        in_peer = (index >= other) & (index < other + width)
        in_prefix = (index >= base) & (index < position)
        own.append(jnp.sum(jnp.where(in_own[:, None], totals, 0.0), axis=0))
        peer.append(jnp.sum(jnp.where(in_peer[:, None], totals, 0.0), axis=0))
        prefix.append(jnp.sum(jnp.where(in_prefix[:, None], totals, 0.0), axis=0))
    return (own, peer, prefix)


def gather_blocks(value, axis):
    position = lax.axis_index(axis)
    blocks = value[None]
    for level_index in range(lax.axis_size(axis).bit_length() - 1):
        other = from_partner(blocks, axis, level_index)
        upper = position // 2**level_index % 2 == 1
        blocks = jnp.where(
            upper,
            jnp.concatenate([other, blocks], axis=0),
            jnp.concatenate([blocks, other], axis=0),
        )
    return blocks


def sum_over(value, axis):
    for level_index in range(lax.axis_size(axis).bit_length() - 1):
        value = value + from_partner(value, axis, level_index)
    return value


def halves_usable(state):
    return state.shape[0] % 2 == 0


def exchange_state(state, level_index):
    if level_index == 0 or not halves_usable(state):
        return from_partner(state, "seq", level_index)
    half = state.shape[0] // 2
    core = lax.axis_index("seq") % 2
    mine = lax.dynamic_slice_in_dim(state, core * half, half, 0)
    got = from_partner(mine, "seq", level_index)
    other = from_partner(got, "seq", 0)
    low = jnp.where(core == 0, got, other)
    high = jnp.where(core == 0, other, got)
    return jnp.concatenate([low, high], axis=0)


def exchange_grad(own_grad, peer_grad, level_index):
    if level_index == 0 or not halves_usable(peer_grad):
        return own_grad + from_partner(peer_grad, "seq", level_index)
    half = peer_grad.shape[0] // 2
    core = lax.axis_index("seq") % 2
    mine = lax.dynamic_slice_in_dim(peer_grad, core * half, half, 0)
    theirs = lax.dynamic_slice_in_dim(peer_grad, (1 - core) * half, half, 0)
    summed = mine + from_partner(theirs, "seq", 0)
    back = from_partner(summed, "seq", level_index)
    own_half = lax.dynamic_slice_in_dim(own_grad, core * half, half, 0)
    return lax.dynamic_update_slice_in_dim(own_grad, own_half + back, core * half, 0)


def state_spread(b_proj, decay_log, state_grad):
    running = jnp.cumsum(decay_log, axis=0)
    factor = jnp.exp(running[-1][None, :] - running)
    pulled = jnp.einsum("tn,hnp->thp", b_proj.astype(jnp.float32), state_grad, precision=highest)
    return (factor, pulled)


def state_backward(inputs, decay_log, state_grad, total_grad, factor, pulled):
    length, head_count = decay_log.shape
    values = inputs.astype(jnp.float32).reshape(length, head_count, -1)
    weighted = values * factor[:, :, None]
    b_grad = jnp.einsum("thp,hnp->tn", weighted, state_grad, precision=highest)
    log_grad = jnp.sum(values * pulled, axis=2) * factor
    running_grad = (-log_grad).at[-1].add(total_grad + jnp.sum(log_grad, axis=0))
    decay_grad = jnp.cumsum(running_grad[::-1], axis=0)[::-1]
    return (b_grad, decay_grad)


def body(inputs, b_proj, c_proj, decay_log, level_weight, out_grad, final_state_grad):
    own_inputs = inputs[0]
    own_b = b_proj[0]
    own_c = c_proj[0]
    own_decay = decay_log[0]
    own_weight = level_weight[0]
    own_grad = out_grad[0]
    length, head_count = own_decay.shape
    head_size = own_inputs.shape[1] // head_count
    group = 8
    group_width = group * head_size
    levels = lax.axis_size("seq").bit_length() - 1
    position = lax.axis_index("seq")
    b_full = own_b.astype(jnp.float32)
    c_full = own_c.astype(jnp.float32)
    grad_full = own_grad.astype(jnp.float32)

    state_now, total_now = block_state(own_inputs, own_b, own_decay)
    totals = gather_blocks(total_now, "seq")
    own_logs, peer_logs, prefixes = level_logs(totals, position, levels)
    uppers = [position // 2**level_index % 2 == 1 for level_index in range(levels)]

    unused, pull_carry = jax.vjp(
        mixer_carry, c_full, own_decay, own_weight[:, 1:, :],
        jnp.zeros((levels,) + state_now.shape, jnp.float32),
    )
    carry_grads = pull_carry(grad_full)[3]

    def group_grads(piece):
        piece_inputs, piece_decay, piece_weight, piece_grad = piece
        unused, pull = jax.vjp(
            mixer_local, piece_inputs.astype(jnp.float32), b_full, c_full, piece_decay, piece_weight
        )
        return pull(piece_grad.astype(jnp.float32))

    group_count = head_count // group
    pieces = [
        (
            own_inputs[:, g * group_width:(g + 1) * group_width],
            own_decay[:, g * group:(g + 1) * group],
            own_weight[:, 0, g * group:(g + 1) * group],
            own_grad[:, g * group_width:(g + 1) * group_width],
        )
        for g in range(group_count)
    ]
    step_groups = [[] for _ in range(levels)]
    for g in range(group_count):
        step_groups[min(g * levels // group_count, levels - 1)].append(g)
    group_results = [None] * group_count
    done_results = ()

    saved_own = [None] * levels
    saved_peer = [None] * levels
    carries = [None] * levels
    joined_grads = [None] * levels
    state_grad = jnp.where(position == 0, final_state_grad[0], 0.0)
    for step in range(levels):
        state_now, state_grad, step_pieces, done_results = lax.optimization_barrier(
            (state_now, state_grad, [pieces[g] for g in step_groups[step]], done_results)
        )
        for g, piece in zip(step_groups[step], step_pieces):
            group_results[g] = group_grads(piece)
        done_results = tuple(group_results[g] for g in step_groups[step])
        level_index = step
        upper = uppers[level_index]
        peer_state = exchange_state(state_now, level_index)
        saved_own[level_index] = state_now
        saved_peer[level_index] = peer_state
        carries[level_index] = jnp.where(
            upper, jnp.exp(prefixes[level_index])[:, None, None] * peer_state, 0.0
        )
        if level_index < levels - 1:
            state_now = jnp.where(
                upper,
                jnp.exp(own_logs[level_index])[:, None, None] * peer_state + state_now,
                jnp.exp(peer_logs[level_index])[:, None, None] * state_now + peer_state,
            )
        level_index = levels - 1 - step
        upper = uppers[level_index]
        joined_grads[level_index] = state_grad
        own_sg = jnp.where(
            upper, state_grad, jnp.exp(peer_logs[level_index])[:, None, None] * state_grad
        )
        peer_sg = jnp.where(
            upper,
            jnp.exp(own_logs[level_index])[:, None, None] * state_grad
            + jnp.exp(prefixes[level_index])[:, None, None] * carry_grads[level_index],
            state_grad,
        )
        state_grad = exchange_grad(own_sg, peer_sg, level_index)
    all_carries = jnp.stack(carries)

    unused, pull_carry = jax.vjp(mixer_carry, c_full, own_decay, own_weight[:, 1:, :], all_carries)
    c_carry, decay_carry, weight_carry, unused_grads = pull_carry(grad_full)

    own_log_grads = []
    peer_log_grads = []
    prefix_grads = []
    for level_index in range(levels):
        upper = uppers[level_index]
        joined_grad = joined_grads[level_index]
        with_peer = jnp.sum(joined_grad * saved_peer[level_index], axis=(1, 2))
        with_own = jnp.sum(joined_grad * saved_own[level_index], axis=(1, 2))
        carry_peer = jnp.sum(carry_grads[level_index] * saved_peer[level_index], axis=(1, 2))
        own_log_grads.append(jnp.where(upper, jnp.exp(own_logs[level_index]) * with_peer, 0.0))
        peer_log_grads.append(jnp.where(upper, 0.0, jnp.exp(peer_logs[level_index]) * with_own))
        prefix_grads.append(jnp.where(upper, jnp.exp(prefixes[level_index]) * carry_peer, 0.0))
    unused, pull_logs = jax.vjp(lambda t: level_logs(t, position, levels), totals)
    (totals_grad,) = pull_logs((own_log_grads, peer_log_grads, prefix_grads))
    totals_grad = sum_over(totals_grad, "seq")
    log_grad = lax.dynamic_index_in_dim(totals_grad, position, 0, keepdims=False)

    input_buf = jnp.concatenate([r[0] for r in group_results], axis=1)
    b_acc = sum(r[1] for r in group_results)
    c_acc = sum(r[2] for r in group_results)
    decay_buf = jnp.concatenate([r[3] for r in group_results], axis=1)
    weight_first = jnp.concatenate([r[4] for r in group_results], axis=1)

    factor, pulled = state_spread(own_b, own_decay, state_grad)
    b_extra, decay_extra = state_backward(
        own_inputs, own_decay, state_grad, log_grad, factor, pulled
    )
    input_grad = input_buf + (factor[:, :, None] * pulled).reshape(length, -1)
    upstream = passed_along(input_grad.astype(jnp.bfloat16), "section", -1)
    b_grad = b_acc + b_extra
    c_grad = c_acc + c_carry
    decay_grad = decay_buf + decay_carry + decay_extra
    weight_grad = jnp.concatenate([weight_first[:, None, :], weight_carry], axis=1)
    return (upstream[None], b_grad[None], c_grad[None], decay_grad[None], weight_grad[None])


def solution(mesh):
    return jax.shard_map(
        body,
        mesh=mesh,
        in_specs=(
            P("section", "seq", None),
            P("section", "seq", None),
            P("section", "seq", None),
            P("section", "seq", None),
            P("section", "seq", None, None),
            P("section", "seq", None),
            P("section", None, None, None),
        ),
        out_specs=(
            P("section", "seq", None),
            P("section", "seq", None),
            P("section", "seq", None),
            P("section", "seq", None),
            P("section", "seq", None, None),
        ),
        check_vma=False,
    )
```

```python
import jax
import jax.numpy as jnp
from jax import lax
from jax.sharding import PartitionSpec as P

highest = lax.Precision.HIGHEST


def from_partner(value, axis, apart):
    return lax.ppermute(value, axis, [(i, i ^ 1 << apart) for i in range(lax.axis_size(axis))])


def passed_along(block, axis, distance):
    devices = range(lax.axis_size(axis))
    route = [((i - distance) % len(devices), i) for i in devices]
    return lax.ppermute(block, axis, route)


def block_state(inputs, b_proj, decay_log):
    length, head_count = decay_log.shape
    running = jnp.cumsum(decay_log, axis=0)
    block_total = running[-1]
    factor = jnp.exp(block_total[None, :] - running)
    weighted = inputs.astype(jnp.float32).reshape(length, head_count, -1) * factor[:, :, None]
    state = jnp.einsum("tn,thp->hnp", b_proj.astype(jnp.float32), weighted, precision=highest)
    return (state, block_total)


def mixer_local(inputs, b_proj, c_proj, decay_log, first_weight):
    length, head_count = decay_log.shape
    running = jnp.cumsum(decay_log, axis=0)
    values = inputs.reshape(length, head_count, -1)
    scores = jnp.dot(c_proj, b_proj.T, precision=highest)
    causal = jnp.arange(length)[:, None] >= jnp.arange(length)[None, :]
    spread = running[:, None, :] - running[None, :, :]
    decays = jnp.exp(jnp.where(causal[:, :, None], spread, -jnp.inf))
    mixing = decays * scores[:, :, None]
    local_part = jnp.einsum("tsh,shp->thp", mixing, values, precision=highest)
    result = first_weight[:, :, None] * local_part
    return result.reshape(length, -1)


def mixer_carry(c_proj, decay_log, upper_weight, carries):
    length, head_count = decay_log.shape
    running = jnp.cumsum(decay_log, axis=0)
    lift = jnp.exp(running)
    result = jnp.zeros((length, head_count, carries.shape[-1]), jnp.float32)
    for level_index in range(carries.shape[0]):
        reach = jnp.einsum("tn,hnp->thp", c_proj, carries[level_index], precision=highest)
        result = result + (upper_weight[:, level_index, :] * lift)[:, :, None] * reach
    return result.reshape(length, -1)


def level_logs(totals, position, levels):
    count = totals.shape[0]
    index = jnp.arange(count)
    own, peer, prefix = [], [], []
    for level_index in range(levels):
        width = 1 << level_index
        base = position // width * width
        other = (position // width ^ 1) * width
        in_own = (index >= base) & (index < base + width)
        in_peer = (index >= other) & (index < other + width)
        in_prefix = (index >= base) & (index < position)
        own.append(jnp.sum(jnp.where(in_own[:, None], totals, 0.0), axis=0))
        peer.append(jnp.sum(jnp.where(in_peer[:, None], totals, 0.0), axis=0))
        prefix.append(jnp.sum(jnp.where(in_prefix[:, None], totals, 0.0), axis=0))
    return (own, peer, prefix)


def gather_blocks(value, axis):
    position = lax.axis_index(axis)
    blocks = value[None]
    for level_index in range(lax.axis_size(axis).bit_length() - 1):
        other = from_partner(blocks, axis, level_index)
        upper = position // 2**level_index % 2 == 1
        blocks = jnp.where(
            upper,
            jnp.concatenate([other, blocks], axis=0),
            jnp.concatenate([blocks, other], axis=0),
        )
    return blocks


def sum_over(value, axis):
    for level_index in range(lax.axis_size(axis).bit_length() - 1):
        value = value + from_partner(value, axis, level_index)
    return value


def halves_usable(state):
    return state.shape[0] % 2 == 0


def exchange_state(state, level_index):
    if level_index == 0 or not halves_usable(state):
        return from_partner(state, "seq", level_index)
    half = state.shape[0] // 2
    core = lax.axis_index("seq") % 2
    mine = lax.dynamic_slice_in_dim(state, core * half, half, 0)
    got = from_partner(mine, "seq", level_index)
    other = from_partner(got, "seq", 0)
    low = jnp.where(core == 0, got, other)
    high = jnp.where(core == 0, other, got)
    return jnp.concatenate([low, high], axis=0)


def exchange_grad(own_grad, peer_grad, level_index):
    if level_index == 0 or not halves_usable(peer_grad):
        return own_grad + from_partner(peer_grad, "seq", level_index)
    half = peer_grad.shape[0] // 2
    core = lax.axis_index("seq") % 2
    mine = lax.dynamic_slice_in_dim(peer_grad, core * half, half, 0)
    theirs = lax.dynamic_slice_in_dim(peer_grad, (1 - core) * half, half, 0)
    summed = mine + from_partner(theirs, "seq", 0)
    back = from_partner(summed, "seq", level_index)
    own_half = lax.dynamic_slice_in_dim(own_grad, core * half, half, 0)
    return lax.dynamic_update_slice_in_dim(own_grad, own_half + back, core * half, 0)


def state_spread(b_proj, decay_log, state_grad):
    running = jnp.cumsum(decay_log, axis=0)
    factor = jnp.exp(running[-1][None, :] - running)
    pulled = jnp.einsum("tn,hnp->thp", b_proj.astype(jnp.float32), state_grad, precision=highest)
    return (factor, pulled)


def state_backward(inputs, decay_log, state_grad, total_grad, factor, pulled):
    length, head_count = decay_log.shape
    values = inputs.astype(jnp.float32).reshape(length, head_count, -1)
    weighted = values * factor[:, :, None]
    b_grad = jnp.einsum("thp,hnp->tn", weighted, state_grad, precision=highest)
    log_grad = jnp.sum(values * pulled, axis=2) * factor
    running_grad = (-log_grad).at[-1].add(total_grad + jnp.sum(log_grad, axis=0))
    decay_grad = jnp.cumsum(running_grad[::-1], axis=0)[::-1]
    return (b_grad, decay_grad)


def body(inputs, b_proj, c_proj, decay_log, level_weight, out_grad, final_state_grad):
    own_inputs = inputs[0]
    own_b = b_proj[0]
    own_c = c_proj[0]
    own_decay = decay_log[0]
    own_weight = level_weight[0]
    own_grad = out_grad[0]
    length, head_count = own_decay.shape
    head_size = own_inputs.shape[1] // head_count
    group = 8
    group_width = group * head_size
    levels = lax.axis_size("seq").bit_length() - 1
    position = lax.axis_index("seq")
    b_full = own_b.astype(jnp.float32)
    c_full = own_c.astype(jnp.float32)
    grad_full = own_grad.astype(jnp.float32)

    state_now, total_now = block_state(own_inputs, own_b, own_decay)
    totals = gather_blocks(total_now, "seq")
    own_logs, peer_logs, prefixes = level_logs(totals, position, levels)
    uppers = [position // 2**level_index % 2 == 1 for level_index in range(levels)]

    unused, pull_carry = jax.vjp(
        mixer_carry, c_full, own_decay, own_weight[:, 1:, :],
        jnp.zeros((levels,) + state_now.shape, jnp.float32),
    )
    carry_grads = pull_carry(grad_full)[3]

    def group_grads(g, piece_decay):
        columns = slice(g * group_width, (g + 1) * group_width)
        heads = slice(g * group, (g + 1) * group)
        unused, pull = jax.vjp(
            mixer_local,
            own_inputs[:, columns].astype(jnp.float32),
            b_full,
            c_full,
            piece_decay,
            own_weight[:, 0, heads],
        )
        return pull(grad_full[:, columns])

    group_count = head_count // group
    step_groups = [[] for _ in range(levels)]
    for g in range(group_count):
        step_groups[min(g * levels // group_count, levels - 1)].append(g)
    group_results = [None] * group_count

    core = position % 2
    half = head_count // 2
    use_halves = head_count % 2 == 0

    def take_half(x, which):
        return lax.dynamic_slice_in_dim(x, which * half, half, 0)

    saved_own = [None] * levels
    saved_peer = [None] * levels
    carries = [None] * levels
    joined_grads = [None] * levels

    def fwd_pre(level_index, state):
        saved_own[level_index] = state
        if level_index == 0 or not use_halves:
            return state
        return take_half(state, core)

    def fwd_post(level_index, state, got):
        if level_index == 0 or not use_halves:
            peer_state = got
        else:
            other = from_partner(got, "seq", 0)
            low = jnp.where(core == 0, got, other)
            high = jnp.where(core == 0, other, got)
            peer_state = jnp.concatenate([low, high], axis=0)
        upper = uppers[level_index]
        saved_peer[level_index] = peer_state
        carries[level_index] = jnp.where(
            upper, jnp.exp(prefixes[level_index])[:, None, None] * peer_state, 0.0
        )
        if level_index == levels - 1:
            return None
        return jnp.where(
            upper,
            jnp.exp(own_logs[level_index])[:, None, None] * peer_state + state,
            jnp.exp(peer_logs[level_index])[:, None, None] * state + peer_state,
        )

    def bwd_pre(level_index, joined_grad):
        upper = uppers[level_index]
        joined_grads[level_index] = joined_grad
        own_sg = jnp.where(
            upper, joined_grad, jnp.exp(peer_logs[level_index])[:, None, None] * joined_grad
        )
        peer_sg = jnp.where(
            upper,
            jnp.exp(own_logs[level_index])[:, None, None] * joined_grad
            + jnp.exp(prefixes[level_index])[:, None, None] * carry_grads[level_index],
            joined_grad,
        )
        if level_index == 0 or not use_halves:
            return (own_sg, peer_sg)
        summed = take_half(peer_sg, core) + from_partner(take_half(peer_sg, 1 - core), "seq", 0)
        return (own_sg, summed)

    def bwd_post(level_index, own_sg, back):
        if level_index == 0 or not use_halves:
            return own_sg + back
        own_half = take_half(own_sg, core)
        return lax.dynamic_update_slice_in_dim(own_sg, own_half + back, core * half, 0)

    def run_groups(step, gates):
        for g, gate in zip(step_groups[step], gates):
            group_results[g] = group_grads(g, gate)
        return tuple(group_results[g] for g in step_groups[step])

    def gates_of(step):
        return [own_decay[:, g * group:(g + 1) * group] for g in step_groups[step]]

    fwd_send = fwd_pre(0, state_now)
    bwd_own, bwd_send = bwd_pre(levels - 1, jnp.where(position == 0, final_state_grad[0], 0.0))
    fwd_send, gates = lax.optimization_barrier((fwd_send, gates_of(0)))
    got = from_partner(fwd_send, "seq", 0)
    finished = run_groups(0, gates)
    state_now = fwd_post(0, state_now, got)
    for step in range(1, levels):
        fwd_send = fwd_pre(step, state_now)
        fwd_send, bwd_send, gates, finished = lax.optimization_barrier(
            (fwd_send, bwd_send, gates_of(step), finished)
        )
        got = from_partner(fwd_send, "seq", step)
        back = from_partner(bwd_send, "seq", levels - step)
        finished = run_groups(step, gates)
        state_now = fwd_post(step, state_now, got)
        state_grad = bwd_post(levels - step, bwd_own, back)
        bwd_own, bwd_send = bwd_pre(levels - step - 1, state_grad)
    state_grad = bwd_post(0, bwd_own, from_partner(bwd_send, "seq", 0))
    all_carries = jnp.stack(carries)

    unused, pull_carry = jax.vjp(mixer_carry, c_full, own_decay, own_weight[:, 1:, :], all_carries)
    c_carry, decay_carry, weight_carry, unused_grads = pull_carry(grad_full)

    own_log_grads = []
    peer_log_grads = []
    prefix_grads = []
    for level_index in range(levels):
        upper = uppers[level_index]
        joined_grad = joined_grads[level_index]
        with_peer = jnp.sum(joined_grad * saved_peer[level_index], axis=(1, 2))
        with_own = jnp.sum(joined_grad * saved_own[level_index], axis=(1, 2))
        carry_peer = jnp.sum(carry_grads[level_index] * saved_peer[level_index], axis=(1, 2))
        own_log_grads.append(jnp.where(upper, jnp.exp(own_logs[level_index]) * with_peer, 0.0))
        peer_log_grads.append(jnp.where(upper, 0.0, jnp.exp(peer_logs[level_index]) * with_own))
        prefix_grads.append(jnp.where(upper, jnp.exp(prefixes[level_index]) * carry_peer, 0.0))
    unused, pull_logs = jax.vjp(lambda t: level_logs(t, position, levels), totals)
    (totals_grad,) = pull_logs((own_log_grads, peer_log_grads, prefix_grads))
    totals_grad = sum_over(totals_grad, "seq")
    log_grad = lax.dynamic_index_in_dim(totals_grad, position, 0, keepdims=False)

    input_buf = jnp.concatenate([r[0] for r in group_results], axis=1)
    b_acc = sum(r[1] for r in group_results)
    c_acc = sum(r[2] for r in group_results)
    decay_buf = jnp.concatenate([r[3] for r in group_results], axis=1)
    weight_first = jnp.concatenate([r[4] for r in group_results], axis=1)

    factor, pulled = state_spread(own_b, own_decay, state_grad)
    b_extra, decay_extra = state_backward(
        own_inputs, own_decay, state_grad, log_grad, factor, pulled
    )
    input_grad = input_buf + (factor[:, :, None] * pulled).reshape(length, -1)
    upstream = passed_along(input_grad.astype(jnp.bfloat16), "section", -1)
    b_grad = b_acc + b_extra
    c_grad = c_acc + c_carry
    decay_grad = decay_buf + decay_carry + decay_extra
    weight_grad = jnp.concatenate([weight_first[:, None, :], weight_carry], axis=1)
    return (upstream[None], b_grad[None], c_grad[None], decay_grad[None], weight_grad[None])


def solution(mesh):
    return jax.shard_map(
        body,
        mesh=mesh,
        in_specs=(
            P("section", "seq", None),
            P("section", "seq", None),
            P("section", "seq", None),
            P("section", "seq", None),
            P("section", "seq", None, None),
            P("section", "seq", None),
            P("section", None, None, None),
        ),
        out_specs=(
            P("section", "seq", None),
            P("section", "seq", None),
            P("section", "seq", None),
            P("section", "seq", None),
            P("section", "seq", None, None),
        ),
        check_vma=False,
    )
```

```python
import jax
import jax.numpy as jnp
from jax import lax
from jax.experimental import pallas as pl
from jax.experimental.pallas import tpu as pltpu
from jax.sharding import PartitionSpec as P

highest = lax.Precision.HIGHEST


def from_partner(value, axis, apart):
    return lax.ppermute(value, axis, [(i, i ^ 1 << apart) for i in range(lax.axis_size(axis))])


def passed_along(block, axis, distance):
    devices = range(lax.axis_size(axis))
    route = [((i - distance) % len(devices), i) for i in devices]
    return lax.ppermute(block, axis, route)


def block_state(inputs, b_proj, decay_log):
    length, head_count = decay_log.shape
    running = jnp.cumsum(decay_log, axis=0)
    block_total = running[-1]
    factor = jnp.exp(block_total[None, :] - running)
    weighted = inputs.astype(jnp.float32).reshape(length, head_count, -1) * factor[:, :, None]
    state = jnp.einsum("tn,thp->hnp", b_proj.astype(jnp.float32), weighted, precision=highest)
    return (state, block_total)


def mixer_local(inputs, b_proj, c_proj, decay_log, first_weight):
    length, head_count = decay_log.shape
    running = jnp.cumsum(decay_log, axis=0)
    values = inputs.reshape(length, head_count, -1)
    scores = jnp.dot(c_proj, b_proj.T, precision=highest)
    causal = jnp.arange(length)[:, None] >= jnp.arange(length)[None, :]
    spread = running[:, None, :] - running[None, :, :]
    decays = jnp.exp(jnp.where(causal[:, :, None], spread, -jnp.inf))
    mixing = decays * scores[:, :, None]
    local_part = jnp.einsum("tsh,shp->thp", mixing, values, precision=highest)
    result = first_weight[:, :, None] * local_part
    return result.reshape(length, -1)


def split_dot(a, b, dims):
    return lax.dot_general(
        a.astype(jnp.float32),
        b.astype(jnp.float32),
        (dims, ((), ())),
        precision=highest,
        preferred_element_type=jnp.float32,
    )


def local_kernel(heads, head_size, x_ref, g_ref, rc_ref, rr_ref, w_ref, sc_ref,
                 dx_ref, dw_ref, drc_ref, drr_ref, dsc_ref):
    scores = sc_ref[...]
    length = scores.shape[0]
    rows = lax.broadcasted_iota(jnp.int32, (length, length), 0)
    cols = lax.broadcasted_iota(jnp.int32, (length, length), 1)
    causal = rows >= cols
    score_grad = jnp.zeros((length, length), jnp.float32)
    for j, h in enumerate(heads):
        x = x_ref[:, h * head_size:(h + 1) * head_size]
        g = g_ref[:, h * head_size:(h + 1) * head_size].astype(jnp.float32)
        decays = jnp.where(causal, jnp.exp(rc_ref[:, h:h + 1] - rr_ref[h:h + 1, :]), 0.0)
        mixing = decays * scores
        local = split_dot(mixing, x, ((1,), (0,)))
        local_grad = w_ref[:, h:h + 1] * g
        dw_ref[:, j:j + 1] = jnp.sum(g * local, axis=1, keepdims=True)
        dx_ref[:, j * head_size:(j + 1) * head_size] = split_dot(
            jnp.transpose(mixing), local_grad, ((1,), (0,))
        )
        mixing_grad = split_dot(local_grad, x, ((1,), (1,)))
        score_grad = score_grad + mixing_grad * decays
        spread_grad = mixing_grad * scores * decays
        drc_ref[:, j:j + 1] = jnp.sum(spread_grad, axis=1, keepdims=True)
        drr_ref[j:j + 1, :] = jnp.sum(spread_grad, axis=0, keepdims=True)
    dsc_ref[...] = score_grad


def local_grads(heads, inputs, grad, running_col, running_row, first_weight, scores):
    length = inputs.shape[0]
    head_size = inputs.shape[1] // running_col.shape[1]
    count = len(heads)
    vmem = pl.BlockSpec(memory_space=pltpu.VMEM)
    flops = count * 7 * 2 * length * length * head_size
    return pl.pallas_call(
        lambda *refs: local_kernel(heads, head_size, *refs),
        out_shape=(
            jax.ShapeDtypeStruct((length, count * head_size), jnp.float32),
            jax.ShapeDtypeStruct((length, count), jnp.float32),
            jax.ShapeDtypeStruct((length, count), jnp.float32),
            jax.ShapeDtypeStruct((count, length), jnp.float32),
            jax.ShapeDtypeStruct((length, length), jnp.float32),
        ),
        in_specs=[vmem] * 6,
        out_specs=(vmem,) * 5,
        cost_estimate=pl.CostEstimate(
            flops=flops,
            transcendentals=count * length * length,
            bytes_accessed=2 * length * inputs.shape[1] * 2 + count * length * head_size * 4,
        ),
    )(inputs, grad, running_col, running_row, first_weight, scores)


def mixer_carry(c_proj, decay_log, upper_weight, carries):
    length, head_count = decay_log.shape
    running = jnp.cumsum(decay_log, axis=0)
    lift = jnp.exp(running)
    result = jnp.zeros((length, head_count, carries.shape[-1]), jnp.float32)
    for level_index in range(carries.shape[0]):
        reach = jnp.einsum("tn,hnp->thp", c_proj, carries[level_index], precision=highest)
        result = result + (upper_weight[:, level_index, :] * lift)[:, :, None] * reach
    return result.reshape(length, -1)


def level_logs(totals, position, levels):
    count = totals.shape[0]
    index = jnp.arange(count)
    own, peer, prefix = [], [], []
    for level_index in range(levels):
        width = 1 << level_index
        base = position // width * width
        other = (position // width ^ 1) * width
        in_own = (index >= base) & (index < base + width)
        in_peer = (index >= other) & (index < other + width)
        in_prefix = (index >= base) & (index < position)
        own.append(jnp.sum(jnp.where(in_own[:, None], totals, 0.0), axis=0))
        peer.append(jnp.sum(jnp.where(in_peer[:, None], totals, 0.0), axis=0))
        prefix.append(jnp.sum(jnp.where(in_prefix[:, None], totals, 0.0), axis=0))
    return (own, peer, prefix)


def gather_blocks(value, axis):
    position = lax.axis_index(axis)
    blocks = value[None]
    for level_index in range(lax.axis_size(axis).bit_length() - 1):
        other = from_partner(blocks, axis, level_index)
        upper = position // 2**level_index % 2 == 1
        blocks = jnp.where(
            upper,
            jnp.concatenate([other, blocks], axis=0),
            jnp.concatenate([blocks, other], axis=0),
        )
    return blocks


def sum_over(value, axis):
    for level_index in range(lax.axis_size(axis).bit_length() - 1):
        value = value + from_partner(value, axis, level_index)
    return value


def halves_usable(state):
    return state.shape[0] % 2 == 0


def exchange_state(state, level_index):
    if level_index == 0 or not halves_usable(state):
        return from_partner(state, "seq", level_index)
    half = state.shape[0] // 2
    core = lax.axis_index("seq") % 2
    mine = lax.dynamic_slice_in_dim(state, core * half, half, 0)
    got = from_partner(mine, "seq", level_index)
    other = from_partner(got, "seq", 0)
    low = jnp.where(core == 0, got, other)
    high = jnp.where(core == 0, other, got)
    return jnp.concatenate([low, high], axis=0)


def exchange_grad(own_grad, peer_grad, level_index):
    if level_index == 0 or not halves_usable(peer_grad):
        return own_grad + from_partner(peer_grad, "seq", level_index)
    half = peer_grad.shape[0] // 2
    core = lax.axis_index("seq") % 2
    mine = lax.dynamic_slice_in_dim(peer_grad, core * half, half, 0)
    theirs = lax.dynamic_slice_in_dim(peer_grad, (1 - core) * half, half, 0)
    summed = mine + from_partner(theirs, "seq", 0)
    back = from_partner(summed, "seq", level_index)
    own_half = lax.dynamic_slice_in_dim(own_grad, core * half, half, 0)
    return lax.dynamic_update_slice_in_dim(own_grad, own_half + back, core * half, 0)


def state_spread(b_proj, decay_log, state_grad):
    running = jnp.cumsum(decay_log, axis=0)
    factor = jnp.exp(running[-1][None, :] - running)
    pulled = jnp.einsum("tn,hnp->thp", b_proj.astype(jnp.float32), state_grad, precision=highest)
    return (factor, pulled)


def state_backward(inputs, decay_log, state_grad, total_grad, factor, pulled):
    length, head_count = decay_log.shape
    values = inputs.astype(jnp.float32).reshape(length, head_count, -1)
    weighted = values * factor[:, :, None]
    b_grad = jnp.einsum("thp,hnp->tn", weighted, state_grad, precision=highest)
    log_grad = jnp.sum(values * pulled, axis=2) * factor
    running_grad = (-log_grad).at[-1].add(total_grad + jnp.sum(log_grad, axis=0))
    decay_grad = jnp.cumsum(running_grad[::-1], axis=0)[::-1]
    return (b_grad, decay_grad)


def body(inputs, b_proj, c_proj, decay_log, level_weight, out_grad, final_state_grad):
    own_inputs = inputs[0]
    own_b = b_proj[0]
    own_c = c_proj[0]
    own_decay = decay_log[0]
    own_weight = level_weight[0]
    own_grad = out_grad[0]
    length, head_count = own_decay.shape
    head_size = own_inputs.shape[1] // head_count
    group = 8
    group_width = group * head_size
    levels = lax.axis_size("seq").bit_length() - 1
    position = lax.axis_index("seq")
    b_full = own_b.astype(jnp.float32)
    c_full = own_c.astype(jnp.float32)
    grad_full = own_grad.astype(jnp.float32)

    state_now, total_now = block_state(own_inputs, own_b, own_decay)
    totals = gather_blocks(total_now, "seq")
    own_logs, peer_logs, prefixes = level_logs(totals, position, levels)
    uppers = [position // 2**level_index % 2 == 1 for level_index in range(levels)]

    unused, pull_carry = jax.vjp(
        mixer_carry, c_full, own_decay, own_weight[:, 1:, :],
        jnp.zeros((levels,) + state_now.shape, jnp.float32),
    )
    carry_grads = pull_carry(grad_full)[3]

    running_col = jnp.cumsum(own_decay, axis=0)
    running_row = jnp.transpose(running_col)
    first_weight = own_weight[:, 0, :]
    scores = jnp.dot(c_full, b_full.T, precision=highest)

    def group_grads(g, gate):
        gate_col, gate_row = gate
        return local_grads(
            tuple(range(g * group, (g + 1) * group)), own_inputs, own_grad, gate_col, gate_row,
            first_weight, scores,
        )

    group_count = head_count // group
    step_groups = [[] for _ in range(levels)]
    for g in range(group_count):
        step_groups[min(g * levels // group_count, levels - 1)].append(g)
    group_results = [None] * group_count

    core = position % 2
    half = head_count // 2
    use_halves = head_count % 2 == 0

    def take_half(x, which):
        return lax.dynamic_slice_in_dim(x, which * half, half, 0)

    saved_own = [None] * levels
    saved_peer = [None] * levels
    carries = [None] * levels
    joined_grads = [None] * levels

    def fwd_pre(level_index, state):
        saved_own[level_index] = state
        if level_index == 0 or not use_halves:
            return state
        return take_half(state, core)

    def fwd_post(level_index, state, got):
        if level_index == 0 or not use_halves:
            peer_state = got
        else:
            other = from_partner(got, "seq", 0)
            low = jnp.where(core == 0, got, other)
            high = jnp.where(core == 0, other, got)
            peer_state = jnp.concatenate([low, high], axis=0)
        upper = uppers[level_index]
        saved_peer[level_index] = peer_state
        carries[level_index] = jnp.where(
            upper, jnp.exp(prefixes[level_index])[:, None, None] * peer_state, 0.0
        )
        if level_index == levels - 1:
            return None
        return jnp.where(
            upper,
            jnp.exp(own_logs[level_index])[:, None, None] * peer_state + state,
            jnp.exp(peer_logs[level_index])[:, None, None] * state + peer_state,
        )

    def bwd_pre(level_index, joined_grad):
        upper = uppers[level_index]
        joined_grads[level_index] = joined_grad
        own_sg = jnp.where(
            upper, joined_grad, jnp.exp(peer_logs[level_index])[:, None, None] * joined_grad
        )
        peer_sg = jnp.where(
            upper,
            jnp.exp(own_logs[level_index])[:, None, None] * joined_grad
            + jnp.exp(prefixes[level_index])[:, None, None] * carry_grads[level_index],
            joined_grad,
        )
        if level_index == 0 or not use_halves:
            return (own_sg, peer_sg)
        summed = take_half(peer_sg, core) + from_partner(take_half(peer_sg, 1 - core), "seq", 0)
        return (own_sg, summed)

    def bwd_post(level_index, own_sg, back):
        if level_index == 0 or not use_halves:
            return own_sg + back
        own_half = take_half(own_sg, core)
        return lax.dynamic_update_slice_in_dim(own_sg, own_half + back, core * half, 0)

    def run_groups(step, gates):
        for g, gate in zip(step_groups[step], gates):
            group_results[g] = group_grads(g, gate)
        return tuple(group_results[g] for g in step_groups[step])

    def gates_of(step):
        return [(running_col, running_row) for g in step_groups[step]]

    fwd_send = fwd_pre(0, state_now)
    bwd_own, bwd_send = bwd_pre(levels - 1, jnp.where(position == 0, final_state_grad[0], 0.0))
    fwd_send, gates = lax.optimization_barrier((fwd_send, gates_of(0)))
    got = from_partner(fwd_send, "seq", 0)
    finished = run_groups(0, gates)
    state_now = fwd_post(0, state_now, got)
    for step in range(1, levels):
        fwd_send = fwd_pre(step, state_now)
        fwd_send, bwd_send, gates, finished = lax.optimization_barrier(
            (fwd_send, bwd_send, gates_of(step), finished)
        )
        got = from_partner(fwd_send, "seq", step)
        back = from_partner(bwd_send, "seq", levels - step)
        finished = run_groups(step, gates)
        state_now = fwd_post(step, state_now, got)
        state_grad = bwd_post(levels - step, bwd_own, back)
        bwd_own, bwd_send = bwd_pre(levels - step - 1, state_grad)
    state_grad = bwd_post(0, bwd_own, from_partner(bwd_send, "seq", 0))
    all_carries = jnp.stack(carries)

    unused, pull_carry = jax.vjp(mixer_carry, c_full, own_decay, own_weight[:, 1:, :], all_carries)
    c_carry, decay_carry, weight_carry, unused_grads = pull_carry(grad_full)

    own_log_grads = []
    peer_log_grads = []
    prefix_grads = []
    for level_index in range(levels):
        upper = uppers[level_index]
        joined_grad = joined_grads[level_index]
        with_peer = jnp.sum(joined_grad * saved_peer[level_index], axis=(1, 2))
        with_own = jnp.sum(joined_grad * saved_own[level_index], axis=(1, 2))
        carry_peer = jnp.sum(carry_grads[level_index] * saved_peer[level_index], axis=(1, 2))
        own_log_grads.append(jnp.where(upper, jnp.exp(own_logs[level_index]) * with_peer, 0.0))
        peer_log_grads.append(jnp.where(upper, 0.0, jnp.exp(peer_logs[level_index]) * with_own))
        prefix_grads.append(jnp.where(upper, jnp.exp(prefixes[level_index]) * carry_peer, 0.0))
    unused, pull_logs = jax.vjp(lambda t: level_logs(t, position, levels), totals)
    (totals_grad,) = pull_logs((own_log_grads, peer_log_grads, prefix_grads))
    totals_grad = sum_over(totals_grad, "seq")
    log_grad = lax.dynamic_index_in_dim(totals_grad, position, 0, keepdims=False)

    input_buf = jnp.concatenate([r[0] for r in group_results], axis=1)
    weight_first = jnp.concatenate([r[1] for r in group_results], axis=1)
    running_grad = jnp.concatenate([r[2] for r in group_results], axis=1) - jnp.transpose(
        jnp.concatenate([r[3] for r in group_results], axis=0)
    )
    decay_buf = jnp.cumsum(running_grad[::-1], axis=0)[::-1]
    score_grad = sum(r[4] for r in group_results)
    c_acc = jnp.dot(score_grad, b_full, precision=highest)
    b_acc = jnp.dot(score_grad.T, c_full, precision=highest)

    factor, pulled = state_spread(own_b, own_decay, state_grad)
    b_extra, decay_extra = state_backward(
        own_inputs, own_decay, state_grad, log_grad, factor, pulled
    )
    input_grad = input_buf + (factor[:, :, None] * pulled).reshape(length, -1)
    upstream = passed_along(input_grad.astype(jnp.bfloat16), "section", -1)
    b_grad = b_acc + b_extra
    c_grad = c_acc + c_carry
    decay_grad = decay_buf + decay_carry + decay_extra
    weight_grad = jnp.concatenate([weight_first[:, None, :], weight_carry], axis=1)
    return (upstream[None], b_grad[None], c_grad[None], decay_grad[None], weight_grad[None])


def solution(mesh):
    return jax.shard_map(
        body,
        mesh=mesh,
        in_specs=(
            P("section", "seq", None),
            P("section", "seq", None),
            P("section", "seq", None),
            P("section", "seq", None),
            P("section", "seq", None, None),
            P("section", "seq", None),
            P("section", None, None, None),
        ),
        out_specs=(
            P("section", "seq", None),
            P("section", "seq", None),
            P("section", "seq", None),
            P("section", "seq", None),
            P("section", "seq", None, None),
        ),
        check_vma=False,
    )
```

```python
import jax
import jax.numpy as jnp
from jax import lax
from jax.experimental import pallas as pl
from jax.experimental.pallas import tpu as pltpu
from jax.sharding import PartitionSpec as P

highest = lax.Precision.HIGHEST


def from_partner(value, axis, apart):
    return lax.ppermute(value, axis, [(i, i ^ 1 << apart) for i in range(lax.axis_size(axis))])


def passed_along(block, axis, distance):
    devices = range(lax.axis_size(axis))
    route = [((i - distance) % len(devices), i) for i in devices]
    return lax.ppermute(block, axis, route)


def block_state(inputs, b_proj, decay_log):
    length, head_count = decay_log.shape
    running = jnp.cumsum(decay_log, axis=0)
    block_total = running[-1]
    factor = jnp.exp(block_total[None, :] - running)
    weighted = inputs.astype(jnp.float32).reshape(length, head_count, -1) * factor[:, :, None]
    state = jnp.einsum("tn,thp->hnp", b_proj.astype(jnp.float32), weighted, precision=highest)
    return (state, block_total)


def mixer_local(inputs, b_proj, c_proj, decay_log, first_weight):
    length, head_count = decay_log.shape
    running = jnp.cumsum(decay_log, axis=0)
    values = inputs.reshape(length, head_count, -1)
    scores = jnp.dot(c_proj, b_proj.T, precision=highest)
    causal = jnp.arange(length)[:, None] >= jnp.arange(length)[None, :]
    spread = running[:, None, :] - running[None, :, :]
    decays = jnp.exp(jnp.where(causal[:, :, None], spread, -jnp.inf))
    mixing = decays * scores[:, :, None]
    local_part = jnp.einsum("tsh,shp->thp", mixing, values, precision=highest)
    result = first_weight[:, :, None] * local_part
    return result.reshape(length, -1)


def split_dot(a, b, dims):
    return lax.dot_general(
        a.astype(jnp.float32),
        b.astype(jnp.float32),
        (dims, ((), ())),
        precision=highest,
        preferred_element_type=jnp.float32,
    )


def local_kernel(heads, head_size, x_ref, g_ref, rc_ref, rr_ref, w_ref, sc_ref,
                 dx_ref, dw_ref, dr_ref, dsc_ref):
    scores = sc_ref[...]
    length = scores.shape[0]
    rows = lax.broadcasted_iota(jnp.int32, (length, length), 0)
    cols = lax.broadcasted_iota(jnp.int32, (length, length), 1)
    causal = rows >= cols
    score_grad = jnp.zeros((length, length), jnp.float32)
    ones_p = jnp.ones((1, head_size), jnp.float32)
    ones_t = jnp.ones((1, length), jnp.float32)
    for j, h in enumerate(heads):
        x = x_ref[:, h * head_size:(h + 1) * head_size]
        g = g_ref[:, h * head_size:(h + 1) * head_size].astype(jnp.float32)
        decays = jnp.where(causal, jnp.exp(rc_ref[:, h:h + 1] - rr_ref[h:h + 1, :]), 0.0)
        mixing = decays * scores
        local = split_dot(mixing, x, ((1,), (0,)))
        local_grad = w_ref[:, h:h + 1] * g
        dw_ref[j:j + 1, :] = split_dot(ones_p, g * local, ((1,), (1,)))
        dx_ref[:, j * head_size:(j + 1) * head_size] = split_dot(
            jnp.transpose(mixing), local_grad, ((1,), (0,))
        )
        mixing_grad = split_dot(local_grad, x, ((1,), (1,)))
        score_grad = score_grad + mixing_grad * decays
        spread_grad = mixing_grad * scores * decays
        dr_ref[j:j + 1, :] = split_dot(ones_t, spread_grad, ((1,), (1,))) - jnp.sum(
            spread_grad, axis=0, keepdims=True
        )
    dsc_ref[...] = score_grad


def local_grads(heads, inputs, grad, running_col, running_row, first_weight, scores):
    length = inputs.shape[0]
    head_size = inputs.shape[1] // running_col.shape[1]
    count = len(heads)
    vmem = pl.BlockSpec(memory_space=pltpu.VMEM)
    flops = count * 7 * 2 * length * length * head_size
    return pl.pallas_call(
        lambda *refs: local_kernel(heads, head_size, *refs),
        out_shape=(
            jax.ShapeDtypeStruct((length, count * head_size), jnp.float32),
            jax.ShapeDtypeStruct((count, length), jnp.float32),
            jax.ShapeDtypeStruct((count, length), jnp.float32),
            jax.ShapeDtypeStruct((length, length), jnp.float32),
        ),
        in_specs=[vmem] * 6,
        out_specs=(vmem,) * 4,
        cost_estimate=pl.CostEstimate(
            flops=flops,
            transcendentals=count * length * length,
            bytes_accessed=2 * length * inputs.shape[1] * 2 + count * length * head_size * 4,
        ),
    )(inputs, grad, running_col, running_row, first_weight, scores)


def mixer_carry(c_proj, decay_log, upper_weight, carries):
    length, head_count = decay_log.shape
    running = jnp.cumsum(decay_log, axis=0)
    lift = jnp.exp(running)
    result = jnp.zeros((length, head_count, carries.shape[-1]), jnp.float32)
    for level_index in range(carries.shape[0]):
        reach = jnp.einsum("tn,hnp->thp", c_proj, carries[level_index], precision=highest)
        result = result + (upper_weight[:, level_index, :] * lift)[:, :, None] * reach
    return result.reshape(length, -1)


def level_logs(totals, position, levels):
    count = totals.shape[0]
    index = jnp.arange(count)
    own, peer, prefix = [], [], []
    for level_index in range(levels):
        width = 1 << level_index
        base = position // width * width
        other = (position // width ^ 1) * width
        in_own = (index >= base) & (index < base + width)
        in_peer = (index >= other) & (index < other + width)
        in_prefix = (index >= base) & (index < position)
        own.append(jnp.sum(jnp.where(in_own[:, None], totals, 0.0), axis=0))
        peer.append(jnp.sum(jnp.where(in_peer[:, None], totals, 0.0), axis=0))
        prefix.append(jnp.sum(jnp.where(in_prefix[:, None], totals, 0.0), axis=0))
    return (own, peer, prefix)


def gather_blocks(value, axis):
    position = lax.axis_index(axis)
    blocks = value[None]
    for level_index in range(lax.axis_size(axis).bit_length() - 1):
        other = from_partner(blocks, axis, level_index)
        upper = position // 2**level_index % 2 == 1
        blocks = jnp.where(
            upper,
            jnp.concatenate([other, blocks], axis=0),
            jnp.concatenate([blocks, other], axis=0),
        )
    return blocks


def sum_over(value, axis):
    for level_index in range(lax.axis_size(axis).bit_length() - 1):
        value = value + from_partner(value, axis, level_index)
    return value


def halves_usable(state):
    return state.shape[0] % 2 == 0


def exchange_state(state, level_index):
    if level_index == 0 or not halves_usable(state):
        return from_partner(state, "seq", level_index)
    half = state.shape[0] // 2
    core = lax.axis_index("seq") % 2
    mine = lax.dynamic_slice_in_dim(state, core * half, half, 0)
    got = from_partner(mine, "seq", level_index)
    other = from_partner(got, "seq", 0)
    low = jnp.where(core == 0, got, other)
    high = jnp.where(core == 0, other, got)
    return jnp.concatenate([low, high], axis=0)


def exchange_grad(own_grad, peer_grad, level_index):
    if level_index == 0 or not halves_usable(peer_grad):
        return own_grad + from_partner(peer_grad, "seq", level_index)
    half = peer_grad.shape[0] // 2
    core = lax.axis_index("seq") % 2
    mine = lax.dynamic_slice_in_dim(peer_grad, core * half, half, 0)
    theirs = lax.dynamic_slice_in_dim(peer_grad, (1 - core) * half, half, 0)
    summed = mine + from_partner(theirs, "seq", 0)
    back = from_partner(summed, "seq", level_index)
    own_half = lax.dynamic_slice_in_dim(own_grad, core * half, half, 0)
    return lax.dynamic_update_slice_in_dim(own_grad, own_half + back, core * half, 0)


def state_spread(b_proj, decay_log, state_grad):
    running = jnp.cumsum(decay_log, axis=0)
    factor = jnp.exp(running[-1][None, :] - running)
    pulled = jnp.einsum("tn,hnp->thp", b_proj.astype(jnp.float32), state_grad, precision=highest)
    return (factor, pulled)


def state_backward(inputs, decay_log, state_grad, total_grad, factor, pulled):
    length, head_count = decay_log.shape
    values = inputs.astype(jnp.float32).reshape(length, head_count, -1)
    weighted = values * factor[:, :, None]
    b_grad = jnp.einsum("thp,hnp->tn", weighted, state_grad, precision=highest)
    log_grad = jnp.sum(values * pulled, axis=2) * factor
    running_grad = (-log_grad).at[-1].add(total_grad + jnp.sum(log_grad, axis=0))
    decay_grad = jnp.cumsum(running_grad[::-1], axis=0)[::-1]
    return (b_grad, decay_grad)


def body(inputs, b_proj, c_proj, decay_log, level_weight, out_grad, final_state_grad):
    own_inputs = inputs[0]
    own_b = b_proj[0]
    own_c = c_proj[0]
    own_decay = decay_log[0]
    own_weight = level_weight[0]
    own_grad = out_grad[0]
    length, head_count = own_decay.shape
    head_size = own_inputs.shape[1] // head_count
    group = 8
    group_width = group * head_size
    levels = lax.axis_size("seq").bit_length() - 1
    position = lax.axis_index("seq")
    b_full = own_b.astype(jnp.float32)
    c_full = own_c.astype(jnp.float32)
    grad_full = own_grad.astype(jnp.float32)

    state_now, total_now = block_state(own_inputs, own_b, own_decay)
    totals = gather_blocks(total_now, "seq")
    own_logs, peer_logs, prefixes = level_logs(totals, position, levels)
    lifted = jnp.exp(jnp.stack(own_logs + peer_logs + prefixes))
    own_lifts = [lifted[k] for k in range(levels)]
    peer_lifts = [lifted[levels + k] for k in range(levels)]
    prefix_lifts = [lifted[2 * levels + k] for k in range(levels)]
    uppers = [position // 2**level_index % 2 == 1 for level_index in range(levels)]

    unused, pull_carry = jax.vjp(
        mixer_carry, c_full, own_decay, own_weight[:, 1:, :],
        jnp.zeros((levels,) + state_now.shape, jnp.float32),
    )
    carry_grads = pull_carry(grad_full)[3]

    running_col = jnp.cumsum(own_decay, axis=0)
    running_row = jnp.transpose(running_col)
    first_weight = own_weight[:, 0, :]
    scores = jnp.dot(c_full, b_full.T, precision=highest)

    def group_grads(g, gate):
        gate_col, gate_row = gate
        return local_grads(
            tuple(range(g * group, (g + 1) * group)), own_inputs, own_grad, gate_col, gate_row,
            first_weight, scores,
        )

    group_count = head_count // group
    step_groups = [[] for _ in range(levels)]
    for g in range(group_count):
        step_groups[min(g * levels // group_count, levels - 1)].append(g)
    group_results = [None] * group_count

    core = position % 2
    half = head_count // 2
    use_halves = head_count % 2 == 0

    def take_half(x, which):
        return lax.dynamic_slice_in_dim(x, which * half, half, 0)

    saved_own = [None] * levels
    saved_peer = [None] * levels
    carries = [None] * levels
    joined_grads = [None] * levels

    def fwd_pre(level_index, state):
        saved_own[level_index] = state
        if level_index == 0 or not use_halves:
            return state
        return take_half(state, core)

    def fwd_post(level_index, state, got):
        if level_index == 0 or not use_halves:
            peer_state = got
        else:
            other = from_partner(got, "seq", 0)
            low = jnp.where(core == 0, got, other)
            high = jnp.where(core == 0, other, got)
            peer_state = jnp.concatenate([low, high], axis=0)
        upper = uppers[level_index]
        saved_peer[level_index] = peer_state
        carries[level_index] = jnp.where(
            upper, prefix_lifts[level_index][:, None, None] * peer_state, 0.0
        )
        if level_index == levels - 1:
            return None
        return jnp.where(
            upper,
            own_lifts[level_index][:, None, None] * peer_state + state,
            peer_lifts[level_index][:, None, None] * state + peer_state,
        )

    def bwd_pre(level_index, joined_grad):
        upper = uppers[level_index]
        joined_grads[level_index] = joined_grad
        own_sg = jnp.where(
            upper, joined_grad, peer_lifts[level_index][:, None, None] * joined_grad
        )
        peer_sg = jnp.where(
            upper,
            own_lifts[level_index][:, None, None] * joined_grad
            + prefix_lifts[level_index][:, None, None] * carry_grads[level_index],
            joined_grad,
        )
        if level_index == 0 or not use_halves:
            return (own_sg, peer_sg)
        summed = take_half(peer_sg, core) + from_partner(take_half(peer_sg, 1 - core), "seq", 0)
        return (own_sg, summed)

    def bwd_post(level_index, own_sg, back):
        if level_index == 0 or not use_halves:
            return own_sg + back
        own_half = take_half(own_sg, core)
        return lax.dynamic_update_slice_in_dim(own_sg, own_half + back, core * half, 0)

    def run_groups(step, gates):
        for g, gate in zip(step_groups[step], gates):
            group_results[g] = group_grads(g, gate)
        return tuple(group_results[g] for g in step_groups[step])

    def gates_of(step):
        return [(running_col, running_row) for g in step_groups[step]]

    fwd_send = fwd_pre(0, state_now)
    bwd_own, bwd_send = bwd_pre(levels - 1, jnp.where(position == 0, final_state_grad[0], 0.0))
    fwd_send, gates = lax.optimization_barrier((fwd_send, gates_of(0)))
    got = from_partner(fwd_send, "seq", 0)
    finished = run_groups(0, gates)
    state_now = fwd_post(0, state_now, got)
    for step in range(1, levels):
        fwd_send = fwd_pre(step, state_now)
        fwd_send, bwd_send, gates, finished = lax.optimization_barrier(
            (fwd_send, bwd_send, gates_of(step), finished)
        )
        got = from_partner(fwd_send, "seq", step)
        back = from_partner(bwd_send, "seq", levels - step)
        finished = run_groups(step, gates)
        state_now = fwd_post(step, state_now, got)
        state_grad = bwd_post(levels - step, bwd_own, back)
        bwd_own, bwd_send = bwd_pre(levels - step - 1, state_grad)
    state_grad = bwd_post(0, bwd_own, from_partner(bwd_send, "seq", 0))
    all_carries = jnp.stack(carries)

    unused, pull_carry = jax.vjp(mixer_carry, c_full, own_decay, own_weight[:, 1:, :], all_carries)
    c_carry, decay_carry, weight_carry, unused_grads = pull_carry(grad_full)

    own_log_grads = []
    peer_log_grads = []
    prefix_grads = []
    for level_index in range(levels):
        upper = uppers[level_index]
        joined_grad = joined_grads[level_index]
        with_peer = jnp.sum(joined_grad * saved_peer[level_index], axis=(1, 2))
        with_own = jnp.sum(joined_grad * saved_own[level_index], axis=(1, 2))
        carry_peer = jnp.sum(carry_grads[level_index] * saved_peer[level_index], axis=(1, 2))
        own_log_grads.append(jnp.where(upper, own_lifts[level_index] * with_peer, 0.0))
        peer_log_grads.append(jnp.where(upper, 0.0, peer_lifts[level_index] * with_own))
        prefix_grads.append(jnp.where(upper, prefix_lifts[level_index] * carry_peer, 0.0))
    unused, pull_logs = jax.vjp(lambda t: level_logs(t, position, levels), totals)
    (totals_grad,) = pull_logs((own_log_grads, peer_log_grads, prefix_grads))
    totals_grad = sum_over(totals_grad, "seq")
    log_grad = lax.dynamic_index_in_dim(totals_grad, position, 0, keepdims=False)

    input_buf = jnp.concatenate([r[0] for r in group_results], axis=1)
    weight_first = jnp.transpose(jnp.concatenate([r[1] for r in group_results], axis=0))
    running_grad = jnp.transpose(jnp.concatenate([r[2] for r in group_results], axis=0))
    decay_buf = jnp.cumsum(running_grad[::-1], axis=0)[::-1]
    score_grad = sum(r[3] for r in group_results)
    c_acc = jnp.dot(score_grad, b_full, precision=highest)
    b_acc = jnp.dot(score_grad.T, c_full, precision=highest)

    factor, pulled = state_spread(own_b, own_decay, state_grad)
    b_extra, decay_extra = state_backward(
        own_inputs, own_decay, state_grad, log_grad, factor, pulled
    )
    input_grad = input_buf + (factor[:, :, None] * pulled).reshape(length, -1)
    upstream = passed_along(input_grad.astype(jnp.bfloat16), "section", -1)
    b_grad = b_acc + b_extra
    c_grad = c_acc + c_carry
    decay_grad = decay_buf + decay_carry + decay_extra
    weight_grad = jnp.concatenate([weight_first[:, None, :], weight_carry], axis=1)
    return (upstream[None], b_grad[None], c_grad[None], decay_grad[None], weight_grad[None])


def solution(mesh):
    return jax.shard_map(
        body,
        mesh=mesh,
        in_specs=(
            P("section", "seq", None),
            P("section", "seq", None),
            P("section", "seq", None),
            P("section", "seq", None),
            P("section", "seq", None, None),
            P("section", "seq", None),
            P("section", None, None, None),
        ),
        out_specs=(
            P("section", "seq", None),
            P("section", "seq", None),
            P("section", "seq", None),
            P("section", "seq", None),
            P("section", "seq", None, None),
        ),
        check_vma=False,
    )
```

```python
import jax
import jax.numpy as jnp
from jax import lax
from jax.experimental import pallas as pl
from jax.experimental.pallas import tpu as pltpu
from jax.sharding import PartitionSpec as P

highest = lax.Precision.HIGHEST


def from_partner(value, axis, apart):
    return lax.ppermute(value, axis, [(i, i ^ 1 << apart) for i in range(lax.axis_size(axis))])


def passed_along(block, axis, distance):
    devices = range(lax.axis_size(axis))
    route = [((i - distance) % len(devices), i) for i in devices]
    return lax.ppermute(block, axis, route)


def block_state(inputs, b_proj, decay_log):
    length, head_count = decay_log.shape
    running = jnp.cumsum(decay_log, axis=0)
    block_total = running[-1]
    factor = jnp.exp(block_total[None, :] - running)
    weighted = inputs.astype(jnp.float32).reshape(length, head_count, -1) * factor[:, :, None]
    state = jnp.einsum("tn,thp->hnp", b_proj.astype(jnp.float32), weighted, precision=highest)
    return (state, block_total)


def mixer_local(inputs, b_proj, c_proj, decay_log, first_weight):
    length, head_count = decay_log.shape
    running = jnp.cumsum(decay_log, axis=0)
    values = inputs.reshape(length, head_count, -1)
    scores = jnp.dot(c_proj, b_proj.T, precision=highest)
    causal = jnp.arange(length)[:, None] >= jnp.arange(length)[None, :]
    spread = running[:, None, :] - running[None, :, :]
    decays = jnp.exp(jnp.where(causal[:, :, None], spread, -jnp.inf))
    mixing = decays * scores[:, :, None]
    local_part = jnp.einsum("tsh,shp->thp", mixing, values, precision=highest)
    result = first_weight[:, :, None] * local_part
    return result.reshape(length, -1)


def split_dot(a, b, dims):
    return lax.dot_general(
        a.astype(jnp.float32),
        b.astype(jnp.float32),
        (dims, ((), ())),
        precision=highest,
        preferred_element_type=jnp.float32,
    )


def local_kernel(heads, head_size, x_ref, g_ref, rc_ref, rr_ref, w_ref, sc_ref,
                 dx_ref, dw_ref, dr_ref, dsc_ref):
    scores = sc_ref[...]
    length = scores.shape[0]
    rows = lax.broadcasted_iota(jnp.int32, (length, length), 0)
    cols = lax.broadcasted_iota(jnp.int32, (length, length), 1)
    causal = rows >= cols
    score_grad = jnp.zeros((length, length), jnp.float32)
    ones_p = jnp.ones((1, head_size), jnp.float32)
    ones_t = jnp.ones((1, length), jnp.float32)
    for j, h in enumerate(heads):
        x = x_ref[:, h * head_size:(h + 1) * head_size]
        g = g_ref[:, h * head_size:(h + 1) * head_size].astype(jnp.float32)
        decays = jnp.where(causal, jnp.exp(rc_ref[:, h:h + 1] - rr_ref[h:h + 1, :]), 0.0)
        mixing = decays * scores
        local = split_dot(mixing, x, ((1,), (0,)))
        local_grad = w_ref[:, h:h + 1] * g
        dw_ref[j:j + 1, :] = split_dot(ones_p, g * local, ((1,), (1,)))
        dx_ref[:, j * head_size:(j + 1) * head_size] = split_dot(
            jnp.transpose(mixing), local_grad, ((1,), (0,))
        )
        mixing_grad = split_dot(local_grad, x, ((1,), (1,)))
        score_grad = score_grad + mixing_grad * decays
        spread_grad = mixing_grad * scores * decays
        dr_ref[j:j + 1, :] = split_dot(ones_t, spread_grad, ((1,), (1,))) - jnp.sum(
            spread_grad, axis=0, keepdims=True
        )
    dsc_ref[...] = score_grad


def local_grads(heads, inputs, grad, running_col, running_row, first_weight, scores):
    length = inputs.shape[0]
    head_size = inputs.shape[1] // running_col.shape[1]
    count = len(heads)
    vmem = pl.BlockSpec(memory_space=pltpu.VMEM)
    flops = count * 7 * 2 * length * length * head_size
    return pl.pallas_call(
        lambda *refs: local_kernel(heads, head_size, *refs),
        out_shape=(
            jax.ShapeDtypeStruct((length, count * head_size), jnp.float32),
            jax.ShapeDtypeStruct((count, length), jnp.float32),
            jax.ShapeDtypeStruct((count, length), jnp.float32),
            jax.ShapeDtypeStruct((length, length), jnp.float32),
        ),
        in_specs=[vmem] * 6,
        out_specs=(vmem,) * 4,
        cost_estimate=pl.CostEstimate(
            flops=flops,
            transcendentals=count * length * length,
            bytes_accessed=2 * length * inputs.shape[1] * 2 + count * length * head_size * 4,
        ),
    )(inputs, grad, running_col, running_row, first_weight, scores)


def mixer_carry(c_proj, decay_log, upper_weight, carries):
    length, head_count = decay_log.shape
    running = jnp.cumsum(decay_log, axis=0)
    lift = jnp.exp(running)
    result = jnp.zeros((length, head_count, carries.shape[-1]), jnp.float32)
    for level_index in range(carries.shape[0]):
        reach = jnp.einsum("tn,hnp->thp", c_proj, carries[level_index], precision=highest)
        result = result + (upper_weight[:, level_index, :] * lift)[:, :, None] * reach
    return result.reshape(length, -1)


def level_logs(totals, position, levels):
    count = totals.shape[0]
    index = jnp.arange(count)
    own, peer, prefix = [], [], []
    for level_index in range(levels):
        width = 1 << level_index
        base = position // width * width
        other = (position // width ^ 1) * width
        in_own = (index >= base) & (index < base + width)
        in_peer = (index >= other) & (index < other + width)
        in_prefix = (index >= base) & (index < position)
        own.append(jnp.sum(jnp.where(in_own[:, None], totals, 0.0), axis=0))
        peer.append(jnp.sum(jnp.where(in_peer[:, None], totals, 0.0), axis=0))
        prefix.append(jnp.sum(jnp.where(in_prefix[:, None], totals, 0.0), axis=0))
    return (own, peer, prefix)


def gather_blocks(value, axis):
    position = lax.axis_index(axis)
    blocks = value[None]
    for level_index in range(lax.axis_size(axis).bit_length() - 1):
        other = from_partner(blocks, axis, level_index)
        upper = position // 2**level_index % 2 == 1
        blocks = jnp.where(
            upper,
            jnp.concatenate([other, blocks], axis=0),
            jnp.concatenate([blocks, other], axis=0),
        )
    return blocks


def sum_over(value, axis):
    for level_index in range(lax.axis_size(axis).bit_length() - 1):
        value = value + from_partner(value, axis, level_index)
    return value


def halves_usable(state):
    return state.shape[0] % 2 == 0


def exchange_state(state, level_index):
    if level_index == 0 or not halves_usable(state):
        return from_partner(state, "seq", level_index)
    half = state.shape[0] // 2
    core = lax.axis_index("seq") % 2
    mine = lax.dynamic_slice_in_dim(state, core * half, half, 0)
    got = from_partner(mine, "seq", level_index)
    other = from_partner(got, "seq", 0)
    low = jnp.where(core == 0, got, other)
    high = jnp.where(core == 0, other, got)
    return jnp.concatenate([low, high], axis=0)


def exchange_grad(own_grad, peer_grad, level_index):
    if level_index == 0 or not halves_usable(peer_grad):
        return own_grad + from_partner(peer_grad, "seq", level_index)
    half = peer_grad.shape[0] // 2
    core = lax.axis_index("seq") % 2
    mine = lax.dynamic_slice_in_dim(peer_grad, core * half, half, 0)
    theirs = lax.dynamic_slice_in_dim(peer_grad, (1 - core) * half, half, 0)
    summed = mine + from_partner(theirs, "seq", 0)
    back = from_partner(summed, "seq", level_index)
    own_half = lax.dynamic_slice_in_dim(own_grad, core * half, half, 0)
    return lax.dynamic_update_slice_in_dim(own_grad, own_half + back, core * half, 0)


def state_spread(b_proj, decay_log, state_grad):
    running = jnp.cumsum(decay_log, axis=0)
    factor = jnp.exp(running[-1][None, :] - running)
    pulled = jnp.einsum("tn,hnp->thp", b_proj.astype(jnp.float32), state_grad, precision=highest)
    return (factor, pulled)


def state_backward(inputs, decay_log, state_grad, total_grad, factor, pulled):
    length, head_count = decay_log.shape
    values = inputs.astype(jnp.float32).reshape(length, head_count, -1)
    weighted = values * factor[:, :, None]
    b_grad = jnp.einsum("thp,hnp->tn", weighted, state_grad, precision=highest)
    log_grad = jnp.sum(values * pulled, axis=2) * factor
    running_grad = (-log_grad).at[-1].add(total_grad + jnp.sum(log_grad, axis=0))
    decay_grad = jnp.cumsum(running_grad[::-1], axis=0)[::-1]
    return (b_grad, decay_grad)


def body(inputs, b_proj, c_proj, decay_log, level_weight, out_grad, final_state_grad):
    own_inputs = inputs[0]
    own_b = b_proj[0]
    own_c = c_proj[0]
    own_decay = decay_log[0]
    own_weight = level_weight[0]
    own_grad = out_grad[0]
    length, head_count = own_decay.shape
    head_size = own_inputs.shape[1] // head_count
    group = 8
    group_width = group * head_size
    levels = lax.axis_size("seq").bit_length() - 1
    position = lax.axis_index("seq")
    b_full = own_b.astype(jnp.float32)
    c_full = own_c.astype(jnp.float32)
    grad_full = own_grad.astype(jnp.float32)

    totals = gather_blocks(jnp.sum(own_decay, axis=0), "seq")
    state_now, total_now = block_state(own_inputs, own_b, own_decay)
    own_logs, peer_logs, prefixes = level_logs(totals, position, levels)
    lifted = jnp.exp(jnp.stack(own_logs + peer_logs + prefixes))
    own_lifts = [lifted[k] for k in range(levels)]
    peer_lifts = [lifted[levels + k] for k in range(levels)]
    prefix_lifts = [lifted[2 * levels + k] for k in range(levels)]
    uppers = [position // 2**level_index % 2 == 1 for level_index in range(levels)]

    unused, pull_carry = jax.vjp(
        mixer_carry, c_full, own_decay, own_weight[:, 1:, :],
        jnp.zeros((levels,) + state_now.shape, jnp.float32),
    )
    carry_grads = pull_carry(grad_full)[3]

    running_col = jnp.cumsum(own_decay, axis=0)
    running_row = jnp.transpose(running_col)
    first_weight = own_weight[:, 0, :]
    scores = jnp.dot(c_full, b_full.T, precision=highest)

    def group_grads(g, gate):
        gate_col, gate_row = gate
        return local_grads(
            tuple(range(g * group, (g + 1) * group)), own_inputs, own_grad, gate_col, gate_row,
            first_weight, scores,
        )

    group_count = head_count // group
    step_groups = [[] for _ in range(levels)]
    for g in range(group_count):
        step_groups[min(g * levels // group_count, levels - 1)].append(g)
    group_results = [None] * group_count

    core = position % 2
    half = head_count // 2
    use_halves = head_count % 2 == 0

    def take_half(x, which):
        return lax.dynamic_slice_in_dim(x, which * half, half, 0)

    saved_own = [None] * levels
    saved_peer = [None] * levels
    carries = [None] * levels
    joined_grads = [None] * levels

    def fwd_pre(level_index, state):
        saved_own[level_index] = state
        if level_index == 0 or not use_halves:
            return state
        return take_half(state, core)

    def fwd_post(level_index, state, got):
        if level_index == 0 or not use_halves:
            peer_state = got
        else:
            other = from_partner(got, "seq", 0)
            low = jnp.where(core == 0, got, other)
            high = jnp.where(core == 0, other, got)
            peer_state = jnp.concatenate([low, high], axis=0)
        upper = uppers[level_index]
        saved_peer[level_index] = peer_state
        carries[level_index] = jnp.where(
            upper, prefix_lifts[level_index][:, None, None] * peer_state, 0.0
        )
        if level_index == levels - 1:
            return None
        return jnp.where(
            upper,
            own_lifts[level_index][:, None, None] * peer_state + state,
            peer_lifts[level_index][:, None, None] * state + peer_state,
        )

    def bwd_pre(level_index, joined_grad):
        upper = uppers[level_index]
        joined_grads[level_index] = joined_grad
        own_sg = jnp.where(
            upper, joined_grad, peer_lifts[level_index][:, None, None] * joined_grad
        )
        peer_sg = jnp.where(
            upper,
            own_lifts[level_index][:, None, None] * joined_grad
            + prefix_lifts[level_index][:, None, None] * carry_grads[level_index],
            joined_grad,
        )
        if level_index == 0 or not use_halves:
            return (own_sg, peer_sg)
        summed = take_half(peer_sg, core) + from_partner(take_half(peer_sg, 1 - core), "seq", 0)
        return (own_sg, summed)

    def bwd_post(level_index, own_sg, back):
        if level_index == 0 or not use_halves:
            return own_sg + back
        own_half = take_half(own_sg, core)
        return lax.dynamic_update_slice_in_dim(own_sg, own_half + back, core * half, 0)

    def run_groups(step, gates):
        for g, gate in zip(step_groups[step], gates):
            group_results[g] = group_grads(g, gate)
        return tuple(group_results[g] for g in step_groups[step])

    def gates_of(step):
        return [(running_col, running_row) for g in step_groups[step]]

    fwd_send = fwd_pre(0, state_now)
    bwd_own, bwd_send = bwd_pre(levels - 1, jnp.where(position == 0, final_state_grad[0], 0.0))
    fwd_send, gates = lax.optimization_barrier((fwd_send, gates_of(0)))
    got = from_partner(fwd_send, "seq", 0)
    finished = run_groups(0, gates)
    state_now = fwd_post(0, state_now, got)
    for step in range(1, levels):
        fwd_send = fwd_pre(step, state_now)
        fwd_send, bwd_send, gates, finished = lax.optimization_barrier(
            (fwd_send, bwd_send, gates_of(step), finished)
        )
        got = from_partner(fwd_send, "seq", step)
        back = from_partner(bwd_send, "seq", levels - step)
        finished = run_groups(step, gates)
        state_now = fwd_post(step, state_now, got)
        state_grad = bwd_post(levels - step, bwd_own, back)
        bwd_own, bwd_send = bwd_pre(levels - step - 1, state_grad)
    state_grad = bwd_post(0, bwd_own, from_partner(bwd_send, "seq", 0))
    all_carries = jnp.stack(carries)

    unused, pull_carry = jax.vjp(mixer_carry, c_full, own_decay, own_weight[:, 1:, :], all_carries)
    c_carry, decay_carry, weight_carry, unused_grads = pull_carry(grad_full)

    own_log_grads = []
    peer_log_grads = []
    prefix_grads = []
    for level_index in range(levels):
        upper = uppers[level_index]
        joined_grad = joined_grads[level_index]
        with_peer = jnp.sum(joined_grad * saved_peer[level_index], axis=(1, 2))
        with_own = jnp.sum(joined_grad * saved_own[level_index], axis=(1, 2))
        carry_peer = jnp.sum(carry_grads[level_index] * saved_peer[level_index], axis=(1, 2))
        own_log_grads.append(jnp.where(upper, own_lifts[level_index] * with_peer, 0.0))
        peer_log_grads.append(jnp.where(upper, 0.0, peer_lifts[level_index] * with_own))
        prefix_grads.append(jnp.where(upper, prefix_lifts[level_index] * carry_peer, 0.0))
    unused, pull_logs = jax.vjp(lambda t: level_logs(t, position, levels), totals)
    (totals_grad,) = pull_logs((own_log_grads, peer_log_grads, prefix_grads))

    input_buf = jnp.concatenate([r[0] for r in group_results], axis=1)
    factor, pulled = state_spread(own_b, own_decay, state_grad)
    input_grad = input_buf + (factor[:, :, None] * pulled).reshape(length, -1)
    upstream_send, totals_grad = lax.optimization_barrier(
        (input_grad.astype(jnp.bfloat16), totals_grad)
    )
    upstream = passed_along(upstream_send, "section", -1)
    totals_grad = sum_over(totals_grad, "seq")
    log_grad = lax.dynamic_index_in_dim(totals_grad, position, 0, keepdims=False)

    weight_first = jnp.transpose(jnp.concatenate([r[1] for r in group_results], axis=0))
    running_grad = jnp.transpose(jnp.concatenate([r[2] for r in group_results], axis=0))
    decay_buf = jnp.cumsum(running_grad[::-1], axis=0)[::-1]
    score_grad = sum(r[3] for r in group_results)
    c_acc = jnp.dot(score_grad, b_full, precision=highest)
    b_acc = jnp.dot(score_grad.T, c_full, precision=highest)

    b_extra, decay_extra = state_backward(
        own_inputs, own_decay, state_grad, log_grad, factor, pulled
    )
    b_grad = b_acc + b_extra
    c_grad = c_acc + c_carry
    decay_grad = decay_buf + decay_carry + decay_extra
    weight_grad = jnp.concatenate([weight_first[:, None, :], weight_carry], axis=1)
    return (upstream[None], b_grad[None], c_grad[None], decay_grad[None], weight_grad[None])


def solution(mesh):
    return jax.shard_map(
        body,
        mesh=mesh,
        in_specs=(
            P("section", "seq", None),
            P("section", "seq", None),
            P("section", "seq", None),
            P("section", "seq", None),
            P("section", "seq", None, None),
            P("section", "seq", None),
            P("section", None, None, None),
        ),
        out_specs=(
            P("section", "seq", None),
            P("section", "seq", None),
            P("section", "seq", None),
            P("section", "seq", None),
            P("section", "seq", None, None),
        ),
        check_vma=False,
    )
```

```python
import jax
import jax.numpy as jnp
from jax import lax
from jax.experimental import pallas as pl
from jax.experimental.pallas import tpu as pltpu
from jax.sharding import PartitionSpec as P

highest = lax.Precision.HIGHEST


def from_partner(value, axis, apart):
    return lax.ppermute(value, axis, [(i, i ^ 1 << apart) for i in range(lax.axis_size(axis))])


def passed_along(block, axis, distance):
    devices = range(lax.axis_size(axis))
    route = [((i - distance) % len(devices), i) for i in devices]
    return lax.ppermute(block, axis, route)


def block_state(inputs, b_proj, decay_log):
    length, head_count = decay_log.shape
    running = jnp.cumsum(decay_log, axis=0)
    block_total = running[-1]
    factor = jnp.exp(block_total[None, :] - running)
    weighted = inputs.astype(jnp.float32).reshape(length, head_count, -1) * factor[:, :, None]
    state = jnp.einsum("tn,thp->hnp", b_proj.astype(jnp.float32), weighted, precision=highest)
    return (state, block_total)


def mixer_local(inputs, b_proj, c_proj, decay_log, first_weight):
    length, head_count = decay_log.shape
    running = jnp.cumsum(decay_log, axis=0)
    values = inputs.reshape(length, head_count, -1)
    scores = jnp.dot(c_proj, b_proj.T, precision=highest)
    causal = jnp.arange(length)[:, None] >= jnp.arange(length)[None, :]
    spread = running[:, None, :] - running[None, :, :]
    decays = jnp.exp(jnp.where(causal[:, :, None], spread, -jnp.inf))
    mixing = decays * scores[:, :, None]
    local_part = jnp.einsum("tsh,shp->thp", mixing, values, precision=highest)
    result = first_weight[:, :, None] * local_part
    return result.reshape(length, -1)


def split_dot(a, b, dims):
    return lax.dot_general(
        a.astype(jnp.float32),
        b.astype(jnp.float32),
        (dims, ((), ())),
        precision=highest,
        preferred_element_type=jnp.float32,
    )


def local_kernel(heads, head_size, x_ref, g_ref, rc_ref, rr_ref, w_ref, sc_ref,
                 dx_ref, dw_ref, dr_ref, dsc_ref):
    scores = sc_ref[...]
    length = scores.shape[0]
    rows = lax.broadcasted_iota(jnp.int32, (length, length), 0)
    cols = lax.broadcasted_iota(jnp.int32, (length, length), 1)
    causal = rows >= cols
    score_grad = jnp.zeros((length, length), jnp.float32)
    ones_p = jnp.ones((1, head_size), jnp.float32)
    ones_t = jnp.ones((1, length), jnp.float32)
    for j, h in enumerate(heads):
        x = x_ref[:, h * head_size:(h + 1) * head_size]
        g = g_ref[:, h * head_size:(h + 1) * head_size].astype(jnp.float32)
        decays = jnp.where(causal, jnp.exp(rc_ref[:, h:h + 1] - rr_ref[h:h + 1, :]), 0.0)
        mixing = decays * scores
        local = split_dot(mixing, x, ((1,), (0,)))
        local_grad = w_ref[:, h:h + 1] * g
        dw_ref[j:j + 1, :] = split_dot(ones_p, g * local, ((1,), (1,)))
        dx_ref[:, j * head_size:(j + 1) * head_size] = split_dot(
            jnp.transpose(mixing), local_grad, ((1,), (0,))
        )
        mixing_grad = split_dot(local_grad, x, ((1,), (1,)))
        score_grad = score_grad + mixing_grad * decays
        spread_grad = mixing_grad * scores * decays
        dr_ref[j:j + 1, :] = split_dot(ones_t, spread_grad, ((1,), (1,))) - jnp.sum(
            spread_grad, axis=0, keepdims=True
        )
    dsc_ref[...] = score_grad


def local_grads(heads, inputs, grad, running_col, running_row, first_weight, scores):
    length = inputs.shape[0]
    head_size = inputs.shape[1] // running_col.shape[1]
    count = len(heads)
    vmem = pl.BlockSpec(memory_space=pltpu.VMEM)
    flops = count * 7 * 2 * length * length * head_size
    return pl.pallas_call(
        lambda *refs: local_kernel(heads, head_size, *refs),
        out_shape=(
            jax.ShapeDtypeStruct((length, count * head_size), jnp.float32),
            jax.ShapeDtypeStruct((count, length), jnp.float32),
            jax.ShapeDtypeStruct((count, length), jnp.float32),
            jax.ShapeDtypeStruct((length, length), jnp.float32),
        ),
        in_specs=[vmem] * 6,
        out_specs=(vmem,) * 4,
        cost_estimate=pl.CostEstimate(
            flops=flops,
            transcendentals=count * length * length,
            bytes_accessed=2 * length * inputs.shape[1] * 2 + count * length * head_size * 4,
        ),
    )(inputs, grad, running_col, running_row, first_weight, scores)


def mixer_carry(c_proj, decay_log, upper_weight, carries):
    length, head_count = decay_log.shape
    running = jnp.cumsum(decay_log, axis=0)
    lift = jnp.exp(running)
    result = jnp.zeros((length, head_count, carries.shape[-1]), jnp.float32)
    for level_index in range(carries.shape[0]):
        reach = jnp.einsum("tn,hnp->thp", c_proj, carries[level_index], precision=highest)
        result = result + (upper_weight[:, level_index, :] * lift)[:, :, None] * reach
    return result.reshape(length, -1)


def level_logs(totals, position, levels):
    count = totals.shape[0]
    index = jnp.arange(count)
    own, peer, prefix = [], [], []
    for level_index in range(levels):
        width = 1 << level_index
        base = position // width * width
        other = (position // width ^ 1) * width
        in_own = (index >= base) & (index < base + width)
        in_peer = (index >= other) & (index < other + width)
        in_prefix = (index >= base) & (index < position)
        own.append(jnp.sum(jnp.where(in_own[:, None], totals, 0.0), axis=0))
        peer.append(jnp.sum(jnp.where(in_peer[:, None], totals, 0.0), axis=0))
        prefix.append(jnp.sum(jnp.where(in_prefix[:, None], totals, 0.0), axis=0))
    return (own, peer, prefix)


def gather_blocks(value, axis):
    position = lax.axis_index(axis)
    blocks = value[None]
    for level_index in range(lax.axis_size(axis).bit_length() - 1):
        other = from_partner(blocks, axis, level_index)
        upper = position // 2**level_index % 2 == 1
        blocks = jnp.where(
            upper,
            jnp.concatenate([other, blocks], axis=0),
            jnp.concatenate([blocks, other], axis=0),
        )
    return blocks


def sum_over(value, axis):
    for level_index in range(lax.axis_size(axis).bit_length() - 1):
        value = value + from_partner(value, axis, level_index)
    return value


def halves_usable(state):
    return state.shape[0] % 2 == 0


def exchange_state(state, level_index):
    if level_index == 0 or not halves_usable(state):
        return from_partner(state, "seq", level_index)
    half = state.shape[0] // 2
    core = lax.axis_index("seq") % 2
    mine = lax.dynamic_slice_in_dim(state, core * half, half, 0)
    got = from_partner(mine, "seq", level_index)
    other = from_partner(got, "seq", 0)
    low = jnp.where(core == 0, got, other)
    high = jnp.where(core == 0, other, got)
    return jnp.concatenate([low, high], axis=0)


def exchange_grad(own_grad, peer_grad, level_index):
    if level_index == 0 or not halves_usable(peer_grad):
        return own_grad + from_partner(peer_grad, "seq", level_index)
    half = peer_grad.shape[0] // 2
    core = lax.axis_index("seq") % 2
    mine = lax.dynamic_slice_in_dim(peer_grad, core * half, half, 0)
    theirs = lax.dynamic_slice_in_dim(peer_grad, (1 - core) * half, half, 0)
    summed = mine + from_partner(theirs, "seq", 0)
    back = from_partner(summed, "seq", level_index)
    own_half = lax.dynamic_slice_in_dim(own_grad, core * half, half, 0)
    return lax.dynamic_update_slice_in_dim(own_grad, own_half + back, core * half, 0)


def state_spread(b_proj, decay_log, state_grad):
    running = jnp.cumsum(decay_log, axis=0)
    factor = jnp.exp(running[-1][None, :] - running)
    pulled = jnp.einsum("tn,hnp->thp", b_proj.astype(jnp.float32), state_grad, precision=highest)
    return (factor, pulled)


def state_backward(inputs, decay_log, state_grad, total_grad, factor, pulled):
    length, head_count = decay_log.shape
    values = inputs.astype(jnp.float32).reshape(length, head_count, -1)
    weighted = values * factor[:, :, None]
    b_grad = jnp.einsum("thp,hnp->tn", weighted, state_grad, precision=highest)
    log_grad = jnp.sum(values * pulled, axis=2) * factor
    running_grad = (-log_grad).at[-1].add(total_grad + jnp.sum(log_grad, axis=0))
    decay_grad = jnp.cumsum(running_grad[::-1], axis=0)[::-1]
    return (b_grad, decay_grad)


def body(inputs, b_proj, c_proj, decay_log, level_weight, out_grad, final_state_grad):
    own_inputs = inputs[0]
    own_b = b_proj[0]
    own_c = c_proj[0]
    own_decay = decay_log[0]
    own_weight = level_weight[0]
    own_grad = out_grad[0]
    length, head_count = own_decay.shape
    head_size = own_inputs.shape[1] // head_count
    group = 8
    group_width = group * head_size
    levels = lax.axis_size("seq").bit_length() - 1
    position = lax.axis_index("seq")
    b_full = own_b.astype(jnp.float32)
    c_full = own_c.astype(jnp.float32)
    grad_full = own_grad.astype(jnp.float32)

    totals = gather_blocks(jnp.sum(own_decay, axis=0), "seq")
    state_now, total_now = block_state(own_inputs, own_b, own_decay)
    own_logs, peer_logs, prefixes = level_logs(totals, position, levels)
    lifted = jnp.exp(jnp.stack(own_logs + peer_logs + prefixes))
    own_lifts = [lifted[k] for k in range(levels)]
    peer_lifts = [lifted[levels + k] for k in range(levels)]
    prefix_lifts = [lifted[2 * levels + k] for k in range(levels)]
    uppers = [position // 2**level_index % 2 == 1 for level_index in range(levels)]

    unused, pull_carry = jax.vjp(
        mixer_carry, c_full, own_decay, own_weight[:, 1:, :],
        jnp.zeros((levels,) + state_now.shape, jnp.float32),
    )
    carry_grads = pull_carry(grad_full)[3]

    running_col = jnp.cumsum(own_decay, axis=0)
    running_row = jnp.transpose(running_col)
    first_weight = own_weight[:, 0, :]
    scores = jnp.dot(c_full, b_full.T, precision=highest)

    def group_grads(g, gate):
        gate_col, gate_row = gate
        return local_grads(
            tuple(range(g * group, (g + 1) * group)), own_inputs, own_grad, gate_col, gate_row,
            first_weight, scores,
        )

    group_count = head_count // group
    step_groups = [[] for _ in range(levels)]
    for g in range(group_count):
        step_groups[min(g * levels // group_count, levels - 1)].append(g)
    group_results = [None] * group_count

    core = position % 2
    half = head_count // 2
    use_halves = head_count % 2 == 0

    def take_half(x, which):
        return lax.dynamic_slice_in_dim(x, which * half, half, 0)

    saved_own = [None] * levels
    saved_peer = [None] * levels
    carries = [None] * levels
    joined_grads = [None] * levels

    def fwd_pre(level_index, state):
        saved_own[level_index] = state
        if level_index == 0 or not use_halves:
            return state
        return take_half(state, core)

    def fwd_post(level_index, state, got):
        if level_index == 0 or not use_halves:
            peer_state = got
        else:
            other = from_partner(got, "seq", 0)
            low = jnp.where(core == 0, got, other)
            high = jnp.where(core == 0, other, got)
            peer_state = jnp.concatenate([low, high], axis=0)
        upper = uppers[level_index]
        saved_peer[level_index] = peer_state
        carries[level_index] = jnp.where(
            upper, prefix_lifts[level_index][:, None, None] * peer_state, 0.0
        )
        if level_index == levels - 1:
            return None
        return jnp.where(
            upper,
            own_lifts[level_index][:, None, None] * peer_state + state,
            peer_lifts[level_index][:, None, None] * state + peer_state,
        )

    def bwd_pre(level_index, joined_grad):
        upper = uppers[level_index]
        joined_grads[level_index] = joined_grad
        own_sg = jnp.where(
            upper, joined_grad, peer_lifts[level_index][:, None, None] * joined_grad
        )
        peer_sg = jnp.where(
            upper,
            own_lifts[level_index][:, None, None] * joined_grad
            + prefix_lifts[level_index][:, None, None] * carry_grads[level_index],
            joined_grad,
        )
        if level_index == 0 or not use_halves:
            return (own_sg, peer_sg)
        summed = take_half(peer_sg, core) + from_partner(take_half(peer_sg, 1 - core), "seq", 0)
        return (own_sg, summed)

    def bwd_post(level_index, own_sg, back):
        if level_index == 0 or not use_halves:
            return own_sg + back
        own_half = take_half(own_sg, core)
        return lax.dynamic_update_slice_in_dim(own_sg, own_half + back, core * half, 0)

    def run_groups(step, gates):
        for g, gate in zip(step_groups[step], gates):
            group_results[g] = group_grads(g, gate)
        return tuple(group_results[g] for g in step_groups[step])

    def gates_of(step):
        return [(running_col, running_row) for g in step_groups[step]]

    def carry_task(level_index):
        def run(carry):
            unused, pull = jax.vjp(
                lambda c, d, w, cr: mixer_carry(c, d, w[:, None, :], cr[None]),
                c_full, own_decay, own_weight[:, level_index + 1, :], carry,
            )
            return pull(grad_full)[:3]
        return run

    def log_task(level_index):
        def run(joined_grad, peer_state, own_state):
            return (
                jnp.sum(joined_grad * peer_state, axis=(1, 2)),
                jnp.sum(joined_grad * own_state, axis=(1, 2)),
                jnp.sum(carry_grads[level_index] * peer_state, axis=(1, 2)),
            )
        return run

    pending = [[] for _ in range(levels + 1)]
    task_results = {}
    log_registered = set()

    def register(step):
        for k in range(levels):
            if carries[k] is not None and ("carry", k) not in task_results and not any(
                key == ("carry", k) for key, _, _ in sum(pending, [])
            ):
                pending[min(step, levels)].append((("carry", k), carry_task(k), (carries[k],)))
            if (
                k not in log_registered
                and saved_peer[k] is not None
                and joined_grads[k] is not None
            ):
                log_registered.add(k)
                pending[min(step, levels)].append(
                    (("log", k), log_task(k), (joined_grads[k], saved_peer[k], saved_own[k]))
                )

    def run_tasks(step, task_args):
        outputs = []
        for (key, fn, unused), args in zip(pending[step], task_args):
            task_results[key] = fn(*args)
            outputs.append(task_results[key])
        return tuple(outputs)

    fwd_send = fwd_pre(0, state_now)
    bwd_own, bwd_send = bwd_pre(levels - 1, jnp.where(position == 0, final_state_grad[0], 0.0))
    fwd_send, gates = lax.optimization_barrier((fwd_send, gates_of(0)))
    got = from_partner(fwd_send, "seq", 0)
    finished = run_groups(0, gates)
    state_now = fwd_post(0, state_now, got)
    for step in range(1, levels):
        register(step)
        fwd_send = fwd_pre(step, state_now)
        fwd_send, bwd_send, gates, task_args, finished = lax.optimization_barrier(
            (fwd_send, bwd_send, gates_of(step), [t[2] for t in pending[step]], finished)
        )
        got = from_partner(fwd_send, "seq", step)
        back = from_partner(bwd_send, "seq", levels - step)
        finished = (run_groups(step, gates), run_tasks(step, task_args))
        state_now = fwd_post(step, state_now, got)
        state_grad = bwd_post(levels - step, bwd_own, back)
        bwd_own, bwd_send = bwd_pre(levels - step - 1, state_grad)
    state_grad = bwd_post(0, bwd_own, from_partner(bwd_send, "seq", 0))
    register(levels)
    run_tasks(levels, [t[2] for t in pending[levels]])
    carry_parts = [task_results[("carry", k)] for k in range(levels)]
    c_carry = sum(p[0] for p in carry_parts)
    decay_carry = sum(p[1] for p in carry_parts)
    weight_carry = jnp.stack([p[2] for p in carry_parts], axis=1)

    own_log_grads = []
    peer_log_grads = []
    prefix_grads = []
    for level_index in range(levels):
        upper = uppers[level_index]
        joined_grad = joined_grads[level_index]
        with_peer, with_own, carry_peer = task_results[("log", level_index)]
        own_log_grads.append(jnp.where(upper, own_lifts[level_index] * with_peer, 0.0))
        peer_log_grads.append(jnp.where(upper, 0.0, peer_lifts[level_index] * with_own))
        prefix_grads.append(jnp.where(upper, prefix_lifts[level_index] * carry_peer, 0.0))
    unused, pull_logs = jax.vjp(lambda t: level_logs(t, position, levels), totals)
    (totals_grad,) = pull_logs((own_log_grads, peer_log_grads, prefix_grads))

    input_buf = jnp.concatenate([r[0] for r in group_results], axis=1)
    factor, pulled = state_spread(own_b, own_decay, state_grad)
    input_grad = input_buf + (factor[:, :, None] * pulled).reshape(length, -1)
    upstream_send, totals_grad = lax.optimization_barrier(
        (input_grad.astype(jnp.bfloat16), totals_grad)
    )
    upstream = passed_along(upstream_send, "section", -1)
    totals_grad = sum_over(totals_grad, "seq")
    log_grad = lax.dynamic_index_in_dim(totals_grad, position, 0, keepdims=False)

    weight_first = jnp.transpose(jnp.concatenate([r[1] for r in group_results], axis=0))
    running_grad = jnp.transpose(jnp.concatenate([r[2] for r in group_results], axis=0))
    decay_buf = jnp.cumsum(running_grad[::-1], axis=0)[::-1]
    score_grad = sum(r[3] for r in group_results)
    c_acc = jnp.dot(score_grad, b_full, precision=highest)
    b_acc = jnp.dot(score_grad.T, c_full, precision=highest)

    b_extra, decay_extra = state_backward(
        own_inputs, own_decay, state_grad, log_grad, factor, pulled
    )
    b_grad = b_acc + b_extra
    c_grad = c_acc + c_carry
    decay_grad = decay_buf + decay_carry + decay_extra
    weight_grad = jnp.concatenate([weight_first[:, None, :], weight_carry], axis=1)
    return (upstream[None], b_grad[None], c_grad[None], decay_grad[None], weight_grad[None])


def solution(mesh):
    return jax.shard_map(
        body,
        mesh=mesh,
        in_specs=(
            P("section", "seq", None),
            P("section", "seq", None),
            P("section", "seq", None),
            P("section", "seq", None),
            P("section", "seq", None, None),
            P("section", "seq", None),
            P("section", None, None, None),
        ),
        out_specs=(
            P("section", "seq", None),
            P("section", "seq", None),
            P("section", "seq", None),
            P("section", "seq", None),
            P("section", "seq", None, None),
        ),
        check_vma=False,
    )
```

```python
import jax
import jax.numpy as jnp
from jax import lax
from jax.experimental import pallas as pl
from jax.experimental.pallas import tpu as pltpu
from jax.sharding import PartitionSpec as P


highest = lax.Precision.HIGHEST


def from_partner(value, axis, apart):
    return lax.ppermute(value, axis, [(i, i ^ 1 << apart) for i in range(lax.axis_size(axis))])


def passed_along(block, axis, distance):
    devices = range(lax.axis_size(axis))
    route = [((i - distance) % len(devices), i) for i in devices]
    return lax.ppermute(block, axis, route)


def block_state(inputs, b_proj, decay_log):
    length, head_count = decay_log.shape
    running = jnp.cumsum(decay_log, axis=0)
    block_total = running[-1]
    factor = jnp.exp(block_total[None, :] - running)
    weighted = inputs.astype(jnp.float32).reshape(length, head_count, -1) * factor[:, :, None]
    state = jnp.einsum("tn,thp->hnp", b_proj.astype(jnp.float32), weighted, precision=highest)
    return (state, block_total)


def split_dot(a, b, dims):
    return lax.dot_general(
        a.astype(jnp.float32),
        b.astype(jnp.float32),
        (dims, ((), ())),
        precision=highest,
        preferred_element_type=jnp.float32,
    )


def local_kernel(heads, head_size, x_ref, g_ref, rc_ref, rr_ref, w_ref, sc_ref,
                 dx_ref, dw_ref, dr_ref, dsc_ref):
    scores = sc_ref[...]
    length = scores.shape[0]
    rows = lax.broadcasted_iota(jnp.int32, (length, length), 0)
    cols = lax.broadcasted_iota(jnp.int32, (length, length), 1)
    causal = rows >= cols
    score_grad = jnp.zeros((length, length), jnp.float32)
    ones_p = jnp.ones((1, head_size), jnp.float32)
    ones_t = jnp.ones((1, length), jnp.float32)
    for j, h in enumerate(heads):
        x = x_ref[:, h * head_size:(h + 1) * head_size]
        g = g_ref[:, h * head_size:(h + 1) * head_size].astype(jnp.float32)
        decays = jnp.where(causal, jnp.exp(rc_ref[:, h:h + 1] - rr_ref[h:h + 1, :]), 0.0)
        mixing = decays * scores
        local = split_dot(mixing, x, ((1,), (0,)))
        local_grad = w_ref[:, h:h + 1] * g
        dw_ref[j:j + 1, :] = split_dot(ones_p, g * local, ((1,), (1,)))
        dx_ref[:, j * head_size:(j + 1) * head_size] = split_dot(
            jnp.transpose(mixing), local_grad, ((1,), (0,))
        )
        mixing_grad = split_dot(local_grad, x, ((1,), (1,)))
        score_grad = score_grad + mixing_grad * decays
        spread_grad = mixing_grad * scores * decays
        dr_ref[j:j + 1, :] = split_dot(ones_t, spread_grad, ((1,), (1,))) - jnp.sum(
            spread_grad, axis=0, keepdims=True
        )
    dsc_ref[...] = score_grad


def local_grads(heads, inputs, grad, running_col, running_row, first_weight, scores):
    length = inputs.shape[0]
    head_size = inputs.shape[1] // running_col.shape[1]
    count = len(heads)
    vmem = pl.BlockSpec(memory_space=pltpu.VMEM)
    flops = count * 7 * 2 * length * length * head_size
    return pl.pallas_call(
        lambda *refs: local_kernel(heads, head_size, *refs),
        out_shape=(
            jax.ShapeDtypeStruct((length, count * head_size), jnp.float32),
            jax.ShapeDtypeStruct((count, length), jnp.float32),
            jax.ShapeDtypeStruct((count, length), jnp.float32),
            jax.ShapeDtypeStruct((length, length), jnp.float32),
        ),
        in_specs=[vmem] * 6,
        out_specs=(vmem,) * 4,
        cost_estimate=pl.CostEstimate(
            flops=flops,
            transcendentals=count * length * length,
            bytes_accessed=2 * length * inputs.shape[1] * 2 + count * length * head_size * 4,
        ),
    )(inputs, grad, running_col, running_row, first_weight, scores)


def mixer_carry(c_proj, decay_log, upper_weight, carries):
    length, head_count = decay_log.shape
    running = jnp.cumsum(decay_log, axis=0)
    lift = jnp.exp(running)
    result = jnp.zeros((length, head_count, carries.shape[-1]), jnp.float32)
    for level_index in range(carries.shape[0]):
        reach = jnp.einsum("tn,hnp->thp", c_proj, carries[level_index], precision=highest)
        result = result + (upper_weight[:, level_index, :] * lift)[:, :, None] * reach
    return result.reshape(length, -1)


def level_logs(totals, position, levels):
    count = totals.shape[0]
    index = jnp.arange(count)
    own, peer, prefix = [], [], []
    for level_index in range(levels):
        width = 1 << level_index
        base = position // width * width
        other = (position // width ^ 1) * width
        in_own = (index >= base) & (index < base + width)
        in_peer = (index >= other) & (index < other + width)
        in_prefix = (index >= base) & (index < position)
        own.append(jnp.sum(jnp.where(in_own[:, None], totals, 0.0), axis=0))
        peer.append(jnp.sum(jnp.where(in_peer[:, None], totals, 0.0), axis=0))
        prefix.append(jnp.sum(jnp.where(in_prefix[:, None], totals, 0.0), axis=0))
    return (own, peer, prefix)


def gather_blocks(value, axis):
    position = lax.axis_index(axis)
    blocks = value[None]
    for level_index in range(lax.axis_size(axis).bit_length() - 1):
        other = from_partner(blocks, axis, level_index)
        upper = position // 2**level_index % 2 == 1
        blocks = jnp.where(
            upper,
            jnp.concatenate([other, blocks], axis=0),
            jnp.concatenate([blocks, other], axis=0),
        )
    return blocks


def sum_over(value, axis):
    for level_index in range(lax.axis_size(axis).bit_length() - 1):
        value = value + from_partner(value, axis, level_index)
    return value


def state_spread(b_proj, decay_log, state_grad):
    running = jnp.cumsum(decay_log, axis=0)
    factor = jnp.exp(running[-1][None, :] - running)
    pulled = jnp.einsum("tn,hnp->thp", b_proj.astype(jnp.float32), state_grad, precision=highest)
    return (factor, pulled)


def state_backward(inputs, decay_log, state_grad, total_grad, factor, pulled):
    length, head_count = decay_log.shape
    values = inputs.astype(jnp.float32).reshape(length, head_count, -1)
    weighted = values * factor[:, :, None]
    b_grad = jnp.einsum("thp,hnp->tn", weighted, state_grad, precision=highest)
    log_grad = jnp.sum(values * pulled, axis=2) * factor
    running_grad = (-log_grad).at[-1].add(total_grad + jnp.sum(log_grad, axis=0))
    decay_grad = jnp.cumsum(running_grad[::-1], axis=0)[::-1]
    return (b_grad, decay_grad)


def body(inputs, b_proj, c_proj, decay_log, level_weight, out_grad, final_state_grad):
    own_inputs = inputs[0]
    own_b = b_proj[0]
    own_c = c_proj[0]
    own_decay = decay_log[0]
    own_weight = level_weight[0]
    own_grad = out_grad[0]
    length, head_count = own_decay.shape
    group = 8
    levels = lax.axis_size("seq").bit_length() - 1
    position = lax.axis_index("seq")
    b_full = own_b.astype(jnp.float32)
    c_full = own_c.astype(jnp.float32)
    grad_full = own_grad.astype(jnp.float32)

    totals = gather_blocks(jnp.sum(own_decay, axis=0), "seq")
    state_now, _ = block_state(own_inputs, own_b, own_decay)
    own_logs, peer_logs, prefixes = level_logs(totals, position, levels)
    lifted = jnp.exp(jnp.stack(own_logs + peer_logs + prefixes))
    own_lifts = [lifted[k] for k in range(levels)]
    peer_lifts = [lifted[levels + k] for k in range(levels)]
    prefix_lifts = [lifted[2 * levels + k] for k in range(levels)]
    uppers = [position // 2**level_index % 2 == 1 for level_index in range(levels)]

    unused, pull_carry = jax.vjp(
        mixer_carry, c_full, own_decay, own_weight[:, 1:, :],
        jnp.zeros((levels,) + state_now.shape, jnp.float32),
    )
    carry_grads = pull_carry(grad_full)[3]

    running_col = jnp.cumsum(own_decay, axis=0)
    running_row = jnp.transpose(running_col)
    first_weight = own_weight[:, 0, :]
    scores = jnp.dot(c_full, b_full.T, precision=highest)

    def group_grads(g, gate):
        gate_col, gate_row = gate
        return local_grads(
            tuple(range(g * group, (g + 1) * group)), own_inputs, own_grad, gate_col, gate_row,
            first_weight, scores,
        )

    group_count = head_count // group
    step_groups = [[] for _ in range(levels)]
    for g in range(group_count):
        step_groups[min(g * levels // group_count, levels - 1)].append(g)
    group_results = [None] * group_count

    core = position % 2
    half = head_count // 2
    use_halves = head_count % 2 == 0

    def take_half(x, which):
        return lax.dynamic_slice_in_dim(x, which * half, half, 0)

    saved_own = [None] * levels
    saved_peer = [None] * levels
    carries = [None] * levels
    joined_grads = [None] * levels

    def fwd_pre(level_index, state):
        saved_own[level_index] = state
        if level_index == 0 or not use_halves:
            return state
        return take_half(state, core)

    def fwd_post(level_index, state, got):
        if level_index == 0 or not use_halves:
            peer_state = got
        else:
            other = from_partner(got, "seq", 0)
            low = jnp.where(core == 0, got, other)
            high = jnp.where(core == 0, other, got)
            peer_state = jnp.concatenate([low, high], axis=0)
        upper = uppers[level_index]
        saved_peer[level_index] = peer_state
        carries[level_index] = jnp.where(
            upper, prefix_lifts[level_index][:, None, None] * peer_state, 0.0
        )
        if level_index == levels - 1:
            return None
        return jnp.where(
            upper,
            own_lifts[level_index][:, None, None] * peer_state + state,
            peer_lifts[level_index][:, None, None] * state + peer_state,
        )

    def bwd_pre(level_index, joined_grad):
        upper = uppers[level_index]
        joined_grads[level_index] = joined_grad
        own_sg = jnp.where(
            upper, joined_grad, peer_lifts[level_index][:, None, None] * joined_grad
        )
        peer_sg = jnp.where(
            upper,
            own_lifts[level_index][:, None, None] * joined_grad
            + prefix_lifts[level_index][:, None, None] * carry_grads[level_index],
            joined_grad,
        )
        if level_index == 0 or not use_halves:
            return (own_sg, peer_sg)
        summed = take_half(peer_sg, core) + from_partner(take_half(peer_sg, 1 - core), "seq", 0)
        return (own_sg, summed)

    def bwd_post(level_index, own_sg, back):
        if level_index == 0 or not use_halves:
            return own_sg + back
        own_half = take_half(own_sg, core)
        return lax.dynamic_update_slice_in_dim(own_sg, own_half + back, core * half, 0)

    def run_groups(step, gates):
        for g, gate in zip(step_groups[step], gates):
            group_results[g] = group_grads(g, gate)
        return tuple(group_results[g] for g in step_groups[step])

    def gates_of(step):
        return [(running_col, running_row) for g in step_groups[step]]

    def carry_task(level_index):
        def run(carry):
            _, pull = jax.vjp(
                lambda c, d, w, cr: mixer_carry(c, d, w[:, None, :], cr[None]),
                c_full, own_decay, own_weight[:, level_index + 1, :], carry,
            )
            return pull(grad_full)[:3]

        return run

    def log_task(level_index):
        def run(joined_grad, peer_state, own_state):
            return (
                jnp.sum(joined_grad * peer_state, axis=(1, 2)),
                jnp.sum(joined_grad * own_state, axis=(1, 2)),
                jnp.sum(carry_grads[level_index] * peer_state, axis=(1, 2)),
            )

        return run

    pending = [[] for _ in range(levels + 1)]
    task_results = {}
    log_registered = set()

    def register(step):
        for k in range(levels):
            if carries[k] is not None and ("carry", k) not in task_results and not any(
                key == ("carry", k) for key, _, _ in sum(pending, [])
            ):
                pending[min(step, levels)].append((("carry", k), carry_task(k), (carries[k],)))
            if (
                k not in log_registered
                and saved_peer[k] is not None
                and joined_grads[k] is not None
            ):
                log_registered.add(k)
                pending[min(step, levels)].append(
                    (("log", k), log_task(k), (joined_grads[k], saved_peer[k], saved_own[k]))
                )

    def run_tasks(step, task_args):
        outputs = []
        for (key, fn, unused), args in zip(pending[step], task_args):
            task_results[key] = fn(*args)
            outputs.append(task_results[key])
        return tuple(outputs)

    fwd_send = fwd_pre(0, state_now)
    bwd_own, bwd_send = bwd_pre(levels - 1, jnp.where(position == 0, final_state_grad[0], 0.0))
    fwd_send, gates = lax.optimization_barrier((fwd_send, gates_of(0)))
    got = from_partner(fwd_send, "seq", 0)
    finished = run_groups(0, gates)
    state_now = fwd_post(0, state_now, got)
    for step in range(1, levels):
        register(step)
        fwd_send = fwd_pre(step, state_now)
        fwd_send, bwd_send, gates, task_args, finished = lax.optimization_barrier(
            (fwd_send, bwd_send, gates_of(step), [t[2] for t in pending[step]], finished)
        )
        got = from_partner(fwd_send, "seq", step)
        back = from_partner(bwd_send, "seq", levels - step)
        kernel_results = run_groups(step, gates)
        finished = (kernel_results, run_tasks(step, task_args))
        state_now = fwd_post(step, state_now, got)
        state_grad = bwd_post(levels - step, bwd_own, back)
        bwd_own, bwd_send = bwd_pre(levels - step - 1, state_grad)
    state_grad = bwd_post(0, bwd_own, from_partner(bwd_send, "seq", 0))
    register(levels)
    run_tasks(levels, [t[2] for t in pending[levels]])
    carry_parts = [task_results[("carry", k)] for k in range(levels)]
    c_carry = sum(p[0] for p in carry_parts)
    decay_carry = sum(p[1] for p in carry_parts)
    weight_carry = jnp.stack([p[2] for p in carry_parts], axis=1)

    own_log_grads = []
    peer_log_grads = []
    prefix_grads = []
    for level_index in range(levels):
        upper = uppers[level_index]
        with_peer, with_own, carry_peer = task_results[("log", level_index)]
        own_log_grads.append(jnp.where(upper, own_lifts[level_index] * with_peer, 0.0))
        peer_log_grads.append(jnp.where(upper, 0.0, peer_lifts[level_index] * with_own))
        prefix_grads.append(jnp.where(upper, prefix_lifts[level_index] * carry_peer, 0.0))
    unused, pull_logs = jax.vjp(lambda t: level_logs(t, position, levels), totals)
    (totals_grad,) = pull_logs((own_log_grads, peer_log_grads, prefix_grads))

    input_buf = jnp.concatenate([r[0] for r in group_results], axis=1)
    factor, pulled = state_spread(own_b, own_decay, state_grad)
    input_grad = input_buf + (factor[:, :, None] * pulled).reshape(length, -1)
    upstream_send, totals_grad = lax.optimization_barrier(
        (input_grad.astype(jnp.bfloat16), totals_grad)
    )
    upstream = passed_along(upstream_send, "section", -1)
    totals_grad = sum_over(totals_grad, "seq")
    log_grad = lax.dynamic_index_in_dim(totals_grad, position, 0, keepdims=False)

    weight_first = jnp.transpose(jnp.concatenate([r[1] for r in group_results], axis=0))
    running_grad = jnp.transpose(jnp.concatenate([r[2] for r in group_results], axis=0))
    decay_buf = jnp.cumsum(running_grad[::-1], axis=0)[::-1]
    score_grad = sum(r[3] for r in group_results)
    c_acc = jnp.dot(score_grad, b_full, precision=highest)
    b_acc = jnp.dot(score_grad.T, c_full, precision=highest)

    b_extra, decay_extra = state_backward(
        own_inputs, own_decay, state_grad, log_grad, factor, pulled
    )
    b_grad = b_acc + b_extra
    c_grad = c_acc + c_carry
    decay_grad = decay_buf + decay_carry + decay_extra
    weight_grad = jnp.concatenate([weight_first[:, None, :], weight_carry], axis=1)
    return (upstream[None], b_grad[None], c_grad[None], decay_grad[None], weight_grad[None])


def solution(mesh):
    return jax.shard_map(
        body,
        mesh=mesh,
        in_specs=(
            P("section", "seq", None),
            P("section", "seq", None),
            P("section", "seq", None),
            P("section", "seq", None),
            P("section", "seq", None, None),
            P("section", "seq", None),
            P("section", None, None, None),
        ),
        out_specs=(
            P("section", "seq", None),
            P("section", "seq", None),
            P("section", "seq", None),
            P("section", "seq", None),
            P("section", "seq", None, None),
        ),
        check_vma=False,
    )
```

```python
import jax
import jax.numpy as jnp
from jax import lax
from jax.experimental import pallas as pl
from jax.experimental.pallas import tpu as pltpu
from jax.sharding import PartitionSpec as P


highest = lax.Precision.HIGHEST


def from_partner(value, axis, apart):
    return lax.ppermute(value, axis, [(i, i ^ 1 << apart) for i in range(lax.axis_size(axis))])


def passed_along(block, axis, distance):
    devices = range(lax.axis_size(axis))
    route = [((i - distance) % len(devices), i) for i in devices]
    return lax.ppermute(block, axis, route)


def block_state(inputs, b_proj, decay_log):
    length, head_count = decay_log.shape
    running = jnp.cumsum(decay_log, axis=0)
    block_total = running[-1]
    factor = jnp.exp(block_total[None, :] - running)
    weighted = inputs.astype(jnp.float32).reshape(length, head_count, -1) * factor[:, :, None]
    state = jnp.einsum("tn,thp->hnp", b_proj.astype(jnp.float32), weighted, precision=highest)
    return (state, block_total)


def split_dot(a, b, dims):
    return lax.dot_general(
        a.astype(jnp.float32),
        b.astype(jnp.float32),
        (dims, ((), ())),
        precision=highest,
        preferred_element_type=jnp.float32,
    )


def local_kernel(heads, head_size, x_ref, g_ref, rc_ref, rr_ref, w_ref, sc_ref,
                 dx_ref, dw_ref, dr_ref, dsc_ref):
    scores = sc_ref[...]
    length = scores.shape[0]
    rows = lax.broadcasted_iota(jnp.int32, (length, length), 0)
    cols = lax.broadcasted_iota(jnp.int32, (length, length), 1)
    causal = rows >= cols
    score_grad = jnp.zeros((length, length), jnp.float32)
    ones_p = jnp.ones((1, head_size), jnp.float32)
    ones_t = jnp.ones((1, length), jnp.float32)
    for j, h in enumerate(heads):
        x = x_ref[:, h * head_size:(h + 1) * head_size]
        g = g_ref[:, h * head_size:(h + 1) * head_size].astype(jnp.float32)
        decays = jnp.where(causal, jnp.exp(rc_ref[:, h:h + 1] - rr_ref[h:h + 1, :]), 0.0)
        mixing = decays * scores
        local = split_dot(mixing, x, ((1,), (0,)))
        local_grad = w_ref[:, h:h + 1] * g
        dw_ref[j:j + 1, :] = split_dot(ones_p, g * local, ((1,), (1,)))
        dx_ref[:, j * head_size:(j + 1) * head_size] = split_dot(
            jnp.transpose(mixing), local_grad, ((1,), (0,))
        )
        mixing_grad = split_dot(local_grad, x, ((1,), (1,)))
        score_grad = score_grad + mixing_grad * decays
        spread_grad = mixing_grad * scores * decays
        dr_ref[j:j + 1, :] = split_dot(ones_t, spread_grad, ((1,), (1,))) - jnp.sum(
            spread_grad, axis=0, keepdims=True
        )
    dsc_ref[...] = score_grad


def local_grads(heads, inputs, grad, running_col, running_row, first_weight, scores):
    length = inputs.shape[0]
    head_size = inputs.shape[1] // running_col.shape[1]
    count = len(heads)
    vmem = pl.BlockSpec(memory_space=pltpu.VMEM)
    flops = count * 7 * 2 * length * length * head_size
    return pl.pallas_call(
        lambda *refs: local_kernel(heads, head_size, *refs),
        out_shape=(
            jax.ShapeDtypeStruct((length, count * head_size), jnp.float32),
            jax.ShapeDtypeStruct((count, length), jnp.float32),
            jax.ShapeDtypeStruct((count, length), jnp.float32),
            jax.ShapeDtypeStruct((length, length), jnp.float32),
        ),
        in_specs=[vmem] * 6,
        out_specs=(vmem,) * 4,
        cost_estimate=pl.CostEstimate(
            flops=flops,
            transcendentals=count * length * length,
            bytes_accessed=2 * length * inputs.shape[1] * 2 + count * length * head_size * 4,
        ),
    )(inputs, grad, running_col, running_row, first_weight, scores)


def mixer_carry(c_proj, decay_log, upper_weight, carries):
    length, head_count = decay_log.shape
    running = jnp.cumsum(decay_log, axis=0)
    lift = jnp.exp(running)
    result = jnp.zeros((length, head_count, carries.shape[-1]), jnp.float32)
    for level_index in range(carries.shape[0]):
        reach = jnp.einsum("tn,hnp->thp", c_proj, carries[level_index], precision=highest)
        result = result + (upper_weight[:, level_index, :] * lift)[:, :, None] * reach
    return result.reshape(length, -1)


def level_logs(totals, position, levels):
    count = totals.shape[0]
    index = jnp.arange(count)
    own, peer, prefix = [], [], []
    for level_index in range(levels):
        width = 1 << level_index
        base = position // width * width
        other = (position // width ^ 1) * width
        in_own = (index >= base) & (index < base + width)
        in_peer = (index >= other) & (index < other + width)
        in_prefix = (index >= base) & (index < position)
        own.append(jnp.sum(jnp.where(in_own[:, None], totals, 0.0), axis=0))
        peer.append(jnp.sum(jnp.where(in_peer[:, None], totals, 0.0), axis=0))
        prefix.append(jnp.sum(jnp.where(in_prefix[:, None], totals, 0.0), axis=0))
    return (own, peer, prefix)


def gather_blocks(value, axis):
    position = lax.axis_index(axis)
    blocks = value[None]
    for level_index in range(lax.axis_size(axis).bit_length() - 1):
        other = from_partner(blocks, axis, level_index)
        upper = position // 2**level_index % 2 == 1
        blocks = jnp.where(
            upper,
            jnp.concatenate([other, blocks], axis=0),
            jnp.concatenate([blocks, other], axis=0),
        )
    return blocks


def sum_over(value, axis):
    for level_index in range(lax.axis_size(axis).bit_length() - 1):
        value = value + from_partner(value, axis, level_index)
    return value


def state_spread(b_proj, decay_log, state_grad):
    running = jnp.cumsum(decay_log, axis=0)
    factor = jnp.exp(running[-1][None, :] - running)
    pulled = jnp.einsum("tn,hnp->thp", b_proj.astype(jnp.float32), state_grad, precision=highest)
    return (factor, pulled)


def state_backward(inputs, decay_log, state_grad, total_grad, factor, pulled):
    length, head_count = decay_log.shape
    values = inputs.astype(jnp.float32).reshape(length, head_count, -1)
    weighted = values * factor[:, :, None]
    b_grad = jnp.einsum("thp,hnp->tn", weighted, state_grad, precision=highest)
    log_grad = jnp.sum(values * pulled, axis=2) * factor
    running_grad = (-log_grad).at[-1].add(total_grad + jnp.sum(log_grad, axis=0))
    decay_grad = jnp.cumsum(running_grad[::-1], axis=0)[::-1]
    return (b_grad, decay_grad)


def body(inputs, b_proj, c_proj, decay_log, level_weight, out_grad, final_state_grad):
    own_inputs = inputs[0]
    own_b = b_proj[0]
    own_c = c_proj[0]
    own_decay = decay_log[0]
    own_weight = level_weight[0]
    own_grad = out_grad[0]
    length, head_count = own_decay.shape
    group = 8
    levels = lax.axis_size("seq").bit_length() - 1
    position = lax.axis_index("seq")
    b_full = own_b.astype(jnp.float32)
    c_full = own_c.astype(jnp.float32)
    grad_full = own_grad.astype(jnp.float32)

    totals = gather_blocks(jnp.sum(own_decay, axis=0), "seq")
    state_now, _ = block_state(own_inputs, own_b, own_decay)
    own_logs, peer_logs, prefixes = level_logs(totals, position, levels)
    lifted = jnp.exp(jnp.stack(own_logs + peer_logs + prefixes))
    own_lifts = [lifted[k] for k in range(levels)]
    peer_lifts = [lifted[levels + k] for k in range(levels)]
    prefix_lifts = [lifted[2 * levels + k] for k in range(levels)]
    uppers = [position // 2**level_index % 2 == 1 for level_index in range(levels)]

    unused, pull_carry = jax.vjp(
        mixer_carry, c_full, own_decay, own_weight[:, 1:, :],
        jnp.zeros((levels,) + state_now.shape, jnp.float32),
    )
    carry_grads = pull_carry(grad_full)[3]

    running_col = jnp.cumsum(own_decay, axis=0)
    running_row = jnp.transpose(running_col)
    first_weight = own_weight[:, 0, :]
    scores = jnp.dot(c_full, b_full.T, precision=highest)

    def group_grads(g, gate):
        gate_col, gate_row = gate
        return local_grads(
            tuple(range(g * group, (g + 1) * group)), own_inputs, own_grad, gate_col, gate_row,
            first_weight, scores,
        )

    group_count = head_count // group
    step_groups = [[] for _ in range(levels)]
    for g in range(group_count):
        step_groups[min(g * levels // group_count, levels - 1)].append(g)
    group_results = [None] * group_count

    core = position % 2
    half = head_count // 2
    use_halves = head_count % 2 == 0

    def take_half(x, which):
        return lax.dynamic_slice_in_dim(x, which * half, half, 0)

    saved_own = [None] * levels
    saved_peer = [None] * levels
    carries = [None] * levels
    joined_grads = [None] * levels

    def fwd_pre(level_index, state):
        saved_own[level_index] = state
        if level_index == 0 or not use_halves:
            return state
        return take_half(state, core)

    def fwd_post(level_index, state, got):
        if level_index == 0 or not use_halves:
            peer_state = got
        else:
            other = from_partner(got, "seq", 0)
            low = jnp.where(core == 0, got, other)
            high = jnp.where(core == 0, other, got)
            peer_state = jnp.concatenate([low, high], axis=0)
        upper = uppers[level_index]
        saved_peer[level_index] = peer_state
        carries[level_index] = jnp.where(
            upper, prefix_lifts[level_index][:, None, None] * peer_state, 0.0
        )
        if level_index == levels - 1:
            return None
        return jnp.where(
            upper,
            own_lifts[level_index][:, None, None] * peer_state + state,
            peer_lifts[level_index][:, None, None] * state + peer_state,
        )

    def bwd_pre(level_index, joined_grad):
        upper = uppers[level_index]
        joined_grads[level_index] = joined_grad
        own_sg = jnp.where(
            upper, joined_grad, peer_lifts[level_index][:, None, None] * joined_grad
        )
        peer_sg = jnp.where(
            upper,
            own_lifts[level_index][:, None, None] * joined_grad
            + prefix_lifts[level_index][:, None, None] * carry_grads[level_index],
            joined_grad,
        )
        if level_index == 0 or not use_halves:
            return (own_sg, peer_sg)
        summed = take_half(peer_sg, core) + from_partner(take_half(peer_sg, 1 - core), "seq", 0)
        return (own_sg, summed)

    def bwd_post(level_index, own_sg, back):
        if level_index == 0 or not use_halves:
            return own_sg + back
        own_half = take_half(own_sg, core)
        return lax.dynamic_update_slice_in_dim(own_sg, own_half + back, core * half, 0)

    def run_groups(step, gates):
        for g, gate in zip(step_groups[step], gates):
            group_results[g] = group_grads(g, gate)
        return tuple(group_results[g] for g in step_groups[step])

    def gates_of(step):
        return [(running_col, running_row) for g in step_groups[step]]

    def carry_task(level_index):
        def run(carry):
            _, pull = jax.vjp(
                lambda c, d, w, cr: mixer_carry(c, d, w[:, None, :], cr[None]),
                c_full, own_decay, own_weight[:, level_index + 1, :], carry,
            )
            return pull(grad_full)[:3]

        return run

    def log_task(level_index):
        def run(joined_grad, peer_state, own_state):
            return (
                jnp.sum(joined_grad * peer_state, axis=(1, 2)),
                jnp.sum(joined_grad * own_state, axis=(1, 2)),
                jnp.sum(carry_grads[level_index] * peer_state, axis=(1, 2)),
            )

        return run

    pending = [[] for _ in range(levels + 1)]
    task_results = {}
    log_registered = set()

    def register(step):
        for k in range(levels):
            if carries[k] is not None and ("carry", k) not in task_results and not any(
                key == ("carry", k) for key, _, _ in sum(pending, [])
            ):
                pending[min(step, levels)].append((("carry", k), carry_task(k), (carries[k],)))
            if (
                k not in log_registered
                and saved_peer[k] is not None
                and joined_grads[k] is not None
            ):
                log_registered.add(k)
                pending[min(step, levels)].append(
                    (("log", k), log_task(k), (joined_grads[k], saved_peer[k], saved_own[k]))
                )

    def run_tasks(step, task_args):
        outputs = []
        for (key, fn, unused), args in zip(pending[step], task_args):
            task_results[key] = fn(*args)
            outputs.append(task_results[key])
        return tuple(outputs)

    fwd_send = fwd_pre(0, state_now)
    bwd_own, bwd_send = bwd_pre(levels - 1, jnp.where(position == 0, final_state_grad[0], 0.0))
    fwd_send, gates = lax.optimization_barrier((fwd_send, gates_of(0)))
    got = from_partner(fwd_send, "seq", 0)
    finished = run_groups(0, gates)
    state_now = fwd_post(0, state_now, got)
    for step in range(1, levels):
        register(step)
        fwd_send = fwd_pre(step, state_now)
        fwd_send, bwd_send, gates, task_args, finished = lax.optimization_barrier(
            (fwd_send, bwd_send, gates_of(step), [t[2] for t in pending[step]], finished)
        )
        got = from_partner(fwd_send, "seq", step)
        back = from_partner(bwd_send, "seq", levels - step)
        kernel_results = run_groups(step, gates)
        finished = (kernel_results, run_tasks(step, task_args))
        state_now = fwd_post(step, state_now, got)
        state_grad = bwd_post(levels - step, bwd_own, back)
        bwd_own, bwd_send = bwd_pre(levels - step - 1, state_grad)
    state_grad = bwd_post(0, bwd_own, from_partner(bwd_send, "seq", 0))
    input_buf = jnp.concatenate([r[0] for r in group_results], axis=1)
    factor, pulled = state_spread(own_b, own_decay, state_grad)
    input_grad = input_buf + (factor[:, :, None] * pulled).reshape(length, -1)
    upstream = passed_along(input_grad.astype(jnp.bfloat16), "section", -1)
    register(levels)
    run_tasks(levels, [t[2] for t in pending[levels]])
    carry_parts = [task_results[("carry", k)] for k in range(levels)]
    c_carry = sum(p[0] for p in carry_parts)
    decay_carry = sum(p[1] for p in carry_parts)
    weight_carry = jnp.stack([p[2] for p in carry_parts], axis=1)
    own_log_grads = []
    peer_log_grads = []
    prefix_grads = []
    for level_index in range(levels):
        upper = uppers[level_index]
        with_peer, with_own, carry_peer = task_results[("log", level_index)]
        own_log_grads.append(jnp.where(upper, own_lifts[level_index] * with_peer, 0.0))
        peer_log_grads.append(
            jnp.where(upper, 0.0, peer_lifts[level_index] * with_own)
        )
        prefix_grads.append(
            jnp.where(upper, prefix_lifts[level_index] * carry_peer, 0.0)
        )
    unused, pull_logs = jax.vjp(lambda t: level_logs(t, position, levels), totals)
    (totals_grad,) = pull_logs((own_log_grads, peer_log_grads, prefix_grads))
    totals_grad = sum_over(totals_grad, "seq")
    log_grad = lax.dynamic_index_in_dim(totals_grad, position, 0, keepdims=False)

    weight_first = jnp.transpose(jnp.concatenate([r[1] for r in group_results], axis=0))
    running_grad = jnp.transpose(jnp.concatenate([r[2] for r in group_results], axis=0))
    decay_buf = jnp.cumsum(running_grad[::-1], axis=0)[::-1]
    score_grad = sum(r[3] for r in group_results)
    c_acc = jnp.dot(score_grad, b_full, precision=highest)
    b_acc = jnp.dot(score_grad.T, c_full, precision=highest)

    b_extra, decay_extra = state_backward(
        own_inputs, own_decay, state_grad, log_grad, factor, pulled
    )
    b_grad = b_acc + b_extra
    c_grad = c_acc + c_carry
    decay_grad = decay_buf + decay_carry + decay_extra
    weight_grad = jnp.concatenate([weight_first[:, None, :], weight_carry], axis=1)
    return (upstream[None], b_grad[None], c_grad[None], decay_grad[None], weight_grad[None])


def solution(mesh):
    return jax.shard_map(
        body,
        mesh=mesh,
        in_specs=(
            P("section", "seq", None),
            P("section", "seq", None),
            P("section", "seq", None),
            P("section", "seq", None),
            P("section", "seq", None, None),
            P("section", "seq", None),
            P("section", None, None, None),
        ),
        out_specs=(
            P("section", "seq", None),
            P("section", "seq", None),
            P("section", "seq", None),
            P("section", "seq", None),
            P("section", "seq", None, None),
        ),
        check_vma=False,
    )
```

```python
import jax
import jax.numpy as jnp
from jax import lax
from jax.experimental import pallas as pl
from jax.experimental.pallas import tpu as pltpu
from jax.sharding import PartitionSpec as P


highest = lax.Precision.HIGHEST


def from_partner(value, axis, apart):
    return lax.ppermute(value, axis, [(i, i ^ 1 << apart) for i in range(lax.axis_size(axis))])


def passed_along(block, axis, distance):
    devices = range(lax.axis_size(axis))
    route = [((i - distance) % len(devices), i) for i in devices]
    return lax.ppermute(block, axis, route)


def block_state(inputs, b_proj, decay_log):
    length, head_count = decay_log.shape
    running = jnp.cumsum(decay_log, axis=0)
    block_total = running[-1]
    factor = jnp.exp(block_total[None, :] - running)
    weighted = inputs.astype(jnp.float32).reshape(length, head_count, -1) * factor[:, :, None]
    state = jnp.einsum("tn,thp->hnp", b_proj.astype(jnp.float32), weighted, precision=highest)
    return (state, block_total)


def split_dot(a, b, dims):
    return lax.dot_general(
        a.astype(jnp.float32),
        b.astype(jnp.float32),
        (dims, ((), ())),
        precision=highest,
        preferred_element_type=jnp.float32,
    )


def local_kernel(heads, head_size, x_ref, g_ref, rc_ref, rr_ref, w_ref, sc_ref,
                 dx_ref, dw_ref, dr_ref, dsc_ref):
    scores = sc_ref[...]
    length = scores.shape[0]
    rows = lax.broadcasted_iota(jnp.int32, (length, length), 0)
    cols = lax.broadcasted_iota(jnp.int32, (length, length), 1)
    causal = rows >= cols
    score_grad = jnp.zeros((length, length), jnp.float32)
    ones_p = jnp.ones((1, head_size), jnp.float32)
    ones_t = jnp.ones((1, length), jnp.float32)
    for j, h in enumerate(heads):
        x = x_ref[:, h * head_size:(h + 1) * head_size]
        g = g_ref[:, h * head_size:(h + 1) * head_size].astype(jnp.float32)
        decays = jnp.where(causal, jnp.exp(rc_ref[:, h:h + 1] - rr_ref[h:h + 1, :]), 0.0)
        mixing = decays * scores
        local = split_dot(mixing, x, ((1,), (0,)))
        local_grad = w_ref[:, h:h + 1] * g
        dw_ref[j:j + 1, :] = split_dot(ones_p, g * local, ((1,), (1,)))
        dx_ref[:, j * head_size:(j + 1) * head_size] = split_dot(
            jnp.transpose(mixing), local_grad, ((1,), (0,))
        )
        mixing_grad = split_dot(local_grad, x, ((1,), (1,)))
        score_grad = score_grad + mixing_grad * decays
        spread_grad = mixing_grad * scores * decays
        dr_ref[j:j + 1, :] = split_dot(ones_t, spread_grad, ((1,), (1,))) - jnp.sum(
            spread_grad, axis=0, keepdims=True
        )
    dsc_ref[...] = score_grad


def local_grads(heads, inputs, grad, running_col, running_row, first_weight, scores):
    length = inputs.shape[0]
    head_size = inputs.shape[1] // running_col.shape[1]
    count = len(heads)
    vmem = pl.BlockSpec(memory_space=pltpu.VMEM)
    flops = count * 7 * 2 * length * length * head_size
    return pl.pallas_call(
        lambda *refs: local_kernel(heads, head_size, *refs),
        out_shape=(
            jax.ShapeDtypeStruct((length, count * head_size), jnp.float32),
            jax.ShapeDtypeStruct((count, length), jnp.float32),
            jax.ShapeDtypeStruct((count, length), jnp.float32),
            jax.ShapeDtypeStruct((length, length), jnp.float32),
        ),
        in_specs=[vmem] * 6,
        out_specs=(vmem,) * 4,
        cost_estimate=pl.CostEstimate(
            flops=flops,
            transcendentals=count * length * length,
            bytes_accessed=2 * length * inputs.shape[1] * 2 + count * length * head_size * 4,
        ),
    )(inputs, grad, running_col, running_row, first_weight, scores)


def mixer_carry(c_proj, decay_log, upper_weight, carries):
    length, head_count = decay_log.shape
    running = jnp.cumsum(decay_log, axis=0)
    lift = jnp.exp(running)
    result = jnp.zeros((length, head_count, carries.shape[-1]), jnp.float32)
    for level_index in range(carries.shape[0]):
        reach = jnp.einsum("tn,hnp->thp", c_proj, carries[level_index], precision=highest)
        result = result + (upper_weight[:, level_index, :] * lift)[:, :, None] * reach
    return result.reshape(length, -1)


def level_logs(totals, position, levels):
    count = totals.shape[0]
    index = jnp.arange(count)
    own, peer, prefix = [], [], []
    for level_index in range(levels):
        width = 1 << level_index
        base = position // width * width
        other = (position // width ^ 1) * width
        in_own = (index >= base) & (index < base + width)
        in_peer = (index >= other) & (index < other + width)
        in_prefix = (index >= base) & (index < position)
        own.append(jnp.sum(jnp.where(in_own[:, None], totals, 0.0), axis=0))
        peer.append(jnp.sum(jnp.where(in_peer[:, None], totals, 0.0), axis=0))
        prefix.append(jnp.sum(jnp.where(in_prefix[:, None], totals, 0.0), axis=0))
    return (own, peer, prefix)


def rounds_of(axis):
    bits = lax.axis_size(axis).bit_length() - 1
    rounds = []
    low = 0
    while low < bits:
        width = 2 if low + 1 < bits else 1
        rounds.append((low, width))
        low += width
    return rounds


def gather_blocks(value, axis):
    position = lax.axis_index(axis)
    count = lax.axis_size(axis)
    blocks = value[None]
    for low, width in rounds_of(axis):
        span = 1 << width
        parts = [blocks] + [
            lax.ppermute(blocks, axis, [(i, i ^ (m << low)) for i in range(count)])
            for m in range(1, span)
        ]
        stacked = jnp.stack(parts)
        mine = position // 2**low % span
        blocks = jnp.concatenate(
            [lax.dynamic_index_in_dim(stacked, mine ^ j, 0, keepdims=False) for j in range(span)],
            axis=0,
        )
    return blocks


def sum_over(value, axis):
    count = lax.axis_size(axis)
    for low, width in rounds_of(axis):
        parts = [
            lax.ppermute(value, axis, [(i, i ^ (m << low)) for i in range(count)])
            for m in range(1, 1 << width)
        ]
        for part in parts:
            value = value + part
    return value


def state_spread(b_proj, decay_log, state_grad):
    running = jnp.cumsum(decay_log, axis=0)
    factor = jnp.exp(running[-1][None, :] - running)
    pulled = jnp.einsum("tn,hnp->thp", b_proj.astype(jnp.float32), state_grad, precision=highest)
    return (factor, pulled)


def state_backward(inputs, decay_log, state_grad, total_grad, factor, pulled):
    length, head_count = decay_log.shape
    values = inputs.astype(jnp.float32).reshape(length, head_count, -1)
    weighted = values * factor[:, :, None]
    b_grad = jnp.einsum("thp,hnp->tn", weighted, state_grad, precision=highest)
    log_grad = jnp.sum(values * pulled, axis=2) * factor
    running_grad = (-log_grad).at[-1].add(total_grad + jnp.sum(log_grad, axis=0))
    decay_grad = jnp.cumsum(running_grad[::-1], axis=0)[::-1]
    return (b_grad, decay_grad)


def body(inputs, b_proj, c_proj, decay_log, level_weight, out_grad, final_state_grad):
    own_inputs = inputs[0]
    own_b = b_proj[0]
    own_c = c_proj[0]
    own_decay = decay_log[0]
    own_weight = level_weight[0]
    own_grad = out_grad[0]
    length, head_count = own_decay.shape
    group = 8
    levels = lax.axis_size("seq").bit_length() - 1
    position = lax.axis_index("seq")
    b_full = own_b.astype(jnp.float32)
    c_full = own_c.astype(jnp.float32)
    grad_full = own_grad.astype(jnp.float32)

    totals = gather_blocks(jnp.sum(own_decay, axis=0), "seq")
    state_now, _ = block_state(own_inputs, own_b, own_decay)
    own_logs, peer_logs, prefixes = level_logs(totals, position, levels)
    lifted = jnp.exp(jnp.stack(own_logs + peer_logs + prefixes))
    own_lifts = [lifted[k] for k in range(levels)]
    peer_lifts = [lifted[levels + k] for k in range(levels)]
    prefix_lifts = [lifted[2 * levels + k] for k in range(levels)]
    uppers = [position // 2**level_index % 2 == 1 for level_index in range(levels)]

    unused, pull_carry = jax.vjp(
        mixer_carry, c_full, own_decay, own_weight[:, 1:, :],
        jnp.zeros((levels,) + state_now.shape, jnp.float32),
    )
    carry_grads = pull_carry(grad_full)[3]

    running_col = jnp.cumsum(own_decay, axis=0)
    running_row = jnp.transpose(running_col)
    first_weight = own_weight[:, 0, :]
    scores = jnp.dot(c_full, b_full.T, precision=highest)

    def group_grads(g, gate):
        gate_col, gate_row = gate
        return local_grads(
            tuple(range(g * group, (g + 1) * group)), own_inputs, own_grad, gate_col, gate_row,
            first_weight, scores,
        )

    group_count = head_count // group
    step_groups = [[] for _ in range(levels)]
    for g in range(group_count):
        step_groups[min(g * levels // group_count, levels - 1)].append(g)
    group_results = [None] * group_count

    core = position % 2
    half = head_count // 2
    use_halves = head_count % 2 == 0

    def take_half(x, which):
        return lax.dynamic_slice_in_dim(x, which * half, half, 0)

    saved_own = [None] * levels
    saved_peer = [None] * levels
    carries = [None] * levels
    joined_grads = [None] * levels

    def fwd_pre(level_index, state):
        saved_own[level_index] = state
        if level_index == 0 or not use_halves:
            return state
        return take_half(state, core)

    def fwd_post(level_index, state, got):
        if level_index == 0 or not use_halves:
            peer_state = got
        else:
            other = from_partner(got, "seq", 0)
            low = jnp.where(core == 0, got, other)
            high = jnp.where(core == 0, other, got)
            peer_state = jnp.concatenate([low, high], axis=0)
        upper = uppers[level_index]
        saved_peer[level_index] = peer_state
        carries[level_index] = jnp.where(
            upper, prefix_lifts[level_index][:, None, None] * peer_state, 0.0
        )
        if level_index == levels - 1:
            return None
        return jnp.where(
            upper,
            own_lifts[level_index][:, None, None] * peer_state + state,
            peer_lifts[level_index][:, None, None] * state + peer_state,
        )

    def bwd_pre(level_index, joined_grad):
        upper = uppers[level_index]
        joined_grads[level_index] = joined_grad
        own_sg = jnp.where(
            upper, joined_grad, peer_lifts[level_index][:, None, None] * joined_grad
        )
        peer_sg = jnp.where(
            upper,
            own_lifts[level_index][:, None, None] * joined_grad
            + prefix_lifts[level_index][:, None, None] * carry_grads[level_index],
            joined_grad,
        )
        if level_index == 0 or not use_halves:
            return (own_sg, peer_sg)
        summed = take_half(peer_sg, core) + from_partner(take_half(peer_sg, 1 - core), "seq", 0)
        return (own_sg, summed)

    def bwd_post(level_index, own_sg, back):
        if level_index == 0 or not use_halves:
            return own_sg + back
        own_half = take_half(own_sg, core)
        return lax.dynamic_update_slice_in_dim(own_sg, own_half + back, core * half, 0)

    def run_groups(step, gates):
        for g, gate in zip(step_groups[step], gates):
            group_results[g] = group_grads(g, gate)
        return tuple(group_results[g] for g in step_groups[step])

    def gates_of(step):
        return [(running_col, running_row) for g in step_groups[step]]

    def carry_task(level_index):
        def run(carry):
            _, pull = jax.vjp(
                lambda c, d, w, cr: mixer_carry(c, d, w[:, None, :], cr[None]),
                c_full, own_decay, own_weight[:, level_index + 1, :], carry,
            )
            return pull(grad_full)[:3]

        return run

    def log_task(level_index):
        def run(joined_grad, peer_state, own_state):
            return (
                jnp.sum(joined_grad * peer_state, axis=(1, 2)),
                jnp.sum(joined_grad * own_state, axis=(1, 2)),
                jnp.sum(carry_grads[level_index] * peer_state, axis=(1, 2)),
            )

        return run

    pending = [[] for _ in range(levels + 1)]
    task_results = {}
    log_registered = set()

    def register(step):
        for k in range(levels):
            if carries[k] is not None and ("carry", k) not in task_results and not any(
                key == ("carry", k) for key, _, _ in sum(pending, [])
            ):
                pending[min(step, levels)].append((("carry", k), carry_task(k), (carries[k],)))
            if (
                k not in log_registered
                and saved_peer[k] is not None
                and joined_grads[k] is not None
            ):
                log_registered.add(k)
                pending[min(step, levels)].append(
                    (("log", k), log_task(k), (joined_grads[k], saved_peer[k], saved_own[k]))
                )

    def run_tasks(step, task_args):
        outputs = []
        for (key, fn, unused), args in zip(pending[step], task_args):
            task_results[key] = fn(*args)
            outputs.append(task_results[key])
        return tuple(outputs)

    fwd_send = fwd_pre(0, state_now)
    bwd_own, bwd_send = bwd_pre(levels - 1, jnp.where(position == 0, final_state_grad[0], 0.0))
    fwd_send, gates = lax.optimization_barrier((fwd_send, gates_of(0)))
    got = from_partner(fwd_send, "seq", 0)
    finished = run_groups(0, gates)
    state_now = fwd_post(0, state_now, got)
    for step in range(1, levels):
        register(step)
        fwd_send = fwd_pre(step, state_now)
        fwd_send, bwd_send, gates, task_args, finished = lax.optimization_barrier(
            (fwd_send, bwd_send, gates_of(step), [t[2] for t in pending[step]], finished)
        )
        got = from_partner(fwd_send, "seq", step)
        back = from_partner(bwd_send, "seq", levels - step)
        kernel_results = run_groups(step, gates)
        finished = (kernel_results, run_tasks(step, task_args))
        state_now = fwd_post(step, state_now, got)
        state_grad = bwd_post(levels - step, bwd_own, back)
        bwd_own, bwd_send = bwd_pre(levels - step - 1, state_grad)
    state_grad = bwd_post(0, bwd_own, from_partner(bwd_send, "seq", 0))
    register(levels)
    run_tasks(levels, [t[2] for t in pending[levels]])
    carry_parts = [task_results[("carry", k)] for k in range(levels)]
    c_carry = sum(p[0] for p in carry_parts)
    decay_carry = sum(p[1] for p in carry_parts)
    weight_carry = jnp.stack([p[2] for p in carry_parts], axis=1)

    own_log_grads = []
    peer_log_grads = []
    prefix_grads = []
    for level_index in range(levels):
        upper = uppers[level_index]
        with_peer, with_own, carry_peer = task_results[("log", level_index)]
        own_log_grads.append(jnp.where(upper, own_lifts[level_index] * with_peer, 0.0))
        peer_log_grads.append(jnp.where(upper, 0.0, peer_lifts[level_index] * with_own))
        prefix_grads.append(jnp.where(upper, prefix_lifts[level_index] * carry_peer, 0.0))
    unused, pull_logs = jax.vjp(lambda t: level_logs(t, position, levels), totals)
    (totals_grad,) = pull_logs((own_log_grads, peer_log_grads, prefix_grads))

    input_buf = jnp.concatenate([r[0] for r in group_results], axis=1)
    factor, pulled = state_spread(own_b, own_decay, state_grad)
    input_grad = input_buf + (factor[:, :, None] * pulled).reshape(length, -1)
    upstream_send, totals_grad = lax.optimization_barrier(
        (input_grad.astype(jnp.bfloat16), totals_grad)
    )
    upstream = passed_along(upstream_send, "section", -1)
    totals_grad = sum_over(totals_grad, "seq")
    log_grad = lax.dynamic_index_in_dim(totals_grad, position, 0, keepdims=False)

    weight_first = jnp.transpose(jnp.concatenate([r[1] for r in group_results], axis=0))
    running_grad = jnp.transpose(jnp.concatenate([r[2] for r in group_results], axis=0))
    decay_buf = jnp.cumsum(running_grad[::-1], axis=0)[::-1]
    score_grad = sum(r[3] for r in group_results)
    c_acc = jnp.dot(score_grad, b_full, precision=highest)
    b_acc = jnp.dot(score_grad.T, c_full, precision=highest)

    b_extra, decay_extra = state_backward(
        own_inputs, own_decay, state_grad, log_grad, factor, pulled
    )
    b_grad = b_acc + b_extra
    c_grad = c_acc + c_carry
    decay_grad = decay_buf + decay_carry + decay_extra
    weight_grad = jnp.concatenate([weight_first[:, None, :], weight_carry], axis=1)
    return (upstream[None], b_grad[None], c_grad[None], decay_grad[None], weight_grad[None])


def solution(mesh):
    return jax.shard_map(
        body,
        mesh=mesh,
        in_specs=(
            P("section", "seq", None),
            P("section", "seq", None),
            P("section", "seq", None),
            P("section", "seq", None),
            P("section", "seq", None, None),
            P("section", "seq", None),
            P("section", None, None, None),
        ),
        out_specs=(
            P("section", "seq", None),
            P("section", "seq", None),
            P("section", "seq", None),
            P("section", "seq", None),
            P("section", "seq", None, None),
        ),
        check_vma=False,
    )
```

```python
import jax
import jax.numpy as jnp
from jax import lax
from jax.experimental import pallas as pl
from jax.experimental.pallas import tpu as pltpu
from jax.sharding import PartitionSpec as P


highest = lax.Precision.HIGHEST


def from_partner(value, axis, apart):
    return lax.ppermute(value, axis, [(i, i ^ 1 << apart) for i in range(lax.axis_size(axis))])


def passed_along(block, axis, distance):
    devices = range(lax.axis_size(axis))
    route = [((i - distance) % len(devices), i) for i in devices]
    return lax.ppermute(block, axis, route)


def block_state(inputs, b_proj, decay_log):
    length, head_count = decay_log.shape
    running = jnp.cumsum(decay_log, axis=0)
    block_total = running[-1]
    factor = jnp.exp(block_total[None, :] - running)
    weighted = inputs.astype(jnp.float32).reshape(length, head_count, -1) * factor[:, :, None]
    state = jnp.einsum("tn,thp->hnp", b_proj.astype(jnp.float32), weighted, precision=highest)
    return (state, block_total)


def split_dot(a, b, dims):
    return lax.dot_general(
        a.astype(jnp.float32),
        b.astype(jnp.float32),
        (dims, ((), ())),
        precision=highest,
        preferred_element_type=jnp.float32,
    )


def local_kernel(heads, head_size, x_ref, g_ref, rc_ref, rr_ref, w_ref, sc_ref,
                 dx_ref, dw_ref, dr_ref, dsc_ref):
    scores = sc_ref[...]
    length = scores.shape[0]
    rows = lax.broadcasted_iota(jnp.int32, (length, length), 0)
    cols = lax.broadcasted_iota(jnp.int32, (length, length), 1)
    causal = rows >= cols
    score_grad = jnp.zeros((length, length), jnp.float32)
    ones_p = jnp.ones((1, head_size), jnp.float32)
    ones_t = jnp.ones((1, length), jnp.float32)
    for j, h in enumerate(heads):
        x = x_ref[:, h * head_size:(h + 1) * head_size]
        g = g_ref[:, h * head_size:(h + 1) * head_size].astype(jnp.float32)
        decays = jnp.where(causal, jnp.exp(rc_ref[:, h:h + 1] - rr_ref[h:h + 1, :]), 0.0)
        mixing = decays * scores
        local = split_dot(mixing, x, ((1,), (0,)))
        local_grad = w_ref[:, h:h + 1] * g
        dw_ref[j:j + 1, :] = split_dot(ones_p, g * local, ((1,), (1,)))
        dx_ref[:, j * head_size:(j + 1) * head_size] = split_dot(
            jnp.transpose(mixing), local_grad, ((1,), (0,))
        )
        mixing_grad = split_dot(local_grad, x, ((1,), (1,)))
        score_grad = score_grad + mixing_grad * decays
        spread_grad = mixing_grad * scores * decays
        dr_ref[j:j + 1, :] = split_dot(ones_t, spread_grad, ((1,), (1,))) - jnp.sum(
            spread_grad, axis=0, keepdims=True
        )
    dsc_ref[...] = score_grad


def local_grads(heads, inputs, grad, running_col, running_row, first_weight, scores):
    length = inputs.shape[0]
    head_size = inputs.shape[1] // running_col.shape[1]
    count = len(heads)
    vmem = pl.BlockSpec(memory_space=pltpu.VMEM)
    flops = count * 7 * 2 * length * length * head_size
    return pl.pallas_call(
        lambda *refs: local_kernel(heads, head_size, *refs),
        out_shape=(
            jax.ShapeDtypeStruct((length, count * head_size), jnp.float32),
            jax.ShapeDtypeStruct((count, length), jnp.float32),
            jax.ShapeDtypeStruct((count, length), jnp.float32),
            jax.ShapeDtypeStruct((length, length), jnp.float32),
        ),
        in_specs=[vmem] * 6,
        out_specs=(vmem,) * 4,
        cost_estimate=pl.CostEstimate(
            flops=flops,
            transcendentals=count * length * length,
            bytes_accessed=2 * length * inputs.shape[1] * 2 + count * length * head_size * 4,
        ),
    )(inputs, grad, running_col, running_row, first_weight, scores)


def mixer_carry(c_proj, decay_log, upper_weight, carries):
    length, head_count = decay_log.shape
    running = jnp.cumsum(decay_log, axis=0)
    lift = jnp.exp(running)
    result = jnp.zeros((length, head_count, carries.shape[-1]), jnp.float32)
    for level_index in range(carries.shape[0]):
        reach = jnp.einsum("tn,hnp->thp", c_proj, carries[level_index], precision=highest)
        result = result + (upper_weight[:, level_index, :] * lift)[:, :, None] * reach
    return result.reshape(length, -1)


def level_logs(totals, position, levels):
    count = totals.shape[0]
    index = jnp.arange(count)
    own, peer, prefix = [], [], []
    for level_index in range(levels):
        width = 1 << level_index
        base = position // width * width
        other = (position // width ^ 1) * width
        in_own = (index >= base) & (index < base + width)
        in_peer = (index >= other) & (index < other + width)
        in_prefix = (index >= base) & (index < position)
        own.append(jnp.sum(jnp.where(in_own[:, None], totals, 0.0), axis=0))
        peer.append(jnp.sum(jnp.where(in_peer[:, None], totals, 0.0), axis=0))
        prefix.append(jnp.sum(jnp.where(in_prefix[:, None], totals, 0.0), axis=0))
    return (own, peer, prefix)


def gather_blocks(value, axis):
    position = lax.axis_index(axis)
    blocks = value[None]
    for level_index in range(lax.axis_size(axis).bit_length() - 1):
        other = from_partner(blocks, axis, level_index)
        upper = position // 2**level_index % 2 == 1
        blocks = jnp.where(
            upper,
            jnp.concatenate([other, blocks], axis=0),
            jnp.concatenate([blocks, other], axis=0),
        )
    return blocks


def sum_over(value, axis):
    for level_index in range(lax.axis_size(axis).bit_length() - 1):
        value = value + from_partner(value, axis, level_index)
    return value


def state_spread(b_proj, decay_log, state_grad):
    running = jnp.cumsum(decay_log, axis=0)
    factor = jnp.exp(running[-1][None, :] - running)
    pulled = jnp.einsum("tn,hnp->thp", b_proj.astype(jnp.float32), state_grad, precision=highest)
    return (factor, pulled)


def state_backward(inputs, decay_log, state_grad, total_grad, factor, pulled):
    length, head_count = decay_log.shape
    values = inputs.astype(jnp.float32).reshape(length, head_count, -1)
    weighted = values * factor[:, :, None]
    b_grad = jnp.einsum("thp,hnp->tn", weighted, state_grad, precision=highest)
    log_grad = jnp.sum(values * pulled, axis=2) * factor
    running_grad = (-log_grad).at[-1].add(total_grad + jnp.sum(log_grad, axis=0))
    decay_grad = jnp.cumsum(running_grad[::-1], axis=0)[::-1]
    return (b_grad, decay_grad)


def body(inputs, b_proj, c_proj, decay_log, level_weight, out_grad, final_state_grad):
    own_inputs = inputs[0]
    own_b = b_proj[0]
    own_c = c_proj[0]
    own_decay = decay_log[0]
    own_weight = level_weight[0]
    own_grad = out_grad[0]
    length, head_count = own_decay.shape
    levels = lax.axis_size("seq").bit_length() - 1
    position = lax.axis_index("seq")
    b_full = own_b.astype(jnp.float32)
    c_full = own_c.astype(jnp.float32)
    grad_full = own_grad.astype(jnp.float32)

    totals = gather_blocks(jnp.sum(own_decay, axis=0), "seq")
    state_now, _ = block_state(own_inputs, own_b, own_decay)
    own_logs, peer_logs, prefixes = level_logs(totals, position, levels)
    lifted = jnp.exp(jnp.stack(own_logs + peer_logs + prefixes))
    own_lifts = [lifted[k] for k in range(levels)]
    peer_lifts = [lifted[levels + k] for k in range(levels)]
    prefix_lifts = [lifted[2 * levels + k] for k in range(levels)]
    uppers = [position // 2**level_index % 2 == 1 for level_index in range(levels)]

    unused, pull_carry = jax.vjp(
        mixer_carry, c_full, own_decay, own_weight[:, 1:, :],
        jnp.zeros((levels,) + state_now.shape, jnp.float32),
    )
    carry_grads = pull_carry(grad_full)[3]

    running_col = jnp.cumsum(own_decay, axis=0)
    running_row = jnp.transpose(running_col)
    first_weight = own_weight[:, 0, :]
    scores = jnp.dot(c_full, b_full.T, precision=highest)

    def group_grads(g, gate):
        gate_col, gate_row = gate
        return local_grads(
            group_heads[g], own_inputs, own_grad, gate_col, gate_row, first_weight, scores
        )

    link_steps = list(range(1, levels)) or [0]
    group_count = len(link_steps)
    group_heads = [
        tuple(range(g * head_count // group_count, (g + 1) * head_count // group_count))
        for g in range(group_count)
    ]
    step_groups = [[] for _ in range(levels)]
    for g, step in enumerate(link_steps):
        step_groups[step].append(g)
    group_results = [None] * group_count

    core = position % 2
    half = head_count // 2
    use_halves = head_count % 2 == 0

    def take_half(x, which):
        return lax.dynamic_slice_in_dim(x, which * half, half, 0)

    saved_own = [None] * levels
    saved_peer = [None] * levels
    carries = [None] * levels
    joined_grads = [None] * levels

    def fwd_pre(level_index, state):
        saved_own[level_index] = state
        if level_index == 0 or not use_halves:
            return state
        return take_half(state, core)

    def fwd_post(level_index, state, got):
        if level_index == 0 or not use_halves:
            peer_state = got
        else:
            other = from_partner(got, "seq", 0)
            low = jnp.where(core == 0, got, other)
            high = jnp.where(core == 0, other, got)
            peer_state = jnp.concatenate([low, high], axis=0)
        upper = uppers[level_index]
        saved_peer[level_index] = peer_state
        carries[level_index] = jnp.where(
            upper, prefix_lifts[level_index][:, None, None] * peer_state, 0.0
        )
        if level_index == levels - 1:
            return None
        return jnp.where(
            upper,
            own_lifts[level_index][:, None, None] * peer_state + state,
            peer_lifts[level_index][:, None, None] * state + peer_state,
        )

    def bwd_pre(level_index, joined_grad):
        upper = uppers[level_index]
        joined_grads[level_index] = joined_grad
        own_sg = jnp.where(
            upper, joined_grad, peer_lifts[level_index][:, None, None] * joined_grad
        )
        peer_sg = jnp.where(
            upper,
            own_lifts[level_index][:, None, None] * joined_grad
            + prefix_lifts[level_index][:, None, None] * carry_grads[level_index],
            joined_grad,
        )
        if level_index == 0 or not use_halves:
            return (own_sg, peer_sg)
        summed = take_half(peer_sg, core) + from_partner(take_half(peer_sg, 1 - core), "seq", 0)
        return (own_sg, summed)

    def bwd_post(level_index, own_sg, back):
        if level_index == 0 or not use_halves:
            return own_sg + back
        own_half = take_half(own_sg, core)
        return lax.dynamic_update_slice_in_dim(own_sg, own_half + back, core * half, 0)

    def run_groups(step, gates):
        for g, gate in zip(step_groups[step], gates):
            group_results[g] = group_grads(g, gate)
        return tuple(group_results[g] for g in step_groups[step])

    def gates_of(step):
        return [(running_col, running_row) for g in step_groups[step]]

    def carry_task(level_index):
        def run(carry):
            _, pull = jax.vjp(
                lambda c, d, w, cr: mixer_carry(c, d, w[:, None, :], cr[None]),
                c_full, own_decay, own_weight[:, level_index + 1, :], carry,
            )
            return pull(grad_full)[:3]

        return run

    def log_task(level_index):
        def run(joined_grad, peer_state, own_state):
            return (
                jnp.sum(joined_grad * peer_state, axis=(1, 2)),
                jnp.sum(joined_grad * own_state, axis=(1, 2)),
                jnp.sum(carry_grads[level_index] * peer_state, axis=(1, 2)),
            )

        return run

    pending = [[] for _ in range(levels + 1)]
    task_results = {}
    log_registered = set()

    def register(step):
        for k in range(levels):
            if carries[k] is not None and ("carry", k) not in task_results and not any(
                key == ("carry", k) for key, _, _ in sum(pending, [])
            ):
                pending[min(step, levels)].append((("carry", k), carry_task(k), (carries[k],)))
            if (
                k not in log_registered
                and saved_peer[k] is not None
                and joined_grads[k] is not None
            ):
                log_registered.add(k)
                pending[min(step, levels)].append(
                    (("log", k), log_task(k), (joined_grads[k], saved_peer[k], saved_own[k]))
                )

    def run_tasks(step, task_args):
        outputs = []
        for (key, fn, unused), args in zip(pending[step], task_args):
            task_results[key] = fn(*args)
            outputs.append(task_results[key])
        return tuple(outputs)

    fwd_send = fwd_pre(0, state_now)
    bwd_own, bwd_send = bwd_pre(levels - 1, jnp.where(position == 0, final_state_grad[0], 0.0))
    fwd_send, gates = lax.optimization_barrier((fwd_send, gates_of(0)))
    got = from_partner(fwd_send, "seq", 0)
    finished = run_groups(0, gates)
    state_now = fwd_post(0, state_now, got)
    for step in range(1, levels):
        register(step)
        fwd_send = fwd_pre(step, state_now)
        fwd_send, bwd_send, gates, task_args, finished = lax.optimization_barrier(
            (fwd_send, bwd_send, gates_of(step), [t[2] for t in pending[step]], finished)
        )
        got = from_partner(fwd_send, "seq", step)
        back = from_partner(bwd_send, "seq", levels - step)
        kernel_results = run_groups(step, gates)
        finished = (kernel_results, run_tasks(step, task_args))
        state_now = fwd_post(step, state_now, got)
        state_grad = bwd_post(levels - step, bwd_own, back)
        bwd_own, bwd_send = bwd_pre(levels - step - 1, state_grad)
    state_grad = bwd_post(0, bwd_own, from_partner(bwd_send, "seq", 0))
    register(levels)
    run_tasks(levels, [t[2] for t in pending[levels]])
    carry_parts = [task_results[("carry", k)] for k in range(levels)]
    c_carry = sum(p[0] for p in carry_parts)
    decay_carry = sum(p[1] for p in carry_parts)
    weight_carry = jnp.stack([p[2] for p in carry_parts], axis=1)

    own_log_grads = []
    peer_log_grads = []
    prefix_grads = []
    for level_index in range(levels):
        upper = uppers[level_index]
        with_peer, with_own, carry_peer = task_results[("log", level_index)]
        own_log_grads.append(jnp.where(upper, own_lifts[level_index] * with_peer, 0.0))
        peer_log_grads.append(jnp.where(upper, 0.0, peer_lifts[level_index] * with_own))
        prefix_grads.append(jnp.where(upper, prefix_lifts[level_index] * carry_peer, 0.0))
    unused, pull_logs = jax.vjp(lambda t: level_logs(t, position, levels), totals)
    (totals_grad,) = pull_logs((own_log_grads, peer_log_grads, prefix_grads))

    input_buf = jnp.concatenate([r[0] for r in group_results], axis=1)
    factor, pulled = state_spread(own_b, own_decay, state_grad)
    input_grad = input_buf + (factor[:, :, None] * pulled).reshape(length, -1)
    upstream_send, totals_grad = lax.optimization_barrier(
        (input_grad.astype(jnp.bfloat16), totals_grad)
    )
    upstream = passed_along(upstream_send, "section", -1)
    totals_grad = sum_over(totals_grad, "seq")
    log_grad = lax.dynamic_index_in_dim(totals_grad, position, 0, keepdims=False)

    weight_first = jnp.transpose(jnp.concatenate([r[1] for r in group_results], axis=0))
    running_grad = jnp.transpose(jnp.concatenate([r[2] for r in group_results], axis=0))
    decay_buf = jnp.cumsum(running_grad[::-1], axis=0)[::-1]
    score_grad = sum(r[3] for r in group_results)
    c_acc = jnp.dot(score_grad, b_full, precision=highest)
    b_acc = jnp.dot(score_grad.T, c_full, precision=highest)

    b_extra, decay_extra = state_backward(
        own_inputs, own_decay, state_grad, log_grad, factor, pulled
    )
    b_grad = b_acc + b_extra
    c_grad = c_acc + c_carry
    decay_grad = decay_buf + decay_carry + decay_extra
    weight_grad = jnp.concatenate([weight_first[:, None, :], weight_carry], axis=1)
    return (upstream[None], b_grad[None], c_grad[None], decay_grad[None], weight_grad[None])


def solution(mesh):
    return jax.shard_map(
        body,
        mesh=mesh,
        in_specs=(
            P("section", "seq", None),
            P("section", "seq", None),
            P("section", "seq", None),
            P("section", "seq", None),
            P("section", "seq", None, None),
            P("section", "seq", None),
            P("section", None, None, None),
        ),
        out_specs=(
            P("section", "seq", None),
            P("section", "seq", None),
            P("section", "seq", None),
            P("section", "seq", None),
            P("section", "seq", None, None),
        ),
        check_vma=False,
    )
```

```python
import jax
import jax.numpy as jnp
from jax import lax
from jax.experimental import pallas as pl
from jax.experimental.pallas import tpu as pltpu
from jax.sharding import PartitionSpec as P


highest = lax.Precision.HIGHEST


def from_partner(value, axis, apart):
    return lax.ppermute(value, axis, [(i, i ^ 1 << apart) for i in range(lax.axis_size(axis))])


def passed_along(block, axis, distance):
    devices = range(lax.axis_size(axis))
    route = [((i - distance) % len(devices), i) for i in devices]
    return lax.ppermute(block, axis, route)


def block_state(inputs, b_proj, decay_log):
    length, head_count = decay_log.shape
    running = jnp.cumsum(decay_log, axis=0)
    block_total = running[-1]
    factor = jnp.exp(block_total[None, :] - running)
    weighted = inputs.astype(jnp.float32).reshape(length, head_count, -1) * factor[:, :, None]
    state = jnp.einsum("tn,thp->hnp", b_proj.astype(jnp.float32), weighted, precision=highest)
    return (state, block_total)


def split_dot(a, b, dims):
    return lax.dot_general(
        a.astype(jnp.float32),
        b.astype(jnp.float32),
        (dims, ((), ())),
        precision=highest,
        preferred_element_type=jnp.float32,
    )


def local_kernel(heads, head_size, x_ref, g_ref, rc_ref, rr_ref, w_ref, sc_ref,
                 dx_ref, dw_ref, dr_ref, dsc_ref):
    scores = sc_ref[...]
    length = scores.shape[0]
    rows = lax.broadcasted_iota(jnp.int32, (length, length), 0)
    cols = lax.broadcasted_iota(jnp.int32, (length, length), 1)
    causal = rows >= cols
    score_grad = jnp.zeros((length, length), jnp.float32)
    ones_p = jnp.ones((1, head_size), jnp.float32)
    ones_t = jnp.ones((1, length), jnp.float32)
    for j, h in enumerate(heads):
        x = x_ref[:, h * head_size:(h + 1) * head_size]
        g = g_ref[:, h * head_size:(h + 1) * head_size].astype(jnp.float32)
        decays = jnp.where(causal, jnp.exp(rc_ref[:, h:h + 1] - rr_ref[h:h + 1, :]), 0.0)
        mixing = decays * scores
        local = split_dot(mixing, x, ((1,), (0,)))
        local_grad = w_ref[:, h:h + 1] * g
        dw_ref[j:j + 1, :] = split_dot(ones_p, g * local, ((1,), (1,)))
        dx_ref[:, j * head_size:(j + 1) * head_size] = split_dot(
            jnp.transpose(mixing), local_grad, ((1,), (0,))
        )
        mixing_grad = split_dot(local_grad, x, ((1,), (1,)))
        score_grad = score_grad + mixing_grad * decays
        spread_grad = mixing_grad * scores * decays
        dr_ref[j:j + 1, :] = split_dot(ones_t, spread_grad, ((1,), (1,))) - jnp.sum(
            spread_grad, axis=0, keepdims=True
        )
    dsc_ref[...] = score_grad


def local_grads(heads, inputs, grad, running_col, running_row, first_weight, scores):
    length = inputs.shape[0]
    head_size = inputs.shape[1] // running_col.shape[1]
    count = len(heads)
    vmem = pl.BlockSpec(memory_space=pltpu.VMEM)
    flops = count * 7 * 2 * length * length * head_size
    return pl.pallas_call(
        lambda *refs: local_kernel(heads, head_size, *refs),
        out_shape=(
            jax.ShapeDtypeStruct((length, count * head_size), jnp.float32),
            jax.ShapeDtypeStruct((count, length), jnp.float32),
            jax.ShapeDtypeStruct((count, length), jnp.float32),
            jax.ShapeDtypeStruct((length, length), jnp.float32),
        ),
        in_specs=[vmem] * 6,
        out_specs=(vmem,) * 4,
        cost_estimate=pl.CostEstimate(
            flops=flops,
            transcendentals=count * length * length,
            bytes_accessed=2 * length * inputs.shape[1] * 2 + count * length * head_size * 4,
        ),
    )(inputs, grad, running_col, running_row, first_weight, scores)


def mixer_carry(c_proj, decay_log, upper_weight, carries):
    length, head_count = decay_log.shape
    running = jnp.cumsum(decay_log, axis=0)
    lift = jnp.exp(running)
    result = jnp.zeros((length, head_count, carries.shape[-1]), jnp.float32)
    for level_index in range(carries.shape[0]):
        reach = jnp.einsum("tn,hnp->thp", c_proj, carries[level_index], precision=highest)
        result = result + (upper_weight[:, level_index, :] * lift)[:, :, None] * reach
    return result.reshape(length, -1)


def level_logs(totals, position, levels):
    count = totals.shape[0]
    index = jnp.arange(count)
    own, peer, prefix = [], [], []
    for level_index in range(levels):
        width = 1 << level_index
        base = position // width * width
        other = (position // width ^ 1) * width
        in_own = (index >= base) & (index < base + width)
        in_peer = (index >= other) & (index < other + width)
        in_prefix = (index >= base) & (index < position)
        own.append(jnp.sum(jnp.where(in_own[:, None], totals, 0.0), axis=0))
        peer.append(jnp.sum(jnp.where(in_peer[:, None], totals, 0.0), axis=0))
        prefix.append(jnp.sum(jnp.where(in_prefix[:, None], totals, 0.0), axis=0))
    return (own, peer, prefix)


def gather_blocks(value, axis):
    position = lax.axis_index(axis)
    blocks = value[None]
    for level_index in range(lax.axis_size(axis).bit_length() - 1):
        other = from_partner(blocks, axis, level_index)
        upper = position // 2**level_index % 2 == 1
        blocks = jnp.where(
            upper,
            jnp.concatenate([other, blocks], axis=0),
            jnp.concatenate([blocks, other], axis=0),
        )
    return blocks


def sum_over(value, axis):
    for level_index in range(lax.axis_size(axis).bit_length() - 1):
        value = value + from_partner(value, axis, level_index)
    return value


def state_spread(b_proj, decay_log, state_grad):
    running = jnp.cumsum(decay_log, axis=0)
    factor = jnp.exp(running[-1][None, :] - running)
    pulled = jnp.einsum("tn,hnp->thp", b_proj.astype(jnp.float32), state_grad, precision=highest)
    return (factor, pulled)


def state_backward(inputs, decay_log, state_grad, total_grad, factor, pulled):
    length, head_count = decay_log.shape
    values = inputs.astype(jnp.float32).reshape(length, head_count, -1)
    weighted = values * factor[:, :, None]
    b_grad = jnp.einsum("thp,hnp->tn", weighted, state_grad, precision=highest)
    log_grad = jnp.sum(values * pulled, axis=2) * factor
    running_grad = (-log_grad).at[-1].add(total_grad + jnp.sum(log_grad, axis=0))
    decay_grad = jnp.cumsum(running_grad[::-1], axis=0)[::-1]
    return (b_grad, decay_grad)


def body(inputs, b_proj, c_proj, decay_log, level_weight, out_grad, final_state_grad):
    own_inputs = inputs[0]
    own_b = b_proj[0]
    own_c = c_proj[0]
    own_decay = decay_log[0]
    own_weight = level_weight[0]
    own_grad = out_grad[0]
    length, head_count = own_decay.shape
    levels = lax.axis_size("seq").bit_length() - 1
    position = lax.axis_index("seq")
    b_full = own_b.astype(jnp.float32)
    c_full = own_c.astype(jnp.float32)
    grad_full = own_grad.astype(jnp.float32)

    totals = gather_blocks(jnp.sum(own_decay, axis=0), "seq")
    state_now, _ = block_state(own_inputs, own_b, own_decay)
    own_logs, peer_logs, prefixes = level_logs(totals, position, levels)
    lifted = jnp.exp(jnp.stack(own_logs + peer_logs + prefixes))
    own_lifts = [lifted[k] for k in range(levels)]
    peer_lifts = [lifted[levels + k] for k in range(levels)]
    prefix_lifts = [lifted[2 * levels + k] for k in range(levels)]
    uppers = [position // 2**level_index % 2 == 1 for level_index in range(levels)]

    unused, pull_carry = jax.vjp(
        mixer_carry, c_full, own_decay, own_weight[:, 1:, :],
        jnp.zeros((levels,) + state_now.shape, jnp.float32),
    )
    carry_grads = pull_carry(grad_full)[3]

    running_col = jnp.cumsum(own_decay, axis=0)
    running_row = jnp.transpose(running_col)
    first_weight = own_weight[:, 0, :]
    scores = jnp.dot(c_full, b_full.T, precision=highest)

    def group_grads(g, gate):
        gate_col, gate_row = gate
        return local_grads(
            group_heads[g], own_inputs, own_grad, gate_col, gate_row, first_weight, scores
        )

    link_steps = list(range(1, levels)) or [0]
    group_count = len(link_steps)
    group_heads = [
        tuple(range(g * head_count // group_count, (g + 1) * head_count // group_count))
        for g in range(group_count)
    ]
    step_groups = [[] for _ in range(levels)]
    for g, step in enumerate(link_steps):
        step_groups[step].append(g)
    group_results = [None] * group_count

    core = position % 2
    half = head_count // 2
    use_halves = head_count % 2 == 0

    def take_half(x, which):
        return lax.dynamic_slice_in_dim(x, which * half, half, 0)

    saved_own = [None] * levels
    saved_peer = [None] * levels
    carries = [None] * levels
    joined_grads = [None] * levels

    def fwd_pre(level_index, state):
        saved_own[level_index] = state
        if level_index == 0 or not use_halves:
            return state
        return take_half(state, core)

    def fwd_post(level_index, state, got):
        if level_index == 0 or not use_halves:
            peer_state = got
        else:
            other = from_partner(got, "seq", 0)
            low = jnp.where(core == 0, got, other)
            high = jnp.where(core == 0, other, got)
            peer_state = jnp.concatenate([low, high], axis=0)
        upper = uppers[level_index]
        saved_peer[level_index] = peer_state
        carries[level_index] = jnp.where(
            upper, prefix_lifts[level_index][:, None, None] * peer_state, 0.0
        )
        if level_index == levels - 1:
            return None
        return jnp.where(
            upper,
            own_lifts[level_index][:, None, None] * peer_state + state,
            peer_lifts[level_index][:, None, None] * state + peer_state,
        )

    def bwd_pre(level_index, joined_grad):
        upper = uppers[level_index]
        joined_grads[level_index] = joined_grad
        own_sg = jnp.where(
            upper, joined_grad, peer_lifts[level_index][:, None, None] * joined_grad
        )
        peer_sg = jnp.where(
            upper,
            own_lifts[level_index][:, None, None] * joined_grad
            + prefix_lifts[level_index][:, None, None] * carry_grads[level_index],
            joined_grad,
        )
        if level_index == 0 or not use_halves:
            return (own_sg, peer_sg)
        summed = take_half(peer_sg, core) + from_partner(take_half(peer_sg, 1 - core), "seq", 0)
        return (own_sg, summed)

    def bwd_post(level_index, own_sg, back):
        if level_index == 0 or not use_halves:
            return own_sg + back
        own_half = take_half(own_sg, core)
        return lax.dynamic_update_slice_in_dim(own_sg, own_half + back, core * half, 0)

    def run_groups(step, gates):
        for g, gate in zip(step_groups[step], gates):
            group_results[g] = group_grads(g, gate)
        return tuple(group_results[g] for g in step_groups[step])

    def gates_of(step):
        return [(running_col, running_row) for g in step_groups[step]]

    def carry_task(level_index):
        def run(carry):
            _, pull = jax.vjp(
                lambda c, d, w, cr: mixer_carry(c, d, w[:, None, :], cr[None]),
                c_full, own_decay, own_weight[:, level_index + 1, :], carry,
            )
            return pull(grad_full)[:3]

        return run

    def log_task():
        def run(joined_grad, peer_state, own_state):
            return (
                jnp.sum(joined_grad * peer_state, axis=(1, 2)),
                jnp.sum(joined_grad * own_state, axis=(1, 2)),
            )

        return run

    def carry_log_task(level_index):
        def run(peer_state):
            return jnp.sum(carry_grads[level_index] * peer_state, axis=(1, 2))

        return run

    pending = [[] for _ in range(levels + 1)]
    task_results = {}
    log_registered = set()

    def register(step):
        for k in range(levels):
            if carries[k] is not None and ("carry", k) not in task_results and not any(
                key == ("carry", k) for key, _, _ in sum(pending, [])
            ):
                pending[min(step, levels)].append((("carry", k), carry_task(k), (carries[k],)))
            if ("carrylog", k) not in log_registered and saved_peer[k] is not None:
                log_registered.add(("carrylog", k))
                pending[min(step, levels)].append(
                    (("carrylog", k), carry_log_task(k), (saved_peer[k],))
                )
            if (
                k not in log_registered
                and saved_peer[k] is not None
                and joined_grads[k] is not None
            ):
                log_registered.add(k)
                pending[min(step, levels)].append(
                    (("log", k), log_task(), (joined_grads[k], saved_peer[k], saved_own[k]))
                )

    def run_tasks(step, task_args):
        outputs = []
        for (key, fn, unused), args in zip(pending[step], task_args):
            task_results[key] = fn(*args)
            outputs.append(task_results[key])
        return tuple(outputs)

    fwd_send = fwd_pre(0, state_now)
    bwd_own, bwd_send = bwd_pre(levels - 1, jnp.where(position == 0, final_state_grad[0], 0.0))
    fwd_send, gates = lax.optimization_barrier((fwd_send, gates_of(0)))
    got = from_partner(fwd_send, "seq", 0)
    finished = run_groups(0, gates)
    state_now = fwd_post(0, state_now, got)
    for step in range(1, levels):
        register(step)
        fwd_send = fwd_pre(step, state_now)
        fwd_send, bwd_send, gates, task_args, finished = lax.optimization_barrier(
            (fwd_send, bwd_send, gates_of(step), [t[2] for t in pending[step]], finished)
        )
        got = from_partner(fwd_send, "seq", step)
        back = from_partner(bwd_send, "seq", levels - step)
        kernel_results = run_groups(step, gates)
        finished = (kernel_results, run_tasks(step, task_args))
        state_now = fwd_post(step, state_now, got)
        state_grad = bwd_post(levels - step, bwd_own, back)
        bwd_own, bwd_send = bwd_pre(levels - step - 1, state_grad)
    state_grad = bwd_post(0, bwd_own, from_partner(bwd_send, "seq", 0))
    register(levels)
    run_tasks(levels, [t[2] for t in pending[levels]])
    carry_parts = [task_results[("carry", k)] for k in range(levels)]
    c_carry = sum(p[0] for p in carry_parts)
    decay_carry = sum(p[1] for p in carry_parts)
    weight_carry = jnp.stack([p[2] for p in carry_parts], axis=1)

    own_log_grads = []
    peer_log_grads = []
    prefix_grads = []
    for level_index in range(levels):
        upper = uppers[level_index]
        with_peer, with_own = task_results[("log", level_index)]
        carry_peer = task_results[("carrylog", level_index)]
        own_log_grads.append(jnp.where(upper, own_lifts[level_index] * with_peer, 0.0))
        peer_log_grads.append(jnp.where(upper, 0.0, peer_lifts[level_index] * with_own))
        prefix_grads.append(jnp.where(upper, prefix_lifts[level_index] * carry_peer, 0.0))
    unused, pull_logs = jax.vjp(lambda t: level_logs(t, position, levels), totals)
    (totals_grad,) = pull_logs((own_log_grads, peer_log_grads, prefix_grads))

    input_buf = jnp.concatenate([r[0] for r in group_results], axis=1)
    factor, pulled = state_spread(own_b, own_decay, state_grad)
    input_grad = input_buf + (factor[:, :, None] * pulled).reshape(length, -1)
    upstream_send, totals_grad = lax.optimization_barrier(
        (input_grad.astype(jnp.bfloat16), totals_grad)
    )
    upstream = passed_along(upstream_send, "section", -1)
    totals_grad = sum_over(totals_grad, "seq")
    log_grad = lax.dynamic_index_in_dim(totals_grad, position, 0, keepdims=False)

    weight_first = jnp.transpose(jnp.concatenate([r[1] for r in group_results], axis=0))
    running_grad = jnp.transpose(jnp.concatenate([r[2] for r in group_results], axis=0))
    decay_buf = jnp.cumsum(running_grad[::-1], axis=0)[::-1]
    score_grad = sum(r[3] for r in group_results)
    c_acc = jnp.dot(score_grad, b_full, precision=highest)
    b_acc = jnp.dot(score_grad.T, c_full, precision=highest)

    b_extra, decay_extra = state_backward(
        own_inputs, own_decay, state_grad, log_grad, factor, pulled
    )
    b_grad = b_acc + b_extra
    c_grad = c_acc + c_carry
    decay_grad = decay_buf + decay_carry + decay_extra
    weight_grad = jnp.concatenate([weight_first[:, None, :], weight_carry], axis=1)
    return (upstream[None], b_grad[None], c_grad[None], decay_grad[None], weight_grad[None])


def solution(mesh):
    return jax.shard_map(
        body,
        mesh=mesh,
        in_specs=(
            P("section", "seq", None),
            P("section", "seq", None),
            P("section", "seq", None),
            P("section", "seq", None),
            P("section", "seq", None, None),
            P("section", "seq", None),
            P("section", None, None, None),
        ),
        out_specs=(
            P("section", "seq", None),
            P("section", "seq", None),
            P("section", "seq", None),
            P("section", "seq", None),
            P("section", "seq", None, None),
        ),
        check_vma=False,
    )
```
